256 devices in a mesh: dp: 16 (over z_lo, y, core), expert: 16 (over z_hi, x).
Axes of the slice: x: 4, y: 4, z: 8 (z_hi: 4, z_lo: 2; z = z_hi * 2 + z_lo), core: 2. Of those that a mesh axis runs over, the one named last changes fastest.
Arguments:
- feats: bfloat16 [16, 64, 128, 512], P('dp', 'expert'), may hold values from -6 to 6
- labels: int32 [16, 64, 128, 1], P('dp', 'expert'), may hold values from 0 to 15; in each aligned block of 512 rows (0 to 511, 512 to 1023, ..., all dimensions but the last counted through in order) at most 64 rows name the same one
- w_first: bfloat16 [16, 512, 2048], P('expert'), may hold values from -0.25 to 0.25
- w_second: bfloat16 [16, 2048, 256], P('expert'), may hold values from -0.125 to 0.125
- kernel: bfloat16 [27, 256, 256], replicated, may hold values from -0.078125 to 0.078125
- cotangent: bfloat16 [16, 64, 128, 256], P('dp', 'expert'), may hold values from -6 to 6
Outputs:
- imitated: bfloat16 [16, 64, 128, 256], P('dp', 'expert')
- feat_grad: bfloat16 [16, 64, 128, 512], P('dp', 'expert')
- grad_first: float32 [16, 512, 2048], P('expert', None, 'dp')
- grad_second: float32 [16, 2048, 256], P('expert', 'dp')
The draws below stay inside these ranges and needn't reach their ends.
Inputs may be any that keep to these rules, and one draw needn't show every extreme that they name: `labels`: within the 512 patches of one device (aligned blocks of 512 patches in grid order), no label occurs more than 64 times, and some label occurs exactly 64 times.
All inputs are finite; a program needn't handle non-finite values.
Results may differ from the reference program's by a relative error of at most 0.023.
Values may be sent and summed in bfloat16 or wider, within the bound.
No kernel may reach another device: no remote copies, remote signals or barrier semaphores. Data moves between devices by JAX's collectives and lax.ppermute only.
A program may use at most 128 MiB of HBM per device.

```python
import math
import jax
import jax.numpy as jnp
import numpy as np
from jax import lax

D = 512
HID = 2048
C = 256
EXPERTS = 16
GZ = 128
TOK_DEV = 512
CAP = 64
NX = 16
NY = 64


def block_scale(stream_key, shape, shards, low, high):
    factor_of = 1.0
    for axis_at, blocks in shards:
        draws = jax.random.uniform(jax.random.fold_in(jax.random.fold_in(stream_key, 6), axis_at), (blocks,), jnp.float32, low / len(shards), high / len(shards))
        factor_of = factor_of * jnp.repeat(jnp.exp(draws), shape[axis_at] // blocks).reshape((-1,) + (1,) * (len(shape) - 1 - axis_at))
    return factor_of


def deal_out(stream_key, own, number, rows, amount, top, bound, lean):
    order = jax.random.permutation(stream_key, amount)
    crowded, ordinary = shares(amount, rows * top, bound, lean, True), shares(amount, rows * top, bound, lean, False)
    places = jnp.arange(amount)

    def named(sizes, offset_by):
        used = int((sizes > 0).sum())
        fixed = max(1, used // 4)
        moved = fixed + (places - fixed + offset_by * (used - fixed)) % max(1, amount - fixed)
        return jnp.zeros((amount,), jnp.int32).at[order[jnp.where(places < fixed, places, moved)]].set(jnp.asarray(sizes, jnp.int32))

    sizes = jnp.where(number % 4 == 0, named(crowded, number // 4), named(ordinary, number - number // 4 - 1))
    mixed = jax.random.permutation(jax.random.fold_in(own, 3), amount)
    source_of, sink = mixed[0:amount // 2 * 2:2], mixed[1:amount // 2 * 2:2]
    margin = jnp.minimum(sizes[source_of] - 1, bound - sizes[sink]) // 2
    margin = jnp.where((source_of == order[0]) | (sink == order[0]) | (sizes[sink] == 0), 0, jnp.maximum(margin, 0))
    moved = jax.random.randint(jax.random.fold_in(own, 4), (amount // 2,), 0, 1 << 20) % (margin + 1)
    sizes = sizes.at[source_of].add(-moved).at[sink].add(moved)
    items = jnp.searchsorted(jnp.cumsum(sizes), jnp.arange(rows * top), side="right").astype(jnp.int32)
    grid = items.reshape(top, rows).T
    grid = grid[jax.random.permutation(jax.random.fold_in(own, 1), rows)]
    offset_by = jax.random.randint(jax.random.fold_in(own, 2), (rows, 1), 0, top)
    return jnp.take_along_axis(grid, (jnp.arange(top)[None, :] + offset_by) % top, axis=1)


def shares(count, total, limit, slope, full):
    portions = [(1 << 20) // math.isqrt(standing ** slope) + 1 for standing in range(1, count + 1)]
    largest = limit if full else min(limit, max(-(-total // count), total * portions[0] // sum(portions)))
    least = 1 if total - largest >= count - 1 else 0
    counts, rest = [largest] + [least] * (count - 1), total - largest - least * (count - 1)
    while rest > 0:
        candidates = [i for i in range(1, count) if counts[i] < largest] or [i for i in range(1, count) if counts[i] < limit]
        pool, left = sum([portions[i] for i in candidates]), rest
        for i in candidates:
            extra = min(limit - counts[i], max(1, left * portions[i] // pool), rest)
            counts[i] = counts[i] + extra
            rest = rest - extra
    return np.array(counts)


def noise(own_key, shape, width, bound, cuts=(), held_as=jnp.bfloat16):
    drawn = jax.random.normal(own_key, shape, jnp.float32) * width
    if len(cuts) > 0:
        drawn = block_scale(own_key, shape, cuts, -0.22, 0.18) * drawn
    return jnp.clip(drawn, min=-bound, max=bound).astype(held_as)


def setup_inputs(seed: int = 0) -> dict:
    streams_of = jax.random.split(jax.random.key(seed), 7)
    feats = noise(streams_of[0], (NX, NY, GZ, D), 1.0, 6.0, ((0, 16), (1, 16)))
    labels_keys = jax.random.split(jax.random.fold_in(streams_of[1], 1), NX * NY * GZ // TOK_DEV)
    labels_turns = jax.random.permutation(jax.random.fold_in(streams_of[1], 3), NX * NY * GZ // TOK_DEV)
    labels = jax.vmap(lambda own, number: deal_out(jax.random.fold_in(streams_of[1], 2), own, number, TOK_DEV, EXPERTS, 1, CAP, 2))(labels_keys, labels_turns).reshape((NX, NY, GZ, 1))
    w_first = noise(streams_of[2], (EXPERTS, D, HID), D ** -0.5, 0.25, ((0, 16),))
    w_second = noise(streams_of[3], (EXPERTS, HID, C), HID ** -0.5, 0.125, ((0, 16),))
    kernel = noise(streams_of[4], (27, C, C), (27 * C) ** -0.5, 0.078125)
    cotangent = noise(streams_of[5], (NX, NY, GZ, C), 1.0, 6.0, ((0, 16), (1, 16)))
    return dict(feats=feats, labels=labels, w_first=w_first, w_second=w_second, kernel=kernel, cotangent=cotangent)


def gelu_act(value):
    return jax.nn.gelu(value, approximate=True)

def gelu_back(preact, upstream):
    return jax.vjp(gelu_act, preact)[1](upstream)[0]

def convolve(field, kernel):
    taps = kernel.astype(jnp.float32).reshape(3, 3, 3, C, C)
    result = lax.conv_general_dilated(field[None], taps, (1, 1, 1), 'SAME', dimension_numbers=('NDHWC', 'DHWIO', 'NDHWC'), precision=lax.Precision.HIGHEST)
    return result[0]

def reference(feats, labels, w_first, w_second, kernel, cotangent):
    patches = NX * NY * GZ
    blocks = patches // TOK_DEV
    flat_feats = feats.reshape(patches, D)
    regime = labels.reshape(patches).astype(jnp.int32)
    onehot = (regime.reshape(blocks, TOK_DEV)[:, :, None] == jnp.arange(EXPERTS, dtype=jnp.int32)[None, None, :]).astype(jnp.int32)
    ranking = jnp.cumsum(onehot, axis=1) - 1
    slot_index = lax.optimization_barrier(jnp.sum(ranking * onehot, axis=2)).reshape(patches)
    block_id = jnp.arange(patches, dtype=jnp.int32) // TOK_DEV
    position = (block_id * CAP + slot_index).astype(jnp.int32)
    table = jnp.full((EXPERTS, blocks * CAP), patches, jnp.int32).at[regime, position].set(jnp.arange(patches, dtype=jnp.int32))
    feats_ext = jnp.concatenate([flat_feats, jnp.zeros((1, D), jnp.bfloat16)], axis=0)

    def forward(operands):
        first, second, index = operands
        row_block = feats_ext[index]
        preact = jnp.dot(row_block, first, preferred_element_type=jnp.float32)
        activation = gelu_act(preact).astype(jnp.bfloat16)
        return jnp.dot(activation, second, preferred_element_type=jnp.float32).astype(jnp.bfloat16)
    out_buffer = lax.map(forward, (w_first, w_second, table))
    expert_out = out_buffer[regime, position].reshape(NX, NY, GZ, C)
    conv_out, conv_vjp = jax.vjp(lambda field: convolve(field, kernel), expert_out.astype(jnp.float32))
    imitated = conv_out.astype(jnp.bfloat16)
    field_grad = conv_vjp(cotangent.astype(jnp.float32))[0].astype(jnp.bfloat16).reshape(patches, C)
    grad_ext = jnp.concatenate([field_grad, jnp.zeros((1, C), jnp.bfloat16)], axis=0)

    def backward(operands):
        first, second, index = operands
        row_block = feats_ext[index]
        preact = jnp.dot(row_block, first, preferred_element_type=jnp.float32)
        activation = gelu_act(preact).astype(jnp.bfloat16)
        grad_rows = grad_ext[index]
        upstream = jnp.dot(grad_rows, second.T, preferred_element_type=jnp.float32)
        gate_grad = gelu_back(preact, upstream).astype(jnp.bfloat16)
        input_grad = jnp.dot(gate_grad, first.T, preferred_element_type=jnp.float32).astype(jnp.bfloat16)
        grad_one = jnp.dot(row_block.T, gate_grad, preferred_element_type=jnp.float32)
        grad_two = jnp.dot(activation.T, grad_rows, preferred_element_type=jnp.float32)
        return (input_grad, grad_one, grad_two)
    input_buffer, grad_first, grad_second = lax.map(backward, (w_first, w_second, table))
    feat_grad = input_buffer[regime, position].reshape(NX, NY, GZ, D)
    return (imitated, feat_grad, grad_first, grad_second)
```

```python
import jax
import jax.numpy as jnp
from jax import lax
from jax.sharding import PartitionSpec as P


def extended(x, sides, width):
    for axis, dim in sides:
        size, length = (lax.axis_size(axis), x.shape[dim])
        up = [(i, (i + 1) % size) for i in range(size - 1)]
        down = [(j, i) for i, j in up]
        last = lax.slice_in_dim(x, length - width, length, axis=dim)
        first = lax.slice_in_dim(x, 0, width, axis=dim)
        before = lax.ppermute(last, axis, up)
        after = lax.ppermute(first, axis, down)
        x = jnp.concatenate([before, x, after], axis=dim)
    return x


def gelu_act(value):
    return jax.nn.gelu(value, approximate=True)


def gelu_back(preact, upstream):
    return jax.vjp(gelu_act, preact)[1](upstream)[0]


def tree_scatter(blocks, order):
    count = blocks.shape[0]
    me = lax.axis_index("dp")
    bits = count.bit_length() - 1
    x = blocks.reshape((2,) * bits + blocks.shape[1:])
    remaining = list(range(bits - 1, -1, -1))
    for bit in order:
        axis = remaining.index(bit)
        mine = (me >> bit) & 1
        keep = lax.dynamic_index_in_dim(x, mine, axis=axis, keepdims=False)
        send = lax.dynamic_index_in_dim(x, 1 - mine, axis=axis, keepdims=False)
        pairs = [(i, i ^ (1 << bit)) for i in range(count)]
        got = lax.ppermute(send.astype(jnp.bfloat16), "dp", pairs)
        x = keep + got.astype(jnp.float32)
        remaining.pop(axis)
    return x


def gather_taps(padded, rows_y, depth_cells, flipped):
    pieces = []
    for plane in range(3):
        for across in range(3):
            for along in range(3):
                if flipped:
                    plane_at, across_at, along_at = (2 - plane, 2 - across, 2 - along)
                else:
                    plane_at, across_at, along_at = (plane, across, along)
                pieces.append(
                    padded[
                        plane_at,
                        across_at : across_at + rows_y,
                        along_at : along_at + depth_cells,
                        :,
                    ]
                )
    stacked = jnp.stack(pieces, axis=2)
    return stacked.reshape(rows_y * depth_cells, 27, padded.shape[3])


def per_device(feats, labels, w_first, w_second, kernel, cotangent):
    experts = lax.axis_size("expert")
    rows_y = feats.shape[1]
    depth_cells = feats.shape[2]
    feat_width = feats.shape[3]
    channels = kernel.shape[2]
    hidden = w_first.shape[2]
    patch_count = rows_y * depth_cells
    capacity = 2 * patch_count // experts
    regime = labels.reshape(patch_count)
    onehot = (regime[:, None] == jnp.arange(experts, dtype=jnp.int32)[None, :]).astype(jnp.int32)
    ranking = jnp.cumsum(onehot, axis=0) - 1
    slot_index = jnp.sum(ranking * onehot, axis=1)
    target = regime * capacity + slot_index
    flat_feats = feats.reshape(patch_count, feat_width)
    outbound = jnp.zeros((experts * capacity, feat_width), jnp.bfloat16).at[target].set(flat_feats)
    outbound = outbound.reshape(experts, capacity, feat_width)
    weight_one = w_first[0]
    weight_two = w_second[0]
    received = lax.all_to_all(outbound, "expert", split_axis=0, concat_axis=0, tiled=True)
    groups = received.shape[0]
    slot_count = received.shape[1]
    row_block = received.reshape(groups * slot_count, feat_width)
    preact = jnp.dot(row_block, weight_one, preferred_element_type=jnp.float32)
    activation = gelu_act(preact).astype(jnp.bfloat16)
    result = jnp.dot(activation, weight_two, preferred_element_type=jnp.float32).astype(
        jnp.bfloat16
    )
    result = result.reshape(groups, slot_count, channels)
    returned = lax.all_to_all(result, "expert", split_axis=0, concat_axis=0, tiled=True)
    returned, received, preact, activation = (
        returned,
        received,
        preact.reshape(groups, slot_count, hidden),
        activation.reshape(groups, slot_count, hidden),
    )
    mixed_rows = returned.reshape(experts * capacity, channels)[target]
    patch_grid = mixed_rows.reshape(1, rows_y, depth_cells, channels)
    padded = extended(patch_grid, (("dp", 0), ("expert", 1)), 1)
    padded = jnp.pad(padded, ((0, 0), (0, 0), (1, 1), (0, 0)))
    columns = gather_taps(padded, rows_y, depth_cells, False)
    imitated = jnp.einsum("tki,kio->to", columns, kernel, preferred_element_type=jnp.float32)
    imitated = imitated.astype(jnp.bfloat16).reshape(1, rows_y, depth_cells, channels)
    grad_padded = extended(cotangent, (("dp", 0), ("expert", 1)), 1)
    grad_padded = jnp.pad(grad_padded, ((0, 0), (0, 0), (1, 1), (0, 0)))
    grad_columns = gather_taps(grad_padded, rows_y, depth_cells, True)
    field_grad = jnp.einsum(
        "tko,kio->ti", grad_columns, kernel, preferred_element_type=jnp.float32
    ).astype(jnp.bfloat16)
    grad_outbound = (
        jnp.zeros((experts * capacity, channels), jnp.bfloat16).at[target].set(field_grad)
    )
    grad_outbound = grad_outbound.reshape(experts, capacity, channels)
    grad_inbound = lax.all_to_all(grad_outbound, "expert", split_axis=0, concat_axis=0, tiled=True)
    feat_rows = received.reshape(experts * capacity, feat_width)
    grad_rows = grad_inbound.reshape(experts * capacity, channels)
    preact_rows = preact.reshape(experts * capacity, hidden)
    activation_rows = activation.reshape(experts * capacity, hidden)
    upstream = lax.dot_general(
        grad_rows, weight_two, (((1,), (1,)), ((), ())), preferred_element_type=jnp.float32
    )
    gate_grad = gelu_back(preact_rows, upstream).astype(jnp.bfloat16)
    input_grad = lax.dot_general(
        gate_grad, weight_one, (((1,), (1,)), ((), ())), preferred_element_type=jnp.float32
    )
    input_grad = input_grad.astype(jnp.bfloat16).reshape(experts, capacity, feat_width)
    input_back = lax.all_to_all(input_grad, "expert", split_axis=0, concat_axis=0, tiled=True)
    feat_grad = input_back.reshape(experts * capacity, feat_width)[target].reshape(
        1, rows_y, depth_cells, feat_width
    )
    slabs = lax.axis_size("dp")
    part_one = lax.dot_general(
        gate_grad, feat_rows, (((0,), (0,)), ((), ())), preferred_element_type=jnp.float32
    )
    part_two = lax.dot_general(
        activation_rows, grad_rows, (((0,), (0,)), ((), ())), preferred_element_type=jnp.float32
    )
    grad_one = tree_scatter(part_one.reshape(slabs, hidden // slabs, feat_width), (0, 1, 3, 2))
    grad_one = grad_one.T
    grad_two = tree_scatter(part_two.reshape(slabs, hidden // slabs, channels), (0, 3, 1, 2))
    return (imitated, feat_grad, grad_one[None], grad_two[None])


def solution(mesh):
    in_specs = (
        P("dp", "expert", None, None),
        P("dp", "expert", None, None),
        P("expert", None, None),
        P("expert", None, None),
        P(),
        P("dp", "expert", None, None),
    )
    out_specs = (
        P("dp", "expert", None, None),
        P("dp", "expert", None, None),
        P("expert", None, "dp"),
        P("expert", "dp", None),
    )
    return jax.shard_map(
        per_device, mesh=mesh, in_specs=in_specs, out_specs=out_specs, check_vma=False
    )
```

```python
import jax
import jax.numpy as jnp
from jax import lax
from jax.sharding import PartitionSpec as P


def extended(x, sides, width):
    for axis, dim in sides:
        size, length = (lax.axis_size(axis), x.shape[dim])
        up = [(i, (i + 1) % size) for i in range(size - 1)]
        down = [(j, i) for i, j in up]
        last = lax.slice_in_dim(x, length - width, length, axis=dim)
        first = lax.slice_in_dim(x, 0, width, axis=dim)
        before = lax.ppermute(last, axis, up)
        after = lax.ppermute(first, axis, down)
        x = jnp.concatenate([before, x, after], axis=dim)
    return x


def gelu_act(value):
    return jax.nn.gelu(value, approximate=True)


def gelu_back(preact, upstream):
    return jax.vjp(gelu_act, preact)[1](upstream)[0]


def tree_scatter(blocks, order):
    count = blocks.shape[0]
    me = lax.axis_index("dp")
    bits = count.bit_length() - 1
    x = blocks.reshape((2,) * bits + blocks.shape[1:])
    remaining = list(range(bits - 1, -1, -1))
    for bit in order:
        axis = remaining.index(bit)
        mine = (me >> bit) & 1
        keep = lax.dynamic_index_in_dim(x, mine, axis=axis, keepdims=False)
        send = lax.dynamic_index_in_dim(x, 1 - mine, axis=axis, keepdims=False)
        pairs = [(i, i ^ (1 << bit)) for i in range(count)]
        got = lax.ppermute(send.astype(jnp.bfloat16), "dp", pairs)
        x = keep + got.astype(jnp.float32)
        remaining.pop(axis)
    return x


def conv_block(grid, taps):
    padded = extended(grid, (("dp", 0), ("expert", 1)), 1)
    padded = jnp.pad(padded, ((0, 0), (0, 0), (1, 1), (0, 0)))
    out = lax.conv_general_dilated(
        padded[None],
        taps,
        (1, 1, 1),
        "VALID",
        dimension_numbers=("NDHWC", "DHWIO", "NDHWC"),
        preferred_element_type=jnp.float32,
    )
    return out[0].astype(jnp.bfloat16)


def per_device(feats, labels, w_first, w_second, kernel, cotangent):
    experts = lax.axis_size("expert")
    rows_y = feats.shape[1]
    depth_cells = feats.shape[2]
    feat_width = feats.shape[3]
    channels = kernel.shape[2]
    hidden = w_first.shape[2]
    patch_count = rows_y * depth_cells
    capacity = 2 * patch_count // experts
    slots = experts * capacity
    regime = labels.reshape(patch_count)
    onehot = (regime[:, None] == jnp.arange(experts, dtype=jnp.int32)[None, :]).astype(
        jnp.bfloat16
    )
    lower = (
        jnp.arange(patch_count)[:, None] >= jnp.arange(patch_count)[None, :]
    ).astype(jnp.bfloat16)
    ranking = jnp.dot(lower, onehot, preferred_element_type=jnp.float32)
    slot_index = jnp.sum(ranking * onehot.astype(jnp.float32), axis=1).astype(jnp.int32) - 1
    target = regime * capacity + slot_index
    route = (target[None, :] == jnp.arange(slots, dtype=jnp.int32)[:, None]).astype(jnp.bfloat16)
    flat_feats = feats.reshape(patch_count, feat_width)
    outbound = jnp.dot(route, flat_feats, preferred_element_type=jnp.float32).astype(jnp.bfloat16)
    outbound = outbound.reshape(experts, capacity, feat_width)
    received = lax.all_to_all(outbound, "expert", split_axis=0, concat_axis=0, tiled=True)

    taps = kernel.reshape(3, 3, 3, channels, channels)
    flipped = taps[::-1, ::-1, ::-1]
    field_grad = conv_block(cotangent, jnp.swapaxes(flipped, 3, 4))
    field_rows = field_grad.reshape(patch_count, channels)
    grad_outbound = jnp.dot(route, field_rows, preferred_element_type=jnp.float32).astype(
        jnp.bfloat16
    )
    grad_outbound = grad_outbound.reshape(experts, capacity, channels)
    grad_inbound = lax.all_to_all(grad_outbound, "expert", split_axis=0, concat_axis=0, tiled=True)

    weight_one = w_first[0]
    weight_two = w_second[0]
    row_block = received.reshape(slots, feat_width)
    preact = jnp.dot(row_block, weight_one, preferred_element_type=jnp.float32)
    activation = gelu_act(preact).astype(jnp.bfloat16)
    result = jnp.dot(activation, weight_two, preferred_element_type=jnp.float32).astype(
        jnp.bfloat16
    )
    returned = lax.all_to_all(
        result.reshape(experts, capacity, channels), "expert", split_axis=0, concat_axis=0, tiled=True
    )
    mixed_rows = lax.dot_general(
        route,
        returned.reshape(slots, channels),
        (((0,), (0,)), ((), ())),
        preferred_element_type=jnp.float32,
    ).astype(jnp.bfloat16)
    patch_grid = mixed_rows.reshape(1, rows_y, depth_cells, channels)
    imitated = conv_block(patch_grid, taps)

    grad_rows = grad_inbound.reshape(slots, channels)
    upstream = lax.dot_general(
        grad_rows, weight_two, (((1,), (1,)), ((), ())), preferred_element_type=jnp.float32
    )
    gate_grad = gelu_back(preact, upstream).astype(jnp.bfloat16)
    input_grad = lax.dot_general(
        gate_grad, weight_one, (((1,), (1,)), ((), ())), preferred_element_type=jnp.float32
    )
    input_grad = input_grad.astype(jnp.bfloat16).reshape(experts, capacity, feat_width)
    input_back = lax.all_to_all(input_grad, "expert", split_axis=0, concat_axis=0, tiled=True)
    feat_grad = lax.dot_general(
        route,
        input_back.reshape(slots, feat_width),
        (((0,), (0,)), ((), ())),
        preferred_element_type=jnp.float32,
    ).astype(jnp.bfloat16)
    feat_grad = feat_grad.reshape(1, rows_y, depth_cells, feat_width)

    slabs = lax.axis_size("dp")
    part_one = lax.dot_general(
        gate_grad, row_block, (((0,), (0,)), ((), ())), preferred_element_type=jnp.float32
    )
    part_two = lax.dot_general(
        activation, grad_rows, (((0,), (0,)), ((), ())), preferred_element_type=jnp.float32
    )
    grad_one = tree_scatter(part_one.reshape(slabs, hidden // slabs, feat_width), (0, 1, 3, 2))
    grad_one = grad_one.T
    grad_two = tree_scatter(part_two.reshape(slabs, hidden // slabs, channels), (0, 3, 1, 2))
    return (imitated, feat_grad, grad_one[None], grad_two[None])


def solution(mesh):
    in_specs = (
        P("dp", "expert", None, None),
        P("dp", "expert", None, None),
        P("expert", None, None),
        P("expert", None, None),
        P(),
        P("dp", "expert", None, None),
    )
    out_specs = (
        P("dp", "expert", None, None),
        P("dp", "expert", None, None),
        P("expert", None, "dp"),
        P("expert", "dp", None),
    )
    return jax.shard_map(
        per_device, mesh=mesh, in_specs=in_specs, out_specs=out_specs, check_vma=False
    )
```

```python
import functools

import jax
import jax.numpy as jnp
from jax import lax
from jax.experimental import pallas as pl
from jax.experimental.pallas import tpu as pltpu
from jax.sharding import PartitionSpec as P


def extended(x, sides, width):
    for axis, dim in sides:
        size, length = (lax.axis_size(axis), x.shape[dim])
        up = [(i, (i + 1) % size) for i in range(size - 1)]
        down = [(j, i) for i, j in up]
        last = lax.slice_in_dim(x, length - width, length, axis=dim)
        first = lax.slice_in_dim(x, 0, width, axis=dim)
        before = lax.ppermute(last, axis, up)
        after = lax.ppermute(first, axis, down)
        x = jnp.concatenate([before, x, after], axis=dim)
    return x


def gelu_act(value):
    return jax.nn.gelu(value, approximate=True)


def gelu_back(preact, upstream):
    return jax.vjp(gelu_act, preact)[1](upstream)[0]


def tree_scatter(blocks, order):
    count = blocks.shape[0]
    me = lax.axis_index("dp")
    bits = count.bit_length() - 1
    x = blocks.reshape((2,) * bits + blocks.shape[1:])
    remaining = list(range(bits - 1, -1, -1))
    for bit in order:
        axis = remaining.index(bit)
        mine = (me >> bit) & 1
        keep = lax.dynamic_index_in_dim(x, mine, axis=axis, keepdims=False)
        send = lax.dynamic_index_in_dim(x, 1 - mine, axis=axis, keepdims=False)
        pairs = [(i, i ^ (1 << bit)) for i in range(count)]
        got = lax.ppermute(send.astype(jnp.bfloat16), "dp", pairs)
        x = keep + got.astype(jnp.float32)
        remaining.pop(axis)
    return x


def conv_block(grid, taps):
    padded = extended(grid, (("dp", 0), ("expert", 1)), 1)
    padded = jnp.pad(padded, ((0, 0), (0, 0), (1, 1), (0, 0)))
    out = lax.conv_general_dilated(
        padded[None],
        taps,
        (1, 1, 1),
        "VALID",
        dimension_numbers=("NDHWC", "DHWIO", "NDHWC"),
        preferred_element_type=jnp.float32,
    )
    return out[0].astype(jnp.bfloat16)


def expert_kernel(
    cols, rows_ref, first_ref, second_ref, back_ref, part_ref, result_acc, input_acc
):
    step = pl.program_id(0)

    @pl.when(step == 0)
    def _():
        result_acc[...] = jnp.zeros_like(result_acc)
        input_acc[...] = jnp.zeros_like(input_acc)

    rows = rows_ref[:, :cols]
    grads = rows_ref[:, cols:]
    first = first_ref[...]
    second = second_ref[...]
    preact = jnp.dot(rows, first, preferred_element_type=jnp.float32)
    activation = gelu_act(preact).astype(jnp.bfloat16)
    result_acc[...] += jnp.dot(activation, second, preferred_element_type=jnp.float32)
    upstream = lax.dot_general(
        grads, second, (((1,), (1,)), ((), ())), preferred_element_type=jnp.float32
    )
    gate_grad = gelu_back(preact, upstream).astype(jnp.bfloat16)
    input_acc[...] += lax.dot_general(
        gate_grad, first, (((1,), (1,)), ((), ())), preferred_element_type=jnp.float32
    )
    part_ref[:, :cols] = lax.dot_general(
        gate_grad, rows, (((0,), (0,)), ((), ())), preferred_element_type=jnp.float32
    )
    part_ref[:, cols:] = lax.dot_general(
        activation, grads, (((0,), (0,)), ((), ())), preferred_element_type=jnp.float32
    )

    @pl.when(step == pl.num_programs(0) - 1)
    def _():
        width = result_acc.shape[1]
        back_ref[:, :width] = result_acc[...].astype(back_ref.dtype)
        back_ref[:, width:] = input_acc[...].astype(back_ref.dtype)


def expert(inbound, weight_one, weight_two, chunk):
    slots, both = inbound.shape
    cols, hidden = weight_one.shape
    channels = weight_two.shape[1]
    flops = 2 * slots * hidden * (3 * cols + 3 * channels)
    return pl.pallas_call(
        functools.partial(expert_kernel, cols),
        grid=(hidden // chunk,),
        in_specs=[
            pl.BlockSpec((slots, both), lambda h: (0, 0)),
            pl.BlockSpec((cols, chunk), lambda h: (0, h)),
            pl.BlockSpec((chunk, channels), lambda h: (h, 0)),
        ],
        out_specs=[
            pl.BlockSpec((slots, both), lambda h: (0, 0)),
            pl.BlockSpec((chunk, both), lambda h: (h, 0)),
        ],
        out_shape=[
            jax.ShapeDtypeStruct((slots, both), jnp.bfloat16),
            jax.ShapeDtypeStruct((hidden, both), jnp.float32),
        ],
        scratch_shapes=[
            pltpu.VMEM((slots, channels), jnp.float32),
            pltpu.VMEM((slots, cols), jnp.float32),
        ],
        compiler_params=pltpu.CompilerParams(
            dimension_semantics=("arbitrary",), vmem_limit_bytes=56 * 1024 * 1024
        ),
        cost_estimate=pl.CostEstimate(
            flops=flops,
            transcendentals=slots * hidden,
            bytes_accessed=2 * (2 * slots * both + hidden * (cols + channels)) + 4 * hidden * both,
        ),
    )(inbound, weight_one, weight_two)


def per_device(feats, labels, w_first, w_second, kernel, cotangent):
    experts = lax.axis_size("expert")
    slabs = lax.axis_size("dp")
    rows_y = feats.shape[1]
    depth_cells = feats.shape[2]
    feat_width = feats.shape[3]
    channels = kernel.shape[2]
    hidden = w_first.shape[2]
    patch_count = rows_y * depth_cells
    capacity = 2 * patch_count // experts
    slots = experts * capacity
    regime = labels.reshape(patch_count)
    onehot = (regime[:, None] == jnp.arange(experts, dtype=jnp.int32)[None, :]).astype(
        jnp.bfloat16
    )
    lower = (
        jnp.arange(patch_count)[:, None] >= jnp.arange(patch_count)[None, :]
    ).astype(jnp.bfloat16)
    ranking = jnp.dot(lower, onehot, preferred_element_type=jnp.float32)
    slot_index = jnp.sum(ranking * onehot.astype(jnp.float32), axis=1).astype(jnp.int32) - 1
    target = regime * capacity + slot_index
    route = (target[None, :] == jnp.arange(slots, dtype=jnp.int32)[:, None]).astype(jnp.bfloat16)

    taps = kernel.reshape(3, 3, 3, channels, channels)
    flipped = taps[::-1, ::-1, ::-1]
    field_grad = conv_block(cotangent, jnp.swapaxes(flipped, 3, 4))
    field_rows = field_grad.reshape(patch_count, channels)
    flat_feats = feats.reshape(patch_count, feat_width)
    local = jnp.concatenate([flat_feats, field_rows], axis=1)
    outbound = jnp.dot(route, local, preferred_element_type=jnp.float32).astype(jnp.bfloat16)
    both = feat_width + channels
    inbound = lax.all_to_all(
        outbound.reshape(experts, capacity, both), "expert", split_axis=0, concat_axis=0, tiled=True
    )
    back, part = expert(inbound.reshape(slots, both), w_first[0], w_second[0], 512)
    returned = lax.all_to_all(
        back.reshape(experts, capacity, both), "expert", split_axis=0, concat_axis=0, tiled=True
    )
    mixed = lax.dot_general(
        route,
        returned.reshape(slots, both),
        (((0,), (0,)), ((), ())),
        preferred_element_type=jnp.float32,
    ).astype(jnp.bfloat16)
    patch_grid = mixed[:, :channels].reshape(1, rows_y, depth_cells, channels)
    imitated = conv_block(patch_grid, taps)
    feat_grad = mixed[:, channels:].reshape(1, rows_y, depth_cells, feat_width)

    grads = tree_scatter(part.reshape(slabs, hidden // slabs, both), (0, 1, 3, 2))
    grad_one = grads[:, :feat_width].T
    grad_two = grads[:, feat_width:]
    return (imitated, feat_grad, grad_one[None], grad_two[None])


def solution(mesh):
    in_specs = (
        P("dp", "expert", None, None),
        P("dp", "expert", None, None),
        P("expert", None, None),
        P("expert", None, None),
        P(),
        P("dp", "expert", None, None),
    )
    out_specs = (
        P("dp", "expert", None, None),
        P("dp", "expert", None, None),
        P("expert", None, "dp"),
        P("expert", "dp", None),
    )
    return jax.shard_map(
        per_device, mesh=mesh, in_specs=in_specs, out_specs=out_specs, check_vma=False
    )
```

```python
import functools

import jax
import jax.numpy as jnp
from jax import lax
from jax.experimental import pallas as pl
from jax.experimental.pallas import tpu as pltpu
from jax.sharding import PartitionSpec as P


def extended(x, sides, width):
    for axis, dim in sides:
        size, length = (lax.axis_size(axis), x.shape[dim])
        up = [(i, (i + 1) % size) for i in range(size - 1)]
        down = [(j, i) for i, j in up]
        last = lax.slice_in_dim(x, length - width, length, axis=dim)
        first = lax.slice_in_dim(x, 0, width, axis=dim)
        before = lax.ppermute(last, axis, up)
        after = lax.ppermute(first, axis, down)
        x = jnp.concatenate([before, x, after], axis=dim)
    return x


def gelu_act(value):
    return jax.nn.gelu(value, approximate=True)


def gelu_back(preact, upstream):
    return jax.vjp(gelu_act, preact)[1](upstream)[0]


def tree_scatter(blocks, order):
    count = blocks.shape[0]
    me = lax.axis_index("dp")
    bits = count.bit_length() - 1
    x = blocks.reshape((2,) * bits + blocks.shape[1:])
    remaining = list(range(bits - 1, -1, -1))
    for bit in order:
        axis = remaining.index(bit)
        mine = (me >> bit) & 1
        keep = lax.dynamic_index_in_dim(x, mine, axis=axis, keepdims=False)
        send = lax.dynamic_index_in_dim(x, 1 - mine, axis=axis, keepdims=False)
        pairs = [(i, i ^ (1 << bit)) for i in range(count)]
        got = lax.ppermute(send.astype(jnp.bfloat16), "dp", pairs)
        x = keep + got.astype(jnp.float32)
        remaining.pop(axis)
    return x


def conv_kernel(flip, shifted_ref, taps_ref, out_ref, acc_ref):
    rows_y = shifted_ref.shape[3] - 2
    depth_cells = shifted_ref.shape[4]
    width = shifted_ref.shape[5]
    acc_ref[...] = jnp.zeros_like(acc_ref)
    for plane in range(3):
        for across in range(3):
            for along in range(3):
                tap = 9 * plane + 3 * across + along
                piece = shifted_ref[0, along, plane, across : across + rows_y]
                piece = piece.reshape(rows_y * depth_cells, width)
                if flip:
                    acc_ref[...] += lax.dot_general(
                        piece,
                        taps_ref[26 - tap],
                        (((1,), (1,)), ((), ())),
                        preferred_element_type=jnp.float32,
                    )
                else:
                    acc_ref[...] += jnp.dot(
                        piece, taps_ref[tap], preferred_element_type=jnp.float32
                    )
    out_ref[...] = acc_ref[...].astype(out_ref.dtype)


def conv_block(grid, kernel, flip):
    padded = extended(grid, (("dp", 0), ("expert", 1)), 1)
    padded = jnp.pad(padded, ((0, 0), (0, 0), (1, 1), (0, 0)))
    depth_cells = grid.shape[2]
    shifted = jnp.stack(
        [padded[:, :, along : along + depth_cells] for along in range(3)], axis=0
    )[None]
    count = grid.shape[1] * depth_cells
    width = kernel.shape[2]
    return pl.pallas_call(
        functools.partial(conv_kernel, flip),
        out_shape=jax.ShapeDtypeStruct((count, width), jnp.bfloat16),
        in_specs=[pl.BlockSpec(memory_space=pltpu.VMEM)] * 2,
        out_specs=pl.BlockSpec(memory_space=pltpu.VMEM),
        scratch_shapes=[pltpu.VMEM((count, width), jnp.float32)],
        compiler_params=pltpu.CompilerParams(vmem_limit_bytes=48 * 1024 * 1024),
        cost_estimate=pl.CostEstimate(
            flops=2 * 27 * count * width * width,
            transcendentals=0,
            bytes_accessed=2 * (shifted.size + kernel.size + count * width),
        ),
    )(shifted, kernel)


def expert_kernel(
    cols, rows_ref, first_ref, second_ref, back_ref, part_ref, result_acc, input_acc
):
    step = pl.program_id(0)

    @pl.when(step == 0)
    def _():
        result_acc[...] = jnp.zeros_like(result_acc)
        input_acc[...] = jnp.zeros_like(input_acc)

    rows = rows_ref[:, :cols]
    grads = rows_ref[:, cols:]
    first = first_ref[...]
    second = second_ref[...]
    preact = jnp.dot(rows, first, preferred_element_type=jnp.float32)
    activation = gelu_act(preact).astype(jnp.bfloat16)
    result_acc[...] += jnp.dot(activation, second, preferred_element_type=jnp.float32)
    upstream = lax.dot_general(
        grads, second, (((1,), (1,)), ((), ())), preferred_element_type=jnp.float32
    )
    gate_grad = gelu_back(preact, upstream).astype(jnp.bfloat16)
    input_acc[...] += lax.dot_general(
        gate_grad, first, (((1,), (1,)), ((), ())), preferred_element_type=jnp.float32
    )
    part_ref[:, :cols] = lax.dot_general(
        gate_grad, rows, (((0,), (0,)), ((), ())), preferred_element_type=jnp.float32
    )
    part_ref[:, cols:] = lax.dot_general(
        activation, grads, (((0,), (0,)), ((), ())), preferred_element_type=jnp.float32
    )

    @pl.when(step == pl.num_programs(0) - 1)
    def _():
        width = result_acc.shape[1]
        back_ref[:, :width] = result_acc[...].astype(back_ref.dtype)
        back_ref[:, width:] = input_acc[...].astype(back_ref.dtype)


def expert(inbound, weight_one, weight_two, chunk):
    slots, both = inbound.shape
    cols, hidden = weight_one.shape
    channels = weight_two.shape[1]
    flops = 2 * slots * hidden * (3 * cols + 3 * channels)
    return pl.pallas_call(
        functools.partial(expert_kernel, cols),
        grid=(hidden // chunk,),
        in_specs=[
            pl.BlockSpec((slots, both), lambda h: (0, 0)),
            pl.BlockSpec((cols, chunk), lambda h: (0, h)),
            pl.BlockSpec((chunk, channels), lambda h: (h, 0)),
        ],
        out_specs=[
            pl.BlockSpec((slots, both), lambda h: (0, 0)),
            pl.BlockSpec((chunk, both), lambda h: (h, 0)),
        ],
        out_shape=[
            jax.ShapeDtypeStruct((slots, both), jnp.bfloat16),
            jax.ShapeDtypeStruct((hidden, both), jnp.float32),
        ],
        scratch_shapes=[
            pltpu.VMEM((slots, channels), jnp.float32),
            pltpu.VMEM((slots, cols), jnp.float32),
        ],
        compiler_params=pltpu.CompilerParams(
            dimension_semantics=("arbitrary",), vmem_limit_bytes=56 * 1024 * 1024
        ),
        cost_estimate=pl.CostEstimate(
            flops=flops,
            transcendentals=slots * hidden,
            bytes_accessed=2 * (2 * slots * both + hidden * (cols + channels)) + 4 * hidden * both,
        ),
    )(inbound, weight_one, weight_two)


def per_device(feats, labels, w_first, w_second, kernel, cotangent):
    experts = lax.axis_size("expert")
    slabs = lax.axis_size("dp")
    rows_y = feats.shape[1]
    depth_cells = feats.shape[2]
    feat_width = feats.shape[3]
    channels = kernel.shape[2]
    hidden = w_first.shape[2]
    patch_count = rows_y * depth_cells
    capacity = 2 * patch_count // experts
    slots = experts * capacity
    regime = labels.reshape(patch_count)
    onehot = (regime[:, None] == jnp.arange(experts, dtype=jnp.int32)[None, :]).astype(
        jnp.bfloat16
    )
    lower = (
        jnp.arange(patch_count)[:, None] >= jnp.arange(patch_count)[None, :]
    ).astype(jnp.bfloat16)
    ranking = jnp.dot(lower, onehot, preferred_element_type=jnp.float32)
    slot_index = jnp.sum(ranking * onehot.astype(jnp.float32), axis=1).astype(jnp.int32) - 1
    target = regime * capacity + slot_index
    route = (target[None, :] == jnp.arange(slots, dtype=jnp.int32)[:, None]).astype(jnp.bfloat16)

    flat_feats = feats.reshape(patch_count, feat_width)
    outbound = jnp.dot(route, flat_feats, preferred_element_type=jnp.float32).astype(jnp.bfloat16)
    received = lax.all_to_all(
        outbound.reshape(experts, capacity, feat_width), "expert", split_axis=0, concat_axis=0, tiled=True
    )
    field_rows = conv_block(cotangent, kernel, True)
    grad_outbound = jnp.dot(route, field_rows, preferred_element_type=jnp.float32).astype(
        jnp.bfloat16
    )
    grad_inbound = lax.all_to_all(
        grad_outbound.reshape(experts, capacity, channels), "expert", split_axis=0, concat_axis=0, tiled=True
    )
    both = feat_width + channels
    inbound = jnp.concatenate(
        [received.reshape(slots, feat_width), grad_inbound.reshape(slots, channels)], axis=1
    )
    back, part = expert(inbound, w_first[0], w_second[0], 512)
    returned = lax.all_to_all(
        back.reshape(experts, capacity, both), "expert", split_axis=0, concat_axis=0, tiled=True
    )
    mixed = lax.dot_general(
        route,
        returned.reshape(slots, both),
        (((0,), (0,)), ((), ())),
        preferred_element_type=jnp.float32,
    ).astype(jnp.bfloat16)
    patch_grid = mixed[:, :channels].reshape(1, rows_y, depth_cells, channels)
    imitated = conv_block(patch_grid, kernel, False).reshape(1, rows_y, depth_cells, channels)
    feat_grad = mixed[:, channels:].reshape(1, rows_y, depth_cells, feat_width)

    grads = tree_scatter(part.reshape(slabs, hidden // slabs, both), (0, 1, 2, 3))
    grad_one = grads[:, :feat_width].T
    grad_two = grads[:, feat_width:]
    return (imitated, feat_grad, grad_one[None], grad_two[None])


def solution(mesh):
    in_specs = (
        P("dp", "expert", None, None),
        P("dp", "expert", None, None),
        P("expert", None, None),
        P("expert", None, None),
        P(),
        P("dp", "expert", None, None),
    )
    out_specs = (
        P("dp", "expert", None, None),
        P("dp", "expert", None, None),
        P("expert", None, "dp"),
        P("expert", "dp", None),
    )
    return jax.shard_map(
        per_device, mesh=mesh, in_specs=in_specs, out_specs=out_specs, check_vma=False
    )
```

```python
import functools

import jax
import jax.numpy as jnp
from jax import lax
from jax.experimental import pallas as pl
from jax.experimental.pallas import tpu as pltpu
from jax.sharding import PartitionSpec as P


def extended(x, sides, width):
    for axis, dim in sides:
        size, length = (lax.axis_size(axis), x.shape[dim])
        up = [(i, (i + 1) % size) for i in range(size - 1)]
        down = [(j, i) for i, j in up]
        last = lax.slice_in_dim(x, length - width, length, axis=dim)
        first = lax.slice_in_dim(x, 0, width, axis=dim)
        before = lax.ppermute(last, axis, up)
        after = lax.ppermute(first, axis, down)
        x = jnp.concatenate([before, x, after], axis=dim)
    return x


def gelu_act(value):
    return jax.nn.gelu(value, approximate=True)


def gelu_back(preact, upstream):
    return jax.vjp(gelu_act, preact)[1](upstream)[0]


def tree_scatter(blocks, order):
    count = blocks.shape[0]
    me = lax.axis_index("dp")
    bits = count.bit_length() - 1
    x = blocks.reshape((2,) * bits + blocks.shape[1:])
    remaining = list(range(bits - 1, -1, -1))
    for bit in order:
        axis = remaining.index(bit)
        mine = (me >> bit) & 1
        keep = lax.dynamic_index_in_dim(x, mine, axis=axis, keepdims=False)
        send = lax.dynamic_index_in_dim(x, 1 - mine, axis=axis, keepdims=False)
        pairs = [(i, i ^ (1 << bit)) for i in range(count)]
        got = lax.ppermute(send.astype(jnp.bfloat16), "dp", pairs)
        x = keep + got.astype(jnp.float32)
        remaining.pop(axis)
    return x


def conv_kernel(flip, shifted_ref, taps_ref, out_ref, acc_ref):
    rows_y = shifted_ref.shape[3] - 2
    depth_cells = shifted_ref.shape[4]
    width = shifted_ref.shape[5]
    acc_ref[...] = jnp.zeros_like(acc_ref)
    for plane in range(3):
        for across in range(3):
            for along in range(3):
                tap = 9 * plane + 3 * across + along
                piece = shifted_ref[0, along, plane, across : across + rows_y]
                piece = piece.reshape(rows_y * depth_cells, width)
                if flip:
                    acc_ref[...] += lax.dot_general(
                        piece,
                        taps_ref[26 - tap],
                        (((1,), (1,)), ((), ())),
                        preferred_element_type=jnp.float32,
                    )
                else:
                    acc_ref[...] += jnp.dot(
                        piece, taps_ref[tap], preferred_element_type=jnp.float32
                    )
    out_ref[...] = acc_ref[...].astype(out_ref.dtype)


def halo(grid):
    slabs, experts = lax.axis_size("dp"), lax.axis_size("expert")
    block = grid[0]
    last, first = block[-1:], block[:1]

    def moved(value, step_dp, step_expert):
        pairs = []
        for d in range(slabs):
            for e in range(experts):
                dd, ee = d + step_dp, e + step_expert
                if 0 <= dd < slabs and 0 <= ee < experts:
                    pairs.append((d * experts + e, dd * experts + ee))
        return lax.ppermute(value, ("dp", "expert"), pairs)

    lower = [moved(last, 1, 1), moved(block, 1, 0), moved(first, 1, -1)]
    middle = [moved(last, 0, 1), block, moved(first, 0, -1)]
    upper = [moved(last, -1, 1), moved(block, -1, 0), moved(first, -1, -1)]
    planes = [jnp.concatenate(side, axis=0) for side in (lower, middle, upper)]
    return jnp.stack(planes, axis=0)


def conv_block(grid, kernel, flip):
    padded = halo(grid)
    padded = jnp.pad(padded, ((0, 0), (0, 0), (1, 1), (0, 0)))
    depth_cells = grid.shape[2]
    shifted = jnp.stack(
        [padded[:, :, along : along + depth_cells] for along in range(3)], axis=0
    )[None]
    count = grid.shape[1] * depth_cells
    width = kernel.shape[2]
    return pl.pallas_call(
        functools.partial(conv_kernel, flip),
        out_shape=jax.ShapeDtypeStruct((count, width), jnp.bfloat16),
        in_specs=[pl.BlockSpec(memory_space=pltpu.VMEM)] * 2,
        out_specs=pl.BlockSpec(memory_space=pltpu.VMEM),
        scratch_shapes=[pltpu.VMEM((count, width), jnp.float32)],
        compiler_params=pltpu.CompilerParams(vmem_limit_bytes=48 * 1024 * 1024),
        cost_estimate=pl.CostEstimate(
            flops=2 * 27 * count * width * width,
            transcendentals=0,
            bytes_accessed=2 * (shifted.size + kernel.size + count * width),
        ),
    )(shifted, kernel)


def expert_kernel(
    cols, rows_ref, first_ref, second_ref, prior_ref, back_ref, part_ref, result_acc, input_acc
):
    step = pl.program_id(0)

    @pl.when(step == 0)
    def _():
        result_acc[...] = jnp.zeros_like(result_acc)
        input_acc[...] = jnp.zeros_like(input_acc)

    rows = rows_ref[:, :cols]
    grads = rows_ref[:, cols:]
    first = first_ref[...]
    second = second_ref[...]
    preact = jnp.dot(rows, first, preferred_element_type=jnp.float32)
    activation = gelu_act(preact).astype(jnp.bfloat16)
    result_acc[...] += jnp.dot(activation, second, preferred_element_type=jnp.float32)
    upstream = lax.dot_general(
        grads, second, (((1,), (1,)), ((), ())), preferred_element_type=jnp.float32
    )
    gate_grad = gelu_back(preact, upstream).astype(jnp.bfloat16)
    input_acc[...] += lax.dot_general(
        gate_grad, first, (((1,), (1,)), ((), ())), preferred_element_type=jnp.float32
    )
    part_ref[:, :cols] = prior_ref[:, :cols] + lax.dot_general(
        gate_grad, rows, (((0,), (0,)), ((), ())), preferred_element_type=jnp.float32
    )
    part_ref[:, cols:] = prior_ref[:, cols:] + lax.dot_general(
        activation, grads, (((0,), (0,)), ((), ())), preferred_element_type=jnp.float32
    )

    @pl.when(step == pl.num_programs(0) - 1)
    def _():
        width = result_acc.shape[1]
        back_ref[:, :width] = result_acc[...].astype(back_ref.dtype)
        back_ref[:, width:] = input_acc[...].astype(back_ref.dtype)


def expert(inbound, weight_one, weight_two, prior, chunk):
    slots, both = inbound.shape
    cols, hidden = weight_one.shape
    channels = weight_two.shape[1]
    flops = 2 * slots * hidden * (3 * cols + 3 * channels)
    return pl.pallas_call(
        functools.partial(expert_kernel, cols),
        grid=(hidden // chunk,),
        in_specs=[
            pl.BlockSpec((slots, both), lambda h: (0, 0)),
            pl.BlockSpec((cols, chunk), lambda h: (0, h)),
            pl.BlockSpec((chunk, channels), lambda h: (h, 0)),
            pl.BlockSpec((chunk, both), lambda h: (h, 0)),
        ],
        out_specs=[
            pl.BlockSpec((slots, both), lambda h: (0, 0)),
            pl.BlockSpec((chunk, both), lambda h: (h, 0)),
        ],
        out_shape=[
            jax.ShapeDtypeStruct((slots, both), jnp.bfloat16),
            jax.ShapeDtypeStruct((hidden, both), jnp.float32),
        ],
        scratch_shapes=[
            pltpu.VMEM((slots, channels), jnp.float32),
            pltpu.VMEM((slots, cols), jnp.float32),
        ],
        input_output_aliases={3: 1},
        compiler_params=pltpu.CompilerParams(
            dimension_semantics=("arbitrary",), vmem_limit_bytes=56 * 1024 * 1024
        ),
        cost_estimate=pl.CostEstimate(
            flops=flops,
            transcendentals=slots * hidden,
            bytes_accessed=2 * (2 * slots * both + hidden * (cols + channels)) + 8 * hidden * both,
        ),
    )(inbound, weight_one, weight_two, prior)


def per_device(feats, labels, w_first, w_second, kernel, cotangent):
    experts = lax.axis_size("expert")
    slabs = lax.axis_size("dp")
    rows_y = feats.shape[1]
    depth_cells = feats.shape[2]
    feat_width = feats.shape[3]
    channels = kernel.shape[2]
    hidden = w_first.shape[2]
    patch_count = rows_y * depth_cells
    capacity = 2 * patch_count // experts
    slots = experts * capacity
    regime = labels.reshape(patch_count)
    onehot = (regime[:, None] == jnp.arange(experts, dtype=jnp.int32)[None, :]).astype(
        jnp.bfloat16
    )
    lower = (
        jnp.arange(patch_count)[:, None] >= jnp.arange(patch_count)[None, :]
    ).astype(jnp.bfloat16)
    ranking = jnp.dot(lower, onehot, preferred_element_type=jnp.float32)
    slot_index = jnp.sum(ranking * onehot.astype(jnp.float32), axis=1).astype(jnp.int32) - 1
    target = regime * capacity + slot_index
    route = (target[None, :] == jnp.arange(slots, dtype=jnp.int32)[:, None]).astype(jnp.bfloat16)

    flat_feats = feats.reshape(patch_count, feat_width)
    outbound = jnp.dot(route, flat_feats, preferred_element_type=jnp.float32).astype(jnp.bfloat16)
    outbound = outbound.reshape(experts, capacity, feat_width)
    field_rows = conv_block(cotangent, kernel, True)
    grad_outbound = jnp.dot(route, field_rows, preferred_element_type=jnp.float32).astype(
        jnp.bfloat16
    )
    grad_outbound = grad_outbound.reshape(experts, capacity, channels)
    both = feat_width + channels
    half = capacity // 2
    part = jnp.zeros((hidden, both), jnp.float32)
    backs = []
    for piece in range(2):
        window = slice(piece * half, (piece + 1) * half)
        received = lax.all_to_all(
            outbound[:, window], "expert", split_axis=0, concat_axis=0, tiled=True
        )
        grad_inbound = lax.all_to_all(
            grad_outbound[:, window], "expert", split_axis=0, concat_axis=0, tiled=True
        )
        inbound = jnp.concatenate(
            [received.reshape(slots // 2, feat_width), grad_inbound.reshape(slots // 2, channels)],
            axis=1,
        )
        back, part = expert(inbound, w_first[0], w_second[0], part, 512)
        backs.append(
            lax.all_to_all(
                back.reshape(experts, half, both), "expert", split_axis=0, concat_axis=0, tiled=True
            )
        )
    returned = jnp.concatenate(backs, axis=1)
    mixed = lax.dot_general(
        route,
        returned.reshape(slots, both),
        (((0,), (0,)), ((), ())),
        preferred_element_type=jnp.float32,
    ).astype(jnp.bfloat16)
    patch_grid = mixed[:, :channels].reshape(1, rows_y, depth_cells, channels)
    imitated = conv_block(patch_grid, kernel, False).reshape(1, rows_y, depth_cells, channels)
    feat_grad = mixed[:, channels:].reshape(1, rows_y, depth_cells, feat_width)

    grads = tree_scatter(part.reshape(slabs, hidden // slabs, both), (0, 1, 2, 3))
    grad_one = grads[:, :feat_width].T
    grad_two = grads[:, feat_width:]
    return (imitated, feat_grad, grad_one[None], grad_two[None])


def solution(mesh):
    in_specs = (
        P("dp", "expert", None, None),
        P("dp", "expert", None, None),
        P("expert", None, None),
        P("expert", None, None),
        P(),
        P("dp", "expert", None, None),
    )
    out_specs = (
        P("dp", "expert", None, None),
        P("dp", "expert", None, None),
        P("expert", None, "dp"),
        P("expert", "dp", None),
    )
    return jax.shard_map(
        per_device, mesh=mesh, in_specs=in_specs, out_specs=out_specs, check_vma=False
    )
```

```python
import functools

import jax
import jax.numpy as jnp
from jax import lax
from jax.experimental import pallas as pl
from jax.experimental.pallas import tpu as pltpu
from jax.sharding import PartitionSpec as P


def extended(x, sides, width):
    for axis, dim in sides:
        size, length = (lax.axis_size(axis), x.shape[dim])
        up = [(i, (i + 1) % size) for i in range(size - 1)]
        down = [(j, i) for i, j in up]
        last = lax.slice_in_dim(x, length - width, length, axis=dim)
        first = lax.slice_in_dim(x, 0, width, axis=dim)
        before = lax.ppermute(last, axis, up)
        after = lax.ppermute(first, axis, down)
        x = jnp.concatenate([before, x, after], axis=dim)
    return x


def gelu_act(value):
    return jax.nn.gelu(value, approximate=True)


def gelu_back(preact, upstream):
    return jax.vjp(gelu_act, preact)[1](upstream)[0]


def tree_scatter(blocks, order):
    count = blocks.shape[0]
    me = lax.axis_index("dp")
    bits = count.bit_length() - 1
    x = blocks.reshape((2,) * bits + blocks.shape[1:])
    remaining = list(range(bits - 1, -1, -1))
    for bit in order:
        axis = remaining.index(bit)
        mine = (me >> bit) & 1
        keep = lax.dynamic_index_in_dim(x, mine, axis=axis, keepdims=False)
        send = lax.dynamic_index_in_dim(x, 1 - mine, axis=axis, keepdims=False)
        pairs = [(i, i ^ (1 << bit)) for i in range(count)]
        got = lax.ppermute(send.astype(jnp.bfloat16), "dp", pairs)
        x = keep + got.astype(jnp.float32)
        remaining.pop(axis)
    return x


def conv_kernel(flip, shifted_ref, taps_ref, out_ref, acc_ref):
    rows_y = shifted_ref.shape[3] - 2
    depth_cells = shifted_ref.shape[4]
    width = shifted_ref.shape[5]
    acc_ref[...] = jnp.zeros_like(acc_ref)
    for plane in range(3):
        for across in range(3):
            for along in range(3):
                tap = 9 * plane + 3 * across + along
                piece = shifted_ref[0, along, plane, across : across + rows_y]
                piece = piece.reshape(rows_y * depth_cells, width)
                if flip:
                    acc_ref[...] += lax.dot_general(
                        piece,
                        taps_ref[26 - tap],
                        (((1,), (1,)), ((), ())),
                        preferred_element_type=jnp.float32,
                    )
                else:
                    acc_ref[...] += jnp.dot(
                        piece, taps_ref[tap], preferred_element_type=jnp.float32
                    )
    out_ref[...] = acc_ref[...].astype(out_ref.dtype)


def conv_block(grid, kernel, flip):
    padded = extended(grid, (("dp", 0), ("expert", 1)), 1)
    padded = jnp.pad(padded, ((0, 0), (0, 0), (1, 1), (0, 0)))
    depth_cells = grid.shape[2]
    shifted = jnp.stack(
        [padded[:, :, along : along + depth_cells] for along in range(3)], axis=0
    )[None]
    count = grid.shape[1] * depth_cells
    width = kernel.shape[2]
    return pl.pallas_call(
        functools.partial(conv_kernel, flip),
        out_shape=jax.ShapeDtypeStruct((count, width), jnp.bfloat16),
        in_specs=[pl.BlockSpec(memory_space=pltpu.VMEM)] * 2,
        out_specs=pl.BlockSpec(memory_space=pltpu.VMEM),
        scratch_shapes=[pltpu.VMEM((count, width), jnp.float32)],
        compiler_params=pltpu.CompilerParams(vmem_limit_bytes=48 * 1024 * 1024),
        cost_estimate=pl.CostEstimate(
            flops=2 * 27 * count * width * width,
            transcendentals=0,
            bytes_accessed=2 * (shifted.size + kernel.size + count * width),
        ),
    )(shifted, kernel)


def expert_kernel(
    cols, rows_ref, first_ref, second_ref, back_ref, part_ref, result_acc, input_acc
):
    step = pl.program_id(0)

    @pl.when(step == 0)
    def _():
        result_acc[...] = jnp.zeros_like(result_acc)
        input_acc[...] = jnp.zeros_like(input_acc)

    rows = rows_ref[:, :cols]
    grads = rows_ref[:, cols:]
    first = first_ref[...]
    second = second_ref[...]
    preact = jnp.dot(rows, first, preferred_element_type=jnp.float32)
    activation = gelu_act(preact).astype(jnp.bfloat16)
    result_acc[...] += jnp.dot(activation, second, preferred_element_type=jnp.float32)
    upstream = lax.dot_general(
        grads, second, (((1,), (1,)), ((), ())), preferred_element_type=jnp.float32
    )
    gate_grad = gelu_back(preact, upstream).astype(jnp.bfloat16)
    input_acc[...] += lax.dot_general(
        gate_grad, first, (((1,), (1,)), ((), ())), preferred_element_type=jnp.float32
    )
    part_ref[:, :cols] = lax.dot_general(
        gate_grad, rows, (((0,), (0,)), ((), ())), preferred_element_type=jnp.float32
    )
    part_ref[:, cols:] = lax.dot_general(
        activation, grads, (((0,), (0,)), ((), ())), preferred_element_type=jnp.float32
    )

    @pl.when(step == pl.num_programs(0) - 1)
    def _():
        width = result_acc.shape[1]
        back_ref[:, :width] = result_acc[...].astype(back_ref.dtype)
        back_ref[:, width:] = input_acc[...].astype(back_ref.dtype)


def expert(inbound, weight_one, weight_two, chunk):
    slots, both = inbound.shape
    cols, hidden = weight_one.shape
    channels = weight_two.shape[1]
    flops = 2 * slots * hidden * (3 * cols + 3 * channels)
    return pl.pallas_call(
        functools.partial(expert_kernel, cols),
        grid=(hidden // chunk,),
        in_specs=[
            pl.BlockSpec((slots, both), lambda h: (0, 0)),
            pl.BlockSpec((cols, chunk), lambda h: (0, h)),
            pl.BlockSpec((chunk, channels), lambda h: (h, 0)),
        ],
        out_specs=[
            pl.BlockSpec((slots, both), lambda h: (0, 0)),
            pl.BlockSpec((chunk, both), lambda h: (h, 0)),
        ],
        out_shape=[
            jax.ShapeDtypeStruct((slots, both), jnp.bfloat16),
            jax.ShapeDtypeStruct((hidden, both), jnp.float32),
        ],
        scratch_shapes=[
            pltpu.VMEM((slots, channels), jnp.float32),
            pltpu.VMEM((slots, cols), jnp.float32),
        ],
        compiler_params=pltpu.CompilerParams(
            dimension_semantics=("arbitrary",), vmem_limit_bytes=56 * 1024 * 1024
        ),
        cost_estimate=pl.CostEstimate(
            flops=flops,
            transcendentals=slots * hidden,
            bytes_accessed=2 * (2 * slots * both + hidden * (cols + channels)) + 4 * hidden * both,
        ),
    )(inbound, weight_one, weight_two)


def per_device(feats, labels, w_first, w_second, kernel, cotangent):
    experts = lax.axis_size("expert")
    slabs = lax.axis_size("dp")
    rows_y = feats.shape[1]
    depth_cells = feats.shape[2]
    feat_width = feats.shape[3]
    channels = kernel.shape[2]
    hidden = w_first.shape[2]
    patch_count = rows_y * depth_cells
    capacity = 2 * patch_count // experts
    slots = experts * capacity
    regime = labels.reshape(patch_count)
    onehot = (regime[:, None] == jnp.arange(experts, dtype=jnp.int32)[None, :]).astype(
        jnp.bfloat16
    )
    lower = (
        jnp.arange(patch_count)[:, None] >= jnp.arange(patch_count)[None, :]
    ).astype(jnp.bfloat16)
    ranking = jnp.dot(lower, onehot, preferred_element_type=jnp.float32)
    slot_index = jnp.sum(ranking * onehot.astype(jnp.float32), axis=1).astype(jnp.int32) - 1
    target = regime * capacity + slot_index
    route = (target[None, :] == jnp.arange(slots, dtype=jnp.int32)[:, None]).astype(jnp.bfloat16)

    flat_feats = feats.reshape(patch_count, feat_width)
    outbound = jnp.dot(route, flat_feats, preferred_element_type=jnp.float32).astype(jnp.bfloat16)
    received = lax.all_to_all(
        outbound.reshape(experts, capacity, feat_width), "expert", split_axis=0, concat_axis=0, tiled=True
    )
    field_rows = conv_block(cotangent, kernel, True)
    grad_outbound = jnp.dot(route, field_rows, preferred_element_type=jnp.float32).astype(
        jnp.bfloat16
    )
    grad_inbound = lax.all_to_all(
        grad_outbound.reshape(experts, capacity, channels), "expert", split_axis=0, concat_axis=0, tiled=True
    )
    both = feat_width + channels
    inbound = jnp.concatenate(
        [received.reshape(slots, feat_width), grad_inbound.reshape(slots, channels)], axis=1
    )
    back, part = expert(inbound, w_first[0], w_second[0], 512)
    returned = lax.all_to_all(
        back.reshape(experts, capacity, both), "expert", split_axis=0, concat_axis=0, tiled=True
    )
    returned, part = lax.optimization_barrier((returned, part))
    mixed = lax.dot_general(
        route,
        returned.reshape(slots, both),
        (((0,), (0,)), ((), ())),
        preferred_element_type=jnp.float32,
    ).astype(jnp.bfloat16)
    patch_grid = mixed[:, :channels].reshape(1, rows_y, depth_cells, channels)
    imitated = conv_block(patch_grid, kernel, False).reshape(1, rows_y, depth_cells, channels)
    feat_grad = mixed[:, channels:].reshape(1, rows_y, depth_cells, feat_width)

    grads = tree_scatter(part.reshape(slabs, hidden // slabs, both), (0, 1, 2, 3))
    grad_one = grads[:, :feat_width].T
    grad_two = grads[:, feat_width:]
    return (imitated, feat_grad, grad_one[None], grad_two[None])


def solution(mesh):
    in_specs = (
        P("dp", "expert", None, None),
        P("dp", "expert", None, None),
        P("expert", None, None),
        P("expert", None, None),
        P(),
        P("dp", "expert", None, None),
    )
    out_specs = (
        P("dp", "expert", None, None),
        P("dp", "expert", None, None),
        P("expert", None, "dp"),
        P("expert", "dp", None),
    )
    return jax.shard_map(
        per_device, mesh=mesh, in_specs=in_specs, out_specs=out_specs, check_vma=False
    )
```

```python
import functools

import jax
import jax.numpy as jnp
from jax import lax
from jax.experimental import pallas as pl
from jax.experimental.pallas import tpu as pltpu
from jax.sharding import PartitionSpec as P


def extended(x, sides, width):
    for axis, dim in sides:
        size, length = (lax.axis_size(axis), x.shape[dim])
        up = [(i, (i + 1) % size) for i in range(size - 1)]
        down = [(j, i) for i, j in up]
        last = lax.slice_in_dim(x, length - width, length, axis=dim)
        first = lax.slice_in_dim(x, 0, width, axis=dim)
        before = lax.ppermute(last, axis, up)
        after = lax.ppermute(first, axis, down)
        x = jnp.concatenate([before, x, after], axis=dim)
    return x


def gelu_act(value):
    return jax.nn.gelu(value, approximate=True)


def gelu_back(preact, upstream):
    return jax.vjp(gelu_act, preact)[1](upstream)[0]


def tree_scatter(blocks, order):
    count = blocks.shape[0]
    me = lax.axis_index("dp")
    bits = count.bit_length() - 1
    x = blocks.reshape((2,) * bits + blocks.shape[1:])
    remaining = list(range(bits - 1, -1, -1))
    for bit in order:
        axis = remaining.index(bit)
        mine = (me >> bit) & 1
        keep = lax.dynamic_index_in_dim(x, mine, axis=axis, keepdims=False)
        send = lax.dynamic_index_in_dim(x, 1 - mine, axis=axis, keepdims=False)
        pairs = [(i, i ^ (1 << bit)) for i in range(count)]
        got = lax.ppermute(send.astype(jnp.bfloat16), "dp", pairs)
        x = keep + got.astype(jnp.float32)
        remaining.pop(axis)
    return x


def conv_kernel(flip, shifted_ref, taps_ref, out_ref, acc_ref):
    rows_y = shifted_ref.shape[3] - 2
    depth_cells = shifted_ref.shape[4]
    width = shifted_ref.shape[5]
    acc_ref[...] = jnp.zeros_like(acc_ref)
    for plane in range(3):
        for across in range(3):
            for along in range(3):
                tap = 9 * plane + 3 * across + along
                piece = shifted_ref[0, along, plane, across : across + rows_y]
                piece = piece.reshape(rows_y * depth_cells, width)
                if flip:
                    acc_ref[...] += lax.dot_general(
                        piece,
                        taps_ref[26 - tap],
                        (((1,), (1,)), ((), ())),
                        preferred_element_type=jnp.float32,
                    )
                else:
                    acc_ref[...] += jnp.dot(
                        piece, taps_ref[tap], preferred_element_type=jnp.float32
                    )
    out_ref[...] = acc_ref[...].astype(out_ref.dtype)


def conv_block(grid, kernel, flip, after=None):
    padded = extended(grid, (("dp", 0), ("expert", 1)), 1)
    if after is not None:
        after, padded = lax.optimization_barrier((after, padded))
    padded = jnp.pad(padded, ((0, 0), (0, 0), (1, 1), (0, 0)))
    depth_cells = grid.shape[2]
    shifted = jnp.stack(
        [padded[:, :, along : along + depth_cells] for along in range(3)], axis=0
    )[None]
    count = grid.shape[1] * depth_cells
    width = kernel.shape[2]
    result = pl.pallas_call(
        functools.partial(conv_kernel, flip),
        out_shape=jax.ShapeDtypeStruct((count, width), jnp.bfloat16),
        in_specs=[pl.BlockSpec(memory_space=pltpu.VMEM)] * 2,
        out_specs=pl.BlockSpec(memory_space=pltpu.VMEM),
        scratch_shapes=[pltpu.VMEM((count, width), jnp.float32)],
        compiler_params=pltpu.CompilerParams(vmem_limit_bytes=48 * 1024 * 1024),
        cost_estimate=pl.CostEstimate(
            flops=2 * 27 * count * width * width,
            transcendentals=0,
            bytes_accessed=2 * (shifted.size + kernel.size + count * width),
        ),
    )(shifted, kernel)
    if after is not None:
        return result, after
    return result


def expert_kernel(
    cols, rows_ref, first_ref, second_ref, back_ref, part_ref, result_acc, input_acc
):
    step = pl.program_id(0)

    @pl.when(step == 0)
    def _():
        result_acc[...] = jnp.zeros_like(result_acc)
        input_acc[...] = jnp.zeros_like(input_acc)

    rows = rows_ref[:, :cols]
    grads = rows_ref[:, cols:]
    first = first_ref[...]
    second = second_ref[...]
    preact = jnp.dot(rows, first, preferred_element_type=jnp.float32)
    activation = gelu_act(preact).astype(jnp.bfloat16)
    result_acc[...] += jnp.dot(activation, second, preferred_element_type=jnp.float32)
    upstream = lax.dot_general(
        grads, second, (((1,), (1,)), ((), ())), preferred_element_type=jnp.float32
    )
    gate_grad = gelu_back(preact, upstream).astype(jnp.bfloat16)
    input_acc[...] += lax.dot_general(
        gate_grad, first, (((1,), (1,)), ((), ())), preferred_element_type=jnp.float32
    )
    part_ref[:, :cols] = lax.dot_general(
        gate_grad, rows, (((0,), (0,)), ((), ())), preferred_element_type=jnp.float32
    )
    part_ref[:, cols:] = lax.dot_general(
        activation, grads, (((0,), (0,)), ((), ())), preferred_element_type=jnp.float32
    )

    @pl.when(step == pl.num_programs(0) - 1)
    def _():
        width = result_acc.shape[1]
        back_ref[:, :width] = result_acc[...].astype(back_ref.dtype)
        back_ref[:, width:] = input_acc[...].astype(back_ref.dtype)


def expert(inbound, weight_one, weight_two, chunk):
    slots, both = inbound.shape
    cols, hidden = weight_one.shape
    channels = weight_two.shape[1]
    flops = 2 * slots * hidden * (3 * cols + 3 * channels)
    return pl.pallas_call(
        functools.partial(expert_kernel, cols),
        grid=(hidden // chunk,),
        in_specs=[
            pl.BlockSpec((slots, both), lambda h: (0, 0)),
            pl.BlockSpec((cols, chunk), lambda h: (0, h)),
            pl.BlockSpec((chunk, channels), lambda h: (h, 0)),
        ],
        out_specs=[
            pl.BlockSpec((slots, both), lambda h: (0, 0)),
            pl.BlockSpec((chunk, both), lambda h: (h, 0)),
        ],
        out_shape=[
            jax.ShapeDtypeStruct((slots, both), jnp.bfloat16),
            jax.ShapeDtypeStruct((hidden, both), jnp.float32),
        ],
        scratch_shapes=[
            pltpu.VMEM((slots, channels), jnp.float32),
            pltpu.VMEM((slots, cols), jnp.float32),
        ],
        compiler_params=pltpu.CompilerParams(
            dimension_semantics=("arbitrary",), vmem_limit_bytes=56 * 1024 * 1024
        ),
        cost_estimate=pl.CostEstimate(
            flops=flops,
            transcendentals=slots * hidden,
            bytes_accessed=2 * (2 * slots * both + hidden * (cols + channels)) + 4 * hidden * both,
        ),
    )(inbound, weight_one, weight_two)


def per_device(feats, labels, w_first, w_second, kernel, cotangent):
    experts = lax.axis_size("expert")
    slabs = lax.axis_size("dp")
    rows_y = feats.shape[1]
    depth_cells = feats.shape[2]
    feat_width = feats.shape[3]
    channels = kernel.shape[2]
    hidden = w_first.shape[2]
    patch_count = rows_y * depth_cells
    capacity = 2 * patch_count // experts
    slots = experts * capacity
    regime = labels.reshape(patch_count)
    onehot = (regime[:, None] == jnp.arange(experts, dtype=jnp.int32)[None, :]).astype(
        jnp.bfloat16
    )
    lower = (
        jnp.arange(patch_count)[:, None] >= jnp.arange(patch_count)[None, :]
    ).astype(jnp.bfloat16)
    ranking = jnp.dot(lower, onehot, preferred_element_type=jnp.float32)
    slot_index = jnp.sum(ranking * onehot.astype(jnp.float32), axis=1).astype(jnp.int32) - 1
    target = regime * capacity + slot_index
    route = (target[None, :] == jnp.arange(slots, dtype=jnp.int32)[:, None]).astype(jnp.bfloat16)

    flat_feats = feats.reshape(patch_count, feat_width)
    outbound = jnp.dot(route, flat_feats, preferred_element_type=jnp.float32).astype(jnp.bfloat16)
    received = lax.all_to_all(
        outbound.reshape(experts, capacity, feat_width), "expert", split_axis=0, concat_axis=0, tiled=True
    )
    field_rows, received = conv_block(cotangent, kernel, True, received)
    grad_outbound = jnp.dot(route, field_rows, preferred_element_type=jnp.float32).astype(
        jnp.bfloat16
    )
    grad_inbound = lax.all_to_all(
        grad_outbound.reshape(experts, capacity, channels), "expert", split_axis=0, concat_axis=0, tiled=True
    )
    both = feat_width + channels
    inbound = jnp.concatenate(
        [received.reshape(slots, feat_width), grad_inbound.reshape(slots, channels)], axis=1
    )
    back, part = expert(inbound, w_first[0], w_second[0], 512)
    returned = lax.all_to_all(
        back.reshape(experts, capacity, both), "expert", split_axis=0, concat_axis=0, tiled=True
    )
    mixed = lax.dot_general(
        route,
        returned.reshape(slots, both),
        (((0,), (0,)), ((), ())),
        preferred_element_type=jnp.float32,
    ).astype(jnp.bfloat16)
    patch_grid = mixed[:, :channels].reshape(1, rows_y, depth_cells, channels)
    imitated = conv_block(patch_grid, kernel, False).reshape(1, rows_y, depth_cells, channels)
    feat_grad = mixed[:, channels:].reshape(1, rows_y, depth_cells, feat_width)

    grads = tree_scatter(part.reshape(slabs, hidden // slabs, both), (0, 1, 2, 3))
    grad_one = grads[:, :feat_width].T
    grad_two = grads[:, feat_width:]
    return (imitated, feat_grad, grad_one[None], grad_two[None])


def solution(mesh):
    in_specs = (
        P("dp", "expert", None, None),
        P("dp", "expert", None, None),
        P("expert", None, None),
        P("expert", None, None),
        P(),
        P("dp", "expert", None, None),
    )
    out_specs = (
        P("dp", "expert", None, None),
        P("dp", "expert", None, None),
        P("expert", None, "dp"),
        P("expert", "dp", None),
    )
    return jax.shard_map(
        per_device, mesh=mesh, in_specs=in_specs, out_specs=out_specs, check_vma=False
    )
```

```python
import functools

import jax
import jax.numpy as jnp
from jax import lax
from jax.experimental import pallas as pl
from jax.experimental.pallas import tpu as pltpu
from jax.sharding import PartitionSpec as P


def extended(x, sides, width):
    for axis, dim in sides:
        size, length = (lax.axis_size(axis), x.shape[dim])
        up = [(i, (i + 1) % size) for i in range(size - 1)]
        down = [(j, i) for i, j in up]
        last = lax.slice_in_dim(x, length - width, length, axis=dim)
        first = lax.slice_in_dim(x, 0, width, axis=dim)
        before = lax.ppermute(last, axis, up)
        after = lax.ppermute(first, axis, down)
        x = jnp.concatenate([before, x, after], axis=dim)
    return x


def gelu_act(value):
    return jax.nn.gelu(value, approximate=True)


def gelu_back(preact, upstream):
    return jax.vjp(gelu_act, preact)[1](upstream)[0]


def tree_scatter(blocks, order):
    count = blocks.shape[0]
    me = lax.axis_index("dp")
    bits = count.bit_length() - 1
    x = blocks.reshape((2,) * bits + blocks.shape[1:])
    remaining = list(range(bits - 1, -1, -1))
    for bit in order:
        axis = remaining.index(bit)
        mine = (me >> bit) & 1
        keep = lax.dynamic_index_in_dim(x, mine, axis=axis, keepdims=False)
        send = lax.dynamic_index_in_dim(x, 1 - mine, axis=axis, keepdims=False)
        pairs = [(i, i ^ (1 << bit)) for i in range(count)]
        got = lax.ppermute(send.astype(jnp.bfloat16), "dp", pairs)
        x = keep + got.astype(jnp.float32)
        remaining.pop(axis)
    return x


def conv_kernel(flip, shifted_ref, taps_ref, out_ref, acc_ref):
    rows_y = shifted_ref.shape[3] - 2
    depth_cells = shifted_ref.shape[4]
    width = shifted_ref.shape[5]
    acc_ref[...] = jnp.zeros_like(acc_ref)
    for plane in range(3):
        for across in range(3):
            for along in range(3):
                tap = 9 * plane + 3 * across + along
                piece = shifted_ref[0, along, plane, across : across + rows_y]
                piece = piece.reshape(rows_y * depth_cells, width)
                if flip:
                    acc_ref[...] += lax.dot_general(
                        piece,
                        taps_ref[26 - tap],
                        (((1,), (1,)), ((), ())),
                        preferred_element_type=jnp.float32,
                    )
                else:
                    acc_ref[...] += jnp.dot(
                        piece, taps_ref[tap], preferred_element_type=jnp.float32
                    )
    out_ref[...] = acc_ref[...].astype(out_ref.dtype)


def conv_block(grid, kernel, flip, after=None):
    padded = extended(grid, (("dp", 0), ("expert", 1)), 1)
    if after is not None:
        after, padded = lax.optimization_barrier((after, padded))
    padded = jnp.pad(padded, ((0, 0), (0, 0), (1, 1), (0, 0)))
    depth_cells = grid.shape[2]
    shifted = jnp.stack(
        [padded[:, :, along : along + depth_cells] for along in range(3)], axis=0
    )[None]
    count = grid.shape[1] * depth_cells
    width = kernel.shape[2]
    result = pl.pallas_call(
        functools.partial(conv_kernel, flip),
        out_shape=jax.ShapeDtypeStruct((count, width), jnp.bfloat16),
        in_specs=[pl.BlockSpec(memory_space=pltpu.VMEM)] * 2,
        out_specs=pl.BlockSpec(memory_space=pltpu.VMEM),
        scratch_shapes=[pltpu.VMEM((count, width), jnp.float32)],
        compiler_params=pltpu.CompilerParams(vmem_limit_bytes=48 * 1024 * 1024),
        cost_estimate=pl.CostEstimate(
            flops=2 * 27 * count * width * width,
            transcendentals=0,
            bytes_accessed=2 * (shifted.size + kernel.size + count * width),
        ),
    )(shifted, kernel)
    if after is not None:
        return result, after
    return result


def expert_kernel(
    cols, rows_ref, first_ref, second_ref, back_ref, part_ref, result_acc, input_acc
):
    step = pl.program_id(0)

    @pl.when(step == 0)
    def _():
        result_acc[...] = jnp.zeros_like(result_acc)
        input_acc[...] = jnp.zeros_like(input_acc)

    rows = rows_ref[:, :cols]
    grads = rows_ref[:, cols:]
    first = first_ref[...]
    second = second_ref[...]
    preact = jnp.dot(rows, first, preferred_element_type=jnp.float32)
    activation = gelu_act(preact).astype(jnp.bfloat16)
    result_acc[...] += jnp.dot(activation, second, preferred_element_type=jnp.float32)
    upstream = lax.dot_general(
        grads, second, (((1,), (1,)), ((), ())), preferred_element_type=jnp.float32
    )
    gate_grad = gelu_back(preact, upstream).astype(jnp.bfloat16)
    input_acc[...] += lax.dot_general(
        gate_grad, first, (((1,), (1,)), ((), ())), preferred_element_type=jnp.float32
    )
    part_ref[:, :cols] = lax.dot_general(
        gate_grad, rows, (((0,), (0,)), ((), ())), preferred_element_type=jnp.float32
    )
    part_ref[:, cols:] = lax.dot_general(
        activation, grads, (((0,), (0,)), ((), ())), preferred_element_type=jnp.float32
    )

    @pl.when(step == pl.num_programs(0) - 1)
    def _():
        width = result_acc.shape[1]
        back_ref[:, :width] = result_acc[...].astype(back_ref.dtype)
        back_ref[:, width:] = input_acc[...].astype(back_ref.dtype)


def expert(inbound, weight_one, weight_two, chunk):
    slots, both = inbound.shape
    cols, hidden = weight_one.shape
    channels = weight_two.shape[1]
    flops = 2 * slots * hidden * (3 * cols + 3 * channels)
    return pl.pallas_call(
        functools.partial(expert_kernel, cols),
        grid=(hidden // chunk,),
        in_specs=[
            pl.BlockSpec((slots, both), lambda h: (0, 0)),
            pl.BlockSpec((cols, chunk), lambda h: (0, h)),
            pl.BlockSpec((chunk, channels), lambda h: (h, 0)),
        ],
        out_specs=[
            pl.BlockSpec((slots, both), lambda h: (0, 0)),
            pl.BlockSpec((chunk, both), lambda h: (h, 0)),
        ],
        out_shape=[
            jax.ShapeDtypeStruct((slots, both), jnp.bfloat16),
            jax.ShapeDtypeStruct((hidden, both), jnp.float32),
        ],
        scratch_shapes=[
            pltpu.VMEM((slots, channels), jnp.float32),
            pltpu.VMEM((slots, cols), jnp.float32),
        ],
        compiler_params=pltpu.CompilerParams(
            dimension_semantics=("arbitrary",), vmem_limit_bytes=56 * 1024 * 1024
        ),
        cost_estimate=pl.CostEstimate(
            flops=flops,
            transcendentals=slots * hidden,
            bytes_accessed=2 * (2 * slots * both + hidden * (cols + channels)) + 4 * hidden * both,
        ),
    )(inbound, weight_one, weight_two)


def per_device(feats, labels, w_first, w_second, kernel, cotangent):
    experts = lax.axis_size("expert")
    slabs = lax.axis_size("dp")
    rows_y = feats.shape[1]
    depth_cells = feats.shape[2]
    feat_width = feats.shape[3]
    channels = kernel.shape[2]
    hidden = w_first.shape[2]
    patch_count = rows_y * depth_cells
    capacity = 2 * patch_count // experts
    slots = experts * capacity
    regime = labels.reshape(patch_count)
    onehot = (regime[:, None] == jnp.arange(experts, dtype=jnp.int32)[None, :]).astype(
        jnp.bfloat16
    )
    lower = (
        jnp.arange(patch_count)[:, None] >= jnp.arange(patch_count)[None, :]
    ).astype(jnp.bfloat16)
    ranking = jnp.dot(lower, onehot, preferred_element_type=jnp.float32)
    slot_index = jnp.sum(ranking * onehot.astype(jnp.float32), axis=1).astype(jnp.int32) - 1
    target = regime * capacity + slot_index
    route = (target[None, :] == jnp.arange(slots, dtype=jnp.int32)[:, None]).astype(jnp.bfloat16)

    flat_feats = feats.reshape(patch_count, feat_width)
    outbound = jnp.dot(route, flat_feats, preferred_element_type=jnp.float32).astype(jnp.bfloat16)
    received = lax.all_to_all(
        outbound.reshape(experts, capacity, feat_width), "expert", split_axis=0, concat_axis=0, tiled=True
    )
    field_rows, received = conv_block(cotangent, kernel, True, received)
    grad_outbound = jnp.dot(route, field_rows, preferred_element_type=jnp.float32).astype(
        jnp.bfloat16
    )
    grad_inbound = lax.all_to_all(
        grad_outbound.reshape(experts, capacity, channels), "expert", split_axis=0, concat_axis=0, tiled=True
    )
    both = feat_width + channels
    inbound = jnp.concatenate(
        [received.reshape(slots, feat_width), grad_inbound.reshape(slots, channels)], axis=1
    )
    back, part = expert(inbound, w_first[0], w_second[0], 512)
    returned = lax.all_to_all(
        back.reshape(experts, capacity, both), "expert", split_axis=0, concat_axis=0, tiled=True
    )
    mixed = lax.dot_general(
        route,
        returned.reshape(slots, both),
        (((0,), (0,)), ((), ())),
        preferred_element_type=jnp.float32,
    ).astype(jnp.bfloat16)
    patch_grid = mixed[:, :channels].reshape(1, rows_y, depth_cells, channels)
    imitated = conv_block(patch_grid, kernel, False).reshape(1, rows_y, depth_cells, channels)
    feat_grad = mixed[:, channels:].reshape(1, rows_y, depth_cells, feat_width)

    grads = lax.psum_scatter(
        part.astype(jnp.bfloat16), "dp", scatter_dimension=0, tiled=True
    ).astype(jnp.float32)
    grad_one = grads[:, :feat_width].T
    grad_two = grads[:, feat_width:]
    return (imitated, feat_grad, grad_one[None], grad_two[None])


def solution(mesh):
    in_specs = (
        P("dp", "expert", None, None),
        P("dp", "expert", None, None),
        P("expert", None, None),
        P("expert", None, None),
        P(),
        P("dp", "expert", None, None),
    )
    out_specs = (
        P("dp", "expert", None, None),
        P("dp", "expert", None, None),
        P("expert", None, "dp"),
        P("expert", "dp", None),
    )
    return jax.shard_map(
        per_device, mesh=mesh, in_specs=in_specs, out_specs=out_specs, check_vma=False
    )
```

```python
import functools

import jax
import jax.numpy as jnp
from jax import lax
from jax.experimental import pallas as pl
from jax.experimental.pallas import tpu as pltpu
from jax.sharding import PartitionSpec as P


def extended(x, sides, width):
    for axis, dim in sides:
        size, length = (lax.axis_size(axis), x.shape[dim])
        up = [(i, (i + 1) % size) for i in range(size - 1)]
        down = [(j, i) for i, j in up]
        last = lax.slice_in_dim(x, length - width, length, axis=dim)
        first = lax.slice_in_dim(x, 0, width, axis=dim)
        before = lax.ppermute(last, axis, up)
        after = lax.ppermute(first, axis, down)
        x = jnp.concatenate([before, x, after], axis=dim)
    return x


def gelu_act(value):
    return jax.nn.gelu(value, approximate=True)


def gelu_back(preact, upstream):
    return jax.vjp(gelu_act, preact)[1](upstream)[0]


def tree_scatter(blocks, order):
    count = blocks.shape[0]
    me = lax.axis_index("dp")
    bits = count.bit_length() - 1
    x = blocks.reshape((2,) * bits + blocks.shape[1:])
    remaining = list(range(bits - 1, -1, -1))
    for bit in order:
        axis = remaining.index(bit)
        mine = (me >> bit) & 1
        keep = lax.dynamic_index_in_dim(x, mine, axis=axis, keepdims=False)
        send = lax.dynamic_index_in_dim(x, 1 - mine, axis=axis, keepdims=False)
        pairs = [(i, i ^ (1 << bit)) for i in range(count)]
        got = lax.ppermute(send.astype(jnp.bfloat16), "dp", pairs)
        x = keep + got.astype(jnp.float32)
        remaining.pop(axis)
    return x


def conv_kernel(flip, shifted_ref, taps_ref, out_ref, acc_ref):
    rows_y = shifted_ref.shape[3] - 2
    depth_cells = shifted_ref.shape[4]
    width = shifted_ref.shape[5]
    acc_ref[...] = jnp.zeros_like(acc_ref)
    for plane in range(3):
        for across in range(3):
            for along in range(3):
                tap = 9 * plane + 3 * across + along
                piece = shifted_ref[0, along, plane, across : across + rows_y]
                piece = piece.reshape(rows_y * depth_cells, width)
                if flip:
                    acc_ref[...] += lax.dot_general(
                        piece,
                        taps_ref[26 - tap],
                        (((1,), (1,)), ((), ())),
                        preferred_element_type=jnp.float32,
                    )
                else:
                    acc_ref[...] += jnp.dot(
                        piece, taps_ref[tap], preferred_element_type=jnp.float32
                    )
    out_ref[...] = acc_ref[...].astype(out_ref.dtype)


def conv_block(grid, kernel, flip, after=None):
    padded = extended(grid, (("dp", 0), ("expert", 1)), 1)
    if after is not None:
        after, padded = lax.optimization_barrier((after, padded))
    padded = jnp.pad(padded, ((0, 0), (0, 0), (1, 1), (0, 0)))
    depth_cells = grid.shape[2]
    shifted = jnp.stack(
        [padded[:, :, along : along + depth_cells] for along in range(3)], axis=0
    )[None]
    count = grid.shape[1] * depth_cells
    width = kernel.shape[2]
    result = pl.pallas_call(
        functools.partial(conv_kernel, flip),
        out_shape=jax.ShapeDtypeStruct((count, width), jnp.bfloat16),
        in_specs=[pl.BlockSpec(memory_space=pltpu.VMEM)] * 2,
        out_specs=pl.BlockSpec(memory_space=pltpu.VMEM),
        scratch_shapes=[pltpu.VMEM((count, width), jnp.float32)],
        compiler_params=pltpu.CompilerParams(vmem_limit_bytes=48 * 1024 * 1024),
        cost_estimate=pl.CostEstimate(
            flops=2 * 27 * count * width * width,
            transcendentals=0,
            bytes_accessed=2 * (shifted.size + kernel.size + count * width),
        ),
    )(shifted, kernel)
    if after is not None:
        return result, after
    return result


def expert_kernel(
    cols, rows_ref, first_ref, second_ref, back_ref, part_ref, result_acc, input_acc
):
    step = pl.program_id(0)

    @pl.when(step == 0)
    def _():
        result_acc[...] = jnp.zeros_like(result_acc)
        input_acc[...] = jnp.zeros_like(input_acc)

    rows = rows_ref[:, :cols]
    grads = rows_ref[:, cols:]
    first = first_ref[...]
    second = second_ref[...]
    preact = jnp.dot(rows, first, preferred_element_type=jnp.float32)
    activation = gelu_act(preact).astype(jnp.bfloat16)
    result_acc[...] += jnp.dot(activation, second, preferred_element_type=jnp.float32)
    upstream = lax.dot_general(
        grads, second, (((1,), (1,)), ((), ())), preferred_element_type=jnp.float32
    )
    gate_grad = gelu_back(preact, upstream).astype(jnp.bfloat16)
    input_acc[...] += lax.dot_general(
        gate_grad, first, (((1,), (1,)), ((), ())), preferred_element_type=jnp.float32
    )
    part_ref[:, :cols] = lax.dot_general(
        gate_grad, rows, (((0,), (0,)), ((), ())), preferred_element_type=jnp.float32
    )
    part_ref[:, cols:] = lax.dot_general(
        activation, grads, (((0,), (0,)), ((), ())), preferred_element_type=jnp.float32
    )

    @pl.when(step == pl.num_programs(0) - 1)
    def _():
        width = result_acc.shape[1]
        back_ref[:, :width] = result_acc[...].astype(back_ref.dtype)
        back_ref[:, width:] = input_acc[...].astype(back_ref.dtype)


def expert(inbound, weight_one, weight_two, chunk):
    slots, both = inbound.shape
    cols, hidden = weight_one.shape
    channels = weight_two.shape[1]
    flops = 2 * slots * hidden * (3 * cols + 3 * channels)
    return pl.pallas_call(
        functools.partial(expert_kernel, cols),
        grid=(hidden // chunk,),
        in_specs=[
            pl.BlockSpec((slots, both), lambda h: (0, 0)),
            pl.BlockSpec((cols, chunk), lambda h: (0, h)),
            pl.BlockSpec((chunk, channels), lambda h: (h, 0)),
        ],
        out_specs=[
            pl.BlockSpec((slots, both), lambda h: (0, 0)),
            pl.BlockSpec((chunk, both), lambda h: (h, 0)),
        ],
        out_shape=[
            jax.ShapeDtypeStruct((slots, both), jnp.bfloat16),
            jax.ShapeDtypeStruct((hidden, both), jnp.float32),
        ],
        scratch_shapes=[
            pltpu.VMEM((slots, channels), jnp.float32),
            pltpu.VMEM((slots, cols), jnp.float32),
        ],
        compiler_params=pltpu.CompilerParams(
            dimension_semantics=("arbitrary",), vmem_limit_bytes=56 * 1024 * 1024
        ),
        cost_estimate=pl.CostEstimate(
            flops=flops,
            transcendentals=slots * hidden,
            bytes_accessed=2 * (2 * slots * both + hidden * (cols + channels)) + 4 * hidden * both,
        ),
    )(inbound, weight_one, weight_two)


def per_device(feats, labels, w_first, w_second, kernel, cotangent):
    experts = lax.axis_size("expert")
    slabs = lax.axis_size("dp")
    rows_y = feats.shape[1]
    depth_cells = feats.shape[2]
    feat_width = feats.shape[3]
    channels = kernel.shape[2]
    hidden = w_first.shape[2]
    patch_count = rows_y * depth_cells
    capacity = 2 * patch_count // experts
    slots = experts * capacity
    regime = labels.reshape(patch_count)
    onehot = (regime[:, None] == jnp.arange(experts, dtype=jnp.int32)[None, :]).astype(
        jnp.bfloat16
    )
    lower = (
        jnp.arange(patch_count)[:, None] >= jnp.arange(patch_count)[None, :]
    ).astype(jnp.bfloat16)
    ranking = jnp.dot(lower, onehot, preferred_element_type=jnp.float32)
    slot_index = jnp.sum(ranking * onehot.astype(jnp.float32), axis=1).astype(jnp.int32) - 1
    target = regime * capacity + slot_index
    route = (target[None, :] == jnp.arange(slots, dtype=jnp.int32)[:, None]).astype(jnp.bfloat16)

    flat_feats = feats.reshape(patch_count, feat_width)
    field_rows = conv_block(cotangent, kernel, True)
    local = jnp.concatenate([flat_feats, field_rows], axis=1)
    outbound = jnp.dot(route, local, preferred_element_type=jnp.float32).astype(jnp.bfloat16)
    both = feat_width + channels
    inbound = lax.all_to_all(
        outbound.reshape(experts, capacity, both), "expert", split_axis=0, concat_axis=0, tiled=True
    ).reshape(slots, both)
    back, part = expert(inbound, w_first[0], w_second[0], 512)
    returned = lax.all_to_all(
        back.reshape(experts, capacity, both), "expert", split_axis=0, concat_axis=0, tiled=True
    )
    mixed = lax.dot_general(
        route,
        returned.reshape(slots, both),
        (((0,), (0,)), ((), ())),
        preferred_element_type=jnp.float32,
    ).astype(jnp.bfloat16)
    patch_grid = mixed[:, :channels].reshape(1, rows_y, depth_cells, channels)
    imitated = conv_block(patch_grid, kernel, False).reshape(1, rows_y, depth_cells, channels)
    feat_grad = mixed[:, channels:].reshape(1, rows_y, depth_cells, feat_width)

    grads = tree_scatter(part.reshape(slabs, hidden // slabs, both), (0, 1, 2, 3))
    grad_one = grads[:, :feat_width].T
    grad_two = grads[:, feat_width:]
    return (imitated, feat_grad, grad_one[None], grad_two[None])


def solution(mesh):
    in_specs = (
        P("dp", "expert", None, None),
        P("dp", "expert", None, None),
        P("expert", None, None),
        P("expert", None, None),
        P(),
        P("dp", "expert", None, None),
    )
    out_specs = (
        P("dp", "expert", None, None),
        P("dp", "expert", None, None),
        P("expert", None, "dp"),
        P("expert", "dp", None),
    )
    return jax.shard_map(
        per_device, mesh=mesh, in_specs=in_specs, out_specs=out_specs, check_vma=False
    )
```

```python
import functools

import jax
import jax.numpy as jnp
from jax import lax
from jax.experimental import pallas as pl
from jax.experimental.pallas import tpu as pltpu
from jax.sharding import PartitionSpec as P


def extended(x, sides, width):
    for axis, dim in sides:
        size, length = (lax.axis_size(axis), x.shape[dim])
        up = [(i, (i + 1) % size) for i in range(size - 1)]
        down = [(j, i) for i, j in up]
        last = lax.slice_in_dim(x, length - width, length, axis=dim)
        first = lax.slice_in_dim(x, 0, width, axis=dim)
        before = lax.ppermute(last, axis, up)
        after = lax.ppermute(first, axis, down)
        x = jnp.concatenate([before, x, after], axis=dim)
    return x


def gelu_act(value):
    return jax.nn.gelu(value, approximate=True)


def gelu_back(preact, upstream):
    return jax.vjp(gelu_act, preact)[1](upstream)[0]


def tree_scatter(blocks, order):
    count = blocks.shape[0]
    me = lax.axis_index("dp")
    bits = count.bit_length() - 1
    x = blocks.reshape((2,) * bits + blocks.shape[1:])
    remaining = list(range(bits - 1, -1, -1))
    for bit in order:
        axis = remaining.index(bit)
        mine = (me >> bit) & 1
        keep = lax.dynamic_index_in_dim(x, mine, axis=axis, keepdims=False)
        send = lax.dynamic_index_in_dim(x, 1 - mine, axis=axis, keepdims=False)
        pairs = [(i, i ^ (1 << bit)) for i in range(count)]
        got = lax.ppermute(send.astype(jnp.bfloat16), "dp", pairs)
        x = keep + got.astype(jnp.float32)
        remaining.pop(axis)
    return x


def conv_kernel(flip, shifted_ref, taps_ref, out_ref, acc_ref):
    rows_y = shifted_ref.shape[3] - 2
    depth_cells = shifted_ref.shape[4]
    width = shifted_ref.shape[5]
    acc_ref[...] = jnp.zeros_like(acc_ref)
    for plane in range(3):
        for across in range(3):
            for along in range(3):
                tap = 9 * plane + 3 * across + along
                piece = shifted_ref[0, along, plane, across : across + rows_y]
                piece = piece.reshape(rows_y * depth_cells, width)
                if flip:
                    acc_ref[...] += lax.dot_general(
                        piece,
                        taps_ref[26 - tap],
                        (((1,), (1,)), ((), ())),
                        preferred_element_type=jnp.float32,
                    )
                else:
                    acc_ref[...] += jnp.dot(
                        piece, taps_ref[tap], preferred_element_type=jnp.float32
                    )
    out_ref[...] = acc_ref[...].astype(out_ref.dtype)


def conv_block(grid, kernel, flip, after=None):
    padded = extended(grid, (("dp", 0), ("expert", 1)), 1)
    if after is not None:
        after, padded = lax.optimization_barrier((after, padded))
    padded = jnp.pad(padded, ((0, 0), (0, 0), (1, 1), (0, 0)))
    depth_cells = grid.shape[2]
    shifted = jnp.stack(
        [padded[:, :, along : along + depth_cells] for along in range(3)], axis=0
    )[None]
    count = grid.shape[1] * depth_cells
    width = kernel.shape[2]
    result = pl.pallas_call(
        functools.partial(conv_kernel, flip),
        out_shape=jax.ShapeDtypeStruct((count, width), jnp.bfloat16),
        in_specs=[pl.BlockSpec(memory_space=pltpu.VMEM)] * 2,
        out_specs=pl.BlockSpec(memory_space=pltpu.VMEM),
        scratch_shapes=[pltpu.VMEM((count, width), jnp.float32)],
        compiler_params=pltpu.CompilerParams(vmem_limit_bytes=48 * 1024 * 1024),
        cost_estimate=pl.CostEstimate(
            flops=2 * 27 * count * width * width,
            transcendentals=0,
            bytes_accessed=2 * (shifted.size + kernel.size + count * width),
        ),
    )(shifted, kernel)
    if after is not None:
        return result, after
    return result


def expert_kernel(
    cols, rows_ref, first_ref, second_ref, back_ref, part_ref, result_acc, input_acc
):
    step = pl.program_id(0)

    @pl.when(step == 0)
    def _():
        result_acc[...] = jnp.zeros_like(result_acc)
        input_acc[...] = jnp.zeros_like(input_acc)

    rows = rows_ref[:, :cols]
    grads = rows_ref[:, cols:]
    first = first_ref[...]
    second = second_ref[...]
    preact = jnp.dot(rows, first, preferred_element_type=jnp.float32)
    activation = gelu_act(preact).astype(jnp.bfloat16)
    result_acc[...] += jnp.dot(activation, second, preferred_element_type=jnp.float32)
    upstream = lax.dot_general(
        grads, second, (((1,), (1,)), ((), ())), preferred_element_type=jnp.float32
    )
    gate_grad = gelu_back(preact, upstream).astype(jnp.bfloat16)
    input_acc[...] += lax.dot_general(
        gate_grad, first, (((1,), (1,)), ((), ())), preferred_element_type=jnp.float32
    )
    part_ref[:, :cols] = lax.dot_general(
        gate_grad, rows, (((0,), (0,)), ((), ())), preferred_element_type=jnp.float32
    )
    part_ref[:, cols:] = lax.dot_general(
        activation, grads, (((0,), (0,)), ((), ())), preferred_element_type=jnp.float32
    )

    @pl.when(step == pl.num_programs(0) - 1)
    def _():
        width = result_acc.shape[1]
        back_ref[:, :width] = result_acc[...].astype(back_ref.dtype)
        back_ref[:, width:] = input_acc[...].astype(back_ref.dtype)


def expert(inbound, weight_one, weight_two, chunk):
    slots, both = inbound.shape
    cols, hidden = weight_one.shape
    channels = weight_two.shape[1]
    flops = 2 * slots * hidden * (3 * cols + 3 * channels)
    return pl.pallas_call(
        functools.partial(expert_kernel, cols),
        grid=(hidden // chunk,),
        in_specs=[
            pl.BlockSpec((slots, both), lambda h: (0, 0)),
            pl.BlockSpec((cols, chunk), lambda h: (0, h)),
            pl.BlockSpec((chunk, channels), lambda h: (h, 0)),
        ],
        out_specs=[
            pl.BlockSpec((slots, both), lambda h: (0, 0)),
            pl.BlockSpec((chunk, both), lambda h: (h, 0)),
        ],
        out_shape=[
            jax.ShapeDtypeStruct((slots, both), jnp.bfloat16),
            jax.ShapeDtypeStruct((hidden, both), jnp.float32),
        ],
        scratch_shapes=[
            pltpu.VMEM((slots, channels), jnp.float32),
            pltpu.VMEM((slots, cols), jnp.float32),
        ],
        compiler_params=pltpu.CompilerParams(
            dimension_semantics=("arbitrary",), vmem_limit_bytes=56 * 1024 * 1024
        ),
        cost_estimate=pl.CostEstimate(
            flops=flops,
            transcendentals=slots * hidden,
            bytes_accessed=2 * (2 * slots * both + hidden * (cols + channels)) + 4 * hidden * both,
        ),
    )(inbound, weight_one, weight_two)


def per_device(feats, labels, w_first, w_second, kernel, cotangent):
    experts = lax.axis_size("expert")
    slabs = lax.axis_size("dp")
    rows_y = feats.shape[1]
    depth_cells = feats.shape[2]
    feat_width = feats.shape[3]
    channels = kernel.shape[2]
    hidden = w_first.shape[2]
    patch_count = rows_y * depth_cells
    capacity = 2 * patch_count // experts
    slots = experts * capacity
    regime = labels.reshape(patch_count)
    onehot = (regime[:, None] == jnp.arange(experts, dtype=jnp.int32)[None, :]).astype(
        jnp.bfloat16
    )
    lower = (
        jnp.arange(patch_count)[:, None] >= jnp.arange(patch_count)[None, :]
    ).astype(jnp.bfloat16)
    ranking = jnp.dot(lower, onehot, preferred_element_type=jnp.float32)
    slot_index = jnp.sum(ranking * onehot.astype(jnp.float32), axis=1).astype(jnp.int32) - 1
    target = regime * capacity + slot_index
    route = (target[None, :] == jnp.arange(slots, dtype=jnp.int32)[:, None]).astype(jnp.bfloat16)

    flat_feats = feats.reshape(patch_count, feat_width)
    field_rows = conv_block(cotangent, kernel, True)
    local = jnp.concatenate([flat_feats, field_rows], axis=1)
    outbound = jnp.dot(route, local, preferred_element_type=jnp.float32).astype(jnp.bfloat16)
    both = feat_width + channels
    inbound = lax.all_to_all(
        outbound.reshape(experts, capacity, both), "expert", split_axis=0, concat_axis=0, tiled=True
    ).reshape(slots, both)
    back, part = expert(inbound, w_first[0], w_second[0], 1024)
    returned = lax.all_to_all(
        back.reshape(experts, capacity, both), "expert", split_axis=0, concat_axis=0, tiled=True
    )
    mixed = lax.dot_general(
        route,
        returned.reshape(slots, both),
        (((0,), (0,)), ((), ())),
        preferred_element_type=jnp.float32,
    ).astype(jnp.bfloat16)
    patch_grid = mixed[:, :channels].reshape(1, rows_y, depth_cells, channels)
    imitated = conv_block(patch_grid, kernel, False).reshape(1, rows_y, depth_cells, channels)
    feat_grad = mixed[:, channels:].reshape(1, rows_y, depth_cells, feat_width)

    grads = tree_scatter(part.reshape(slabs, hidden // slabs, both), (0, 1, 2, 3))
    grad_one = grads[:, :feat_width].T
    grad_two = grads[:, feat_width:]
    return (imitated, feat_grad, grad_one[None], grad_two[None])


def solution(mesh):
    in_specs = (
        P("dp", "expert", None, None),
        P("dp", "expert", None, None),
        P("expert", None, None),
        P("expert", None, None),
        P(),
        P("dp", "expert", None, None),
    )
    out_specs = (
        P("dp", "expert", None, None),
        P("dp", "expert", None, None),
        P("expert", None, "dp"),
        P("expert", "dp", None),
    )
    return jax.shard_map(
        per_device, mesh=mesh, in_specs=in_specs, out_specs=out_specs, check_vma=False
    )
```

```python
import functools

import jax
import jax.numpy as jnp
from jax import lax
from jax.experimental import pallas as pl
from jax.experimental.pallas import tpu as pltpu
from jax.sharding import PartitionSpec as P


def extended(x, sides, width):
    for axis, dim in sides:
        size, length = (lax.axis_size(axis), x.shape[dim])
        up = [(i, (i + 1) % size) for i in range(size - 1)]
        down = [(j, i) for i, j in up]
        last = lax.slice_in_dim(x, length - width, length, axis=dim)
        first = lax.slice_in_dim(x, 0, width, axis=dim)
        before = lax.ppermute(last, axis, up)
        after = lax.ppermute(first, axis, down)
        x = jnp.concatenate([before, x, after], axis=dim)
    return x


def gelu_act(value):
    return jax.nn.gelu(value, approximate=True)


def gelu_back(preact, upstream):
    return jax.vjp(gelu_act, preact)[1](upstream)[0]


def tree_scatter(blocks, order):
    count = blocks.shape[0]
    me = lax.axis_index("dp")
    bits = count.bit_length() - 1
    x = blocks.reshape((2,) * bits + blocks.shape[1:])
    remaining = list(range(bits - 1, -1, -1))
    for bit in order:
        axis = remaining.index(bit)
        mine = (me >> bit) & 1
        keep = lax.dynamic_index_in_dim(x, mine, axis=axis, keepdims=False).astype(jnp.float32)
        send = lax.dynamic_index_in_dim(x, 1 - mine, axis=axis, keepdims=False)
        pairs = [(i, i ^ (1 << bit)) for i in range(count)]
        got = lax.ppermute(send.astype(jnp.bfloat16), "dp", pairs)
        x = keep + got.astype(jnp.float32)
        remaining.pop(axis)
    return x


def conv_kernel(flip, shifted_ref, taps_ref, out_ref, acc_ref):
    rows_y = shifted_ref.shape[3] - 2
    depth_cells = shifted_ref.shape[4]
    width = shifted_ref.shape[5]
    acc_ref[...] = jnp.zeros_like(acc_ref)
    for plane in range(3):
        for across in range(3):
            for along in range(3):
                tap = 9 * plane + 3 * across + along
                piece = shifted_ref[0, along, plane, across : across + rows_y]
                piece = piece.reshape(rows_y * depth_cells, width)
                if flip:
                    acc_ref[...] += lax.dot_general(
                        piece,
                        taps_ref[26 - tap],
                        (((1,), (1,)), ((), ())),
                        preferred_element_type=jnp.float32,
                    )
                else:
                    acc_ref[...] += jnp.dot(
                        piece, taps_ref[tap], preferred_element_type=jnp.float32
                    )
    out_ref[...] = acc_ref[...].astype(out_ref.dtype)


def conv_block(grid, kernel, flip, after=None):
    padded = extended(grid, (("dp", 0), ("expert", 1)), 1)
    if after is not None:
        after, padded = lax.optimization_barrier((after, padded))
    padded = jnp.pad(padded, ((0, 0), (0, 0), (1, 1), (0, 0)))
    depth_cells = grid.shape[2]
    shifted = jnp.stack(
        [padded[:, :, along : along + depth_cells] for along in range(3)], axis=0
    )[None]
    count = grid.shape[1] * depth_cells
    width = kernel.shape[2]
    result = pl.pallas_call(
        functools.partial(conv_kernel, flip),
        out_shape=jax.ShapeDtypeStruct((count, width), jnp.bfloat16),
        in_specs=[pl.BlockSpec(memory_space=pltpu.VMEM)] * 2,
        out_specs=pl.BlockSpec(memory_space=pltpu.VMEM),
        scratch_shapes=[pltpu.VMEM((count, width), jnp.float32)],
        compiler_params=pltpu.CompilerParams(vmem_limit_bytes=48 * 1024 * 1024),
        cost_estimate=pl.CostEstimate(
            flops=2 * 27 * count * width * width,
            transcendentals=0,
            bytes_accessed=2 * (shifted.size + kernel.size + count * width),
        ),
    )(shifted, kernel)
    if after is not None:
        return result, after
    return result


def expert_kernel(
    cols, rows_ref, first_ref, second_ref, back_ref, part_ref, result_acc, input_acc
):
    step = pl.program_id(0)

    @pl.when(step == 0)
    def _():
        result_acc[...] = jnp.zeros_like(result_acc)
        input_acc[...] = jnp.zeros_like(input_acc)

    rows = rows_ref[:, :cols]
    grads = rows_ref[:, cols:]
    first = first_ref[...]
    second = second_ref[...]
    preact = jnp.dot(rows, first, preferred_element_type=jnp.float32)
    activation = gelu_act(preact).astype(jnp.bfloat16)
    result_acc[...] += jnp.dot(activation, second, preferred_element_type=jnp.float32)
    upstream = lax.dot_general(
        grads, second, (((1,), (1,)), ((), ())), preferred_element_type=jnp.float32
    )
    gate_grad = gelu_back(preact, upstream).astype(jnp.bfloat16)
    input_acc[...] += lax.dot_general(
        gate_grad, first, (((1,), (1,)), ((), ())), preferred_element_type=jnp.float32
    )
    part_ref[:, :cols] = lax.dot_general(
        gate_grad, rows, (((0,), (0,)), ((), ())), preferred_element_type=jnp.float32
    ).astype(part_ref.dtype)
    part_ref[:, cols:] = lax.dot_general(
        activation, grads, (((0,), (0,)), ((), ())), preferred_element_type=jnp.float32
    ).astype(part_ref.dtype)

    @pl.when(step == pl.num_programs(0) - 1)
    def _():
        width = result_acc.shape[1]
        back_ref[:, :width] = result_acc[...].astype(back_ref.dtype)
        back_ref[:, width:] = input_acc[...].astype(back_ref.dtype)


def expert(inbound, weight_one, weight_two, chunk):
    slots, both = inbound.shape
    cols, hidden = weight_one.shape
    channels = weight_two.shape[1]
    flops = 2 * slots * hidden * (3 * cols + 3 * channels)
    return pl.pallas_call(
        functools.partial(expert_kernel, cols),
        grid=(hidden // chunk,),
        in_specs=[
            pl.BlockSpec((slots, both), lambda h: (0, 0)),
            pl.BlockSpec((cols, chunk), lambda h: (0, h)),
            pl.BlockSpec((chunk, channels), lambda h: (h, 0)),
        ],
        out_specs=[
            pl.BlockSpec((slots, both), lambda h: (0, 0)),
            pl.BlockSpec((chunk, both), lambda h: (h, 0)),
        ],
        out_shape=[
            jax.ShapeDtypeStruct((slots, both), jnp.bfloat16),
            jax.ShapeDtypeStruct((hidden, both), jnp.bfloat16),
        ],
        scratch_shapes=[
            pltpu.VMEM((slots, channels), jnp.float32),
            pltpu.VMEM((slots, cols), jnp.float32),
        ],
        compiler_params=pltpu.CompilerParams(
            dimension_semantics=("arbitrary",), vmem_limit_bytes=56 * 1024 * 1024
        ),
        cost_estimate=pl.CostEstimate(
            flops=flops,
            transcendentals=slots * hidden,
            bytes_accessed=2 * (2 * slots * both + hidden * (cols + channels)) + 2 * hidden * both,
        ),
    )(inbound, weight_one, weight_two)


def per_device(feats, labels, w_first, w_second, kernel, cotangent):
    experts = lax.axis_size("expert")
    slabs = lax.axis_size("dp")
    rows_y = feats.shape[1]
    depth_cells = feats.shape[2]
    feat_width = feats.shape[3]
    channels = kernel.shape[2]
    hidden = w_first.shape[2]
    patch_count = rows_y * depth_cells
    capacity = 2 * patch_count // experts
    slots = experts * capacity
    regime = labels.reshape(patch_count)
    onehot = (regime[:, None] == jnp.arange(experts, dtype=jnp.int32)[None, :]).astype(
        jnp.bfloat16
    )
    lower = (
        jnp.arange(patch_count)[:, None] >= jnp.arange(patch_count)[None, :]
    ).astype(jnp.bfloat16)
    ranking = jnp.dot(lower, onehot, preferred_element_type=jnp.float32)
    slot_index = jnp.sum(ranking * onehot.astype(jnp.float32), axis=1).astype(jnp.int32) - 1
    target = regime * capacity + slot_index
    route = (target[None, :] == jnp.arange(slots, dtype=jnp.int32)[:, None]).astype(jnp.bfloat16)

    flat_feats = feats.reshape(patch_count, feat_width)
    field_rows = conv_block(cotangent, kernel, True)
    local = jnp.concatenate([flat_feats, field_rows], axis=1)
    outbound = jnp.dot(route, local, preferred_element_type=jnp.float32).astype(jnp.bfloat16)
    both = feat_width + channels
    inbound = lax.all_to_all(
        outbound.reshape(experts, capacity, both), "expert", split_axis=0, concat_axis=0, tiled=True
    ).reshape(slots, both)
    back, part = expert(inbound, w_first[0], w_second[0], 1024)
    returned = lax.all_to_all(
        back.reshape(experts, capacity, both), "expert", split_axis=0, concat_axis=0, tiled=True
    )
    mixed = lax.dot_general(
        route,
        returned.reshape(slots, both),
        (((0,), (0,)), ((), ())),
        preferred_element_type=jnp.float32,
    ).astype(jnp.bfloat16)
    patch_grid = mixed[:, :channels].reshape(1, rows_y, depth_cells, channels)
    imitated = conv_block(patch_grid, kernel, False).reshape(1, rows_y, depth_cells, channels)
    feat_grad = mixed[:, channels:].reshape(1, rows_y, depth_cells, feat_width)

    grads = tree_scatter(part.reshape(slabs, hidden // slabs, both), (0, 1, 2, 3))
    grad_one = grads[:, :feat_width].T
    grad_two = grads[:, feat_width:]
    return (imitated, feat_grad, grad_one[None], grad_two[None])


def solution(mesh):
    in_specs = (
        P("dp", "expert", None, None),
        P("dp", "expert", None, None),
        P("expert", None, None),
        P("expert", None, None),
        P(),
        P("dp", "expert", None, None),
    )
    out_specs = (
        P("dp", "expert", None, None),
        P("dp", "expert", None, None),
        P("expert", None, "dp"),
        P("expert", "dp", None),
    )
    return jax.shard_map(
        per_device, mesh=mesh, in_specs=in_specs, out_specs=out_specs, check_vma=False
    )
```

```python
import functools

import jax
import jax.numpy as jnp
from jax import lax
from jax.experimental import pallas as pl
from jax.experimental.pallas import tpu as pltpu
from jax.sharding import PartitionSpec as P


def extended(x, sides, width):
    for axis, dim in sides:
        size, length = (lax.axis_size(axis), x.shape[dim])
        up = [(i, (i + 1) % size) for i in range(size - 1)]
        down = [(j, i) for i, j in up]
        last = lax.slice_in_dim(x, length - width, length, axis=dim)
        first = lax.slice_in_dim(x, 0, width, axis=dim)
        before = lax.ppermute(last, axis, up)
        after = lax.ppermute(first, axis, down)
        x = jnp.concatenate([before, x, after], axis=dim)
    return x


def gelu_act(value):
    return jax.nn.gelu(value, approximate=True)


def gelu_back(preact, upstream):
    return jax.vjp(gelu_act, preact)[1](upstream)[0]


def tree_scatter(blocks, order):
    count = blocks.shape[0]
    me = lax.axis_index("dp")
    bits = count.bit_length() - 1
    x = blocks.reshape((2,) * bits + blocks.shape[1:])
    remaining = list(range(bits - 1, -1, -1))
    for bit in order:
        axis = remaining.index(bit)
        mine = (me >> bit) & 1
        keep = lax.dynamic_index_in_dim(x, mine, axis=axis, keepdims=False).astype(jnp.float32)
        send = lax.dynamic_index_in_dim(x, 1 - mine, axis=axis, keepdims=False)
        pairs = [(i, i ^ (1 << bit)) for i in range(count)]
        got = lax.ppermute(send.astype(jnp.bfloat16), "dp", pairs)
        x = keep + got.astype(jnp.float32)
        remaining.pop(axis)
    return x


def conv_kernel(flip, shifted_ref, taps_ref, out_ref, acc_ref):
    rows_y = shifted_ref.shape[3] - 2
    depth_cells = shifted_ref.shape[4]
    width = shifted_ref.shape[5]
    acc_ref[...] = jnp.zeros_like(acc_ref)
    for plane in range(3):
        for across in range(3):
            for along in range(3):
                tap = 9 * plane + 3 * across + along
                piece = shifted_ref[0, along, plane, across : across + rows_y]
                piece = piece.reshape(rows_y * depth_cells, width)
                if flip:
                    acc_ref[...] += lax.dot_general(
                        piece,
                        taps_ref[26 - tap],
                        (((1,), (1,)), ((), ())),
                        preferred_element_type=jnp.float32,
                    )
                else:
                    acc_ref[...] += jnp.dot(
                        piece, taps_ref[tap], preferred_element_type=jnp.float32
                    )
    out_ref[...] = acc_ref[...].astype(out_ref.dtype)


def conv_block(grid, kernel, flip, after=None):
    padded = extended(grid, (("dp", 0), ("expert", 1)), 1)
    if after is not None:
        after, padded = lax.optimization_barrier((after, padded))
    padded = jnp.pad(padded, ((0, 0), (0, 0), (1, 1), (0, 0)))
    depth_cells = grid.shape[2]
    shifted = jnp.stack(
        [padded[:, :, along : along + depth_cells] for along in range(3)], axis=0
    )[None]
    count = grid.shape[1] * depth_cells
    width = kernel.shape[2]
    result = pl.pallas_call(
        functools.partial(conv_kernel, flip),
        out_shape=jax.ShapeDtypeStruct((count, width), jnp.bfloat16),
        in_specs=[pl.BlockSpec(memory_space=pltpu.VMEM)] * 2,
        out_specs=pl.BlockSpec(memory_space=pltpu.VMEM),
        scratch_shapes=[pltpu.VMEM((count, width), jnp.float32)],
        compiler_params=pltpu.CompilerParams(vmem_limit_bytes=48 * 1024 * 1024),
        cost_estimate=pl.CostEstimate(
            flops=2 * 27 * count * width * width,
            transcendentals=0,
            bytes_accessed=2 * (shifted.size + kernel.size + count * width),
        ),
    )(shifted, kernel)
    if after is not None:
        return result, after
    return result


def expert_kernel(
    cols, rows_ref, first_ref, second_ref, back_ref, part_ref, result_acc, input_acc, across_ref
):
    step = pl.program_id(0)

    @pl.when(step == 0)
    def _():
        result_acc[...] = jnp.zeros_like(result_acc)
        input_acc[...] = jnp.zeros_like(input_acc)
        across_ref[...] = rows_ref[...].T

    rows = rows_ref[:, :cols]
    grads = rows_ref[:, cols:]
    first = first_ref[...]
    second = second_ref[...]
    preact = jnp.dot(rows, first, preferred_element_type=jnp.float32)
    activation = gelu_act(preact).astype(jnp.bfloat16)
    result_acc[...] += jnp.dot(activation, second, preferred_element_type=jnp.float32)
    upstream = lax.dot_general(
        grads, second, (((1,), (1,)), ((), ())), preferred_element_type=jnp.float32
    )
    gate_grad = gelu_back(preact, upstream).astype(jnp.bfloat16)
    input_acc[...] += lax.dot_general(
        gate_grad, first, (((1,), (1,)), ((), ())), preferred_element_type=jnp.float32
    )
    part_one = jnp.dot(across_ref[:cols, :], gate_grad, preferred_element_type=jnp.float32)
    part_two = jnp.dot(across_ref[cols:, :], activation, preferred_element_type=jnp.float32)
    lanes = part_ref.shape[2]
    for block in range(part_ref.shape[0]):
        window = slice(block * lanes, (block + 1) * lanes)
        part_ref[block, :cols, :] = part_one[:, window].astype(part_ref.dtype)
        part_ref[block, cols:, :] = part_two[:, window].astype(part_ref.dtype)

    @pl.when(step == pl.num_programs(0) - 1)
    def _():
        width = result_acc.shape[1]
        back_ref[:, :width] = result_acc[...].astype(back_ref.dtype)
        back_ref[:, width:] = input_acc[...].astype(back_ref.dtype)


def expert(inbound, weight_one, weight_two, chunk, blocks):
    slots, both = inbound.shape
    cols, hidden = weight_one.shape
    channels = weight_two.shape[1]
    lanes = hidden // blocks
    per_step = chunk // lanes
    flops = 2 * slots * hidden * (3 * cols + 3 * channels)
    return pl.pallas_call(
        functools.partial(expert_kernel, cols),
        grid=(hidden // chunk,),
        in_specs=[
            pl.BlockSpec((slots, both), lambda h: (0, 0)),
            pl.BlockSpec((cols, chunk), lambda h: (0, h)),
            pl.BlockSpec((chunk, channels), lambda h: (h, 0)),
        ],
        out_specs=[
            pl.BlockSpec((slots, both), lambda h: (0, 0)),
            pl.BlockSpec((per_step, both, lanes), lambda h: (h, 0, 0)),
        ],
        out_shape=[
            jax.ShapeDtypeStruct((slots, both), jnp.bfloat16),
            jax.ShapeDtypeStruct((blocks, both, lanes), jnp.bfloat16),
        ],
        scratch_shapes=[
            pltpu.VMEM((slots, channels), jnp.float32),
            pltpu.VMEM((slots, cols), jnp.float32),
            pltpu.VMEM((both, slots), jnp.bfloat16),
        ],
        compiler_params=pltpu.CompilerParams(
            dimension_semantics=("arbitrary",), vmem_limit_bytes=56 * 1024 * 1024
        ),
        cost_estimate=pl.CostEstimate(
            flops=flops,
            transcendentals=slots * hidden,
            bytes_accessed=2 * (2 * slots * both + hidden * (cols + channels)) + 2 * hidden * both,
        ),
    )(inbound, weight_one, weight_two)


def per_device(feats, labels, w_first, w_second, kernel, cotangent):
    experts = lax.axis_size("expert")
    slabs = lax.axis_size("dp")
    rows_y = feats.shape[1]
    depth_cells = feats.shape[2]
    feat_width = feats.shape[3]
    channels = kernel.shape[2]
    hidden = w_first.shape[2]
    patch_count = rows_y * depth_cells
    capacity = 2 * patch_count // experts
    slots = experts * capacity
    regime = labels.reshape(patch_count)
    onehot = (regime[:, None] == jnp.arange(experts, dtype=jnp.int32)[None, :]).astype(
        jnp.bfloat16
    )
    lower = (
        jnp.arange(patch_count)[:, None] >= jnp.arange(patch_count)[None, :]
    ).astype(jnp.bfloat16)
    ranking = jnp.dot(lower, onehot, preferred_element_type=jnp.float32)
    slot_index = jnp.sum(ranking * onehot.astype(jnp.float32), axis=1).astype(jnp.int32) - 1
    target = regime * capacity + slot_index
    route = (target[None, :] == jnp.arange(slots, dtype=jnp.int32)[:, None]).astype(jnp.bfloat16)

    flat_feats = feats.reshape(patch_count, feat_width)
    field_rows = conv_block(cotangent, kernel, True)
    local = jnp.concatenate([flat_feats, field_rows], axis=1)
    outbound = jnp.dot(route, local, preferred_element_type=jnp.float32).astype(jnp.bfloat16)
    both = feat_width + channels
    inbound = lax.all_to_all(
        outbound.reshape(experts, capacity, both), "expert", split_axis=0, concat_axis=0, tiled=True
    ).reshape(slots, both)
    back, part = expert(inbound, w_first[0], w_second[0], 1024, slabs)
    returned = lax.all_to_all(
        back.reshape(experts, capacity, both), "expert", split_axis=0, concat_axis=0, tiled=True
    )
    mixed = lax.dot_general(
        route,
        returned.reshape(slots, both),
        (((0,), (0,)), ((), ())),
        preferred_element_type=jnp.float32,
    ).astype(jnp.bfloat16)
    patch_grid = mixed[:, :channels].reshape(1, rows_y, depth_cells, channels)
    imitated = conv_block(patch_grid, kernel, False).reshape(1, rows_y, depth_cells, channels)
    feat_grad = mixed[:, channels:].reshape(1, rows_y, depth_cells, feat_width)

    grads = tree_scatter(part, (0, 1, 2, 3))
    grad_one = grads[:feat_width]
    grad_two = grads[feat_width:].T
    return (imitated, feat_grad, grad_one[None], grad_two[None])


def solution(mesh):
    in_specs = (
        P("dp", "expert", None, None),
        P("dp", "expert", None, None),
        P("expert", None, None),
        P("expert", None, None),
        P(),
        P("dp", "expert", None, None),
    )
    out_specs = (
        P("dp", "expert", None, None),
        P("dp", "expert", None, None),
        P("expert", None, "dp"),
        P("expert", "dp", None),
    )
    return jax.shard_map(
        per_device, mesh=mesh, in_specs=in_specs, out_specs=out_specs, check_vma=False
    )
```

```python
import functools

import jax
import jax.numpy as jnp
from jax import lax
from jax.experimental import pallas as pl
from jax.experimental.pallas import tpu as pltpu
from jax.sharding import PartitionSpec as P


def extended(x, sides, width):
    for axis, dim in sides:
        size, length = (lax.axis_size(axis), x.shape[dim])
        up = [(i, (i + 1) % size) for i in range(size - 1)]
        down = [(j, i) for i, j in up]
        last = lax.slice_in_dim(x, length - width, length, axis=dim)
        first = lax.slice_in_dim(x, 0, width, axis=dim)
        before = lax.ppermute(last, axis, up)
        after = lax.ppermute(first, axis, down)
        x = jnp.concatenate([before, x, after], axis=dim)
    return x


def gelu_act(value):
    return jax.nn.gelu(value, approximate=True)


def gelu_back(preact, upstream):
    return jax.vjp(gelu_act, preact)[1](upstream)[0]


def tree_scatter(blocks, order):
    count = blocks.shape[0]
    me = lax.axis_index("dp")
    bits = count.bit_length() - 1
    x = blocks.reshape((2,) * bits + blocks.shape[1:])
    remaining = list(range(bits))
    for bit in order:
        axis = remaining.index(bit)
        mine = (me >> bit) & 1
        keep = lax.dynamic_index_in_dim(x, mine, axis=axis, keepdims=False).astype(jnp.float32)
        send = lax.dynamic_index_in_dim(x, 1 - mine, axis=axis, keepdims=False)
        pairs = [(i, i ^ (1 << bit)) for i in range(count)]
        got = lax.ppermute(send.astype(jnp.bfloat16), "dp", pairs)
        x = keep + got.astype(jnp.float32)
        remaining.pop(axis)
    return x


def conv_kernel(flip, shifted_ref, taps_ref, out_ref, acc_ref):
    rows_y = shifted_ref.shape[3] - 2
    depth_cells = shifted_ref.shape[4]
    width = shifted_ref.shape[5]
    acc_ref[...] = jnp.zeros_like(acc_ref)
    for plane in range(3):
        for across in range(3):
            for along in range(3):
                tap = 9 * plane + 3 * across + along
                piece = shifted_ref[0, along, plane, across : across + rows_y]
                piece = piece.reshape(rows_y * depth_cells, width)
                if flip:
                    acc_ref[...] += lax.dot_general(
                        piece,
                        taps_ref[26 - tap],
                        (((1,), (1,)), ((), ())),
                        preferred_element_type=jnp.float32,
                    )
                else:
                    acc_ref[...] += jnp.dot(
                        piece, taps_ref[tap], preferred_element_type=jnp.float32
                    )
    out_ref[...] = acc_ref[...].astype(out_ref.dtype)


def conv_block(grid, kernel, flip, after=None):
    padded = extended(grid, (("dp", 0), ("expert", 1)), 1)
    if after is not None:
        after, padded = lax.optimization_barrier((after, padded))
    padded = jnp.pad(padded, ((0, 0), (0, 0), (1, 1), (0, 0)))
    depth_cells = grid.shape[2]
    shifted = jnp.stack(
        [padded[:, :, along : along + depth_cells] for along in range(3)], axis=0
    )[None]
    count = grid.shape[1] * depth_cells
    width = kernel.shape[2]
    result = pl.pallas_call(
        functools.partial(conv_kernel, flip),
        out_shape=jax.ShapeDtypeStruct((count, width), jnp.bfloat16),
        in_specs=[pl.BlockSpec(memory_space=pltpu.VMEM)] * 2,
        out_specs=pl.BlockSpec(memory_space=pltpu.VMEM),
        scratch_shapes=[pltpu.VMEM((count, width), jnp.float32)],
        compiler_params=pltpu.CompilerParams(vmem_limit_bytes=48 * 1024 * 1024),
        cost_estimate=pl.CostEstimate(
            flops=2 * 27 * count * width * width,
            transcendentals=0,
            bytes_accessed=2 * (shifted.size + kernel.size + count * width),
        ),
    )(shifted, kernel)
    if after is not None:
        return result, after
    return result


def expert_kernel(
    cols, rows_ref, first_ref, second_ref, back_ref, part_ref, result_acc, input_acc, across_ref
):
    step = pl.program_id(0)

    @pl.when(step == 0)
    def _():
        result_acc[...] = jnp.zeros_like(result_acc)
        input_acc[...] = jnp.zeros_like(input_acc)
        across_ref[...] = rows_ref[...].T

    rows = rows_ref[:, :cols]
    grads = rows_ref[:, cols:]
    first = first_ref[...]
    second = second_ref[...]
    preact = jnp.dot(rows, first, preferred_element_type=jnp.float32)
    activation = gelu_act(preact).astype(jnp.bfloat16)
    result_acc[...] += jnp.dot(activation, second, preferred_element_type=jnp.float32)
    upstream = lax.dot_general(
        grads, second, (((1,), (1,)), ((), ())), preferred_element_type=jnp.float32
    )
    gate_grad = gelu_back(preact, upstream).astype(jnp.bfloat16)
    input_acc[...] += lax.dot_general(
        gate_grad, first, (((1,), (1,)), ((), ())), preferred_element_type=jnp.float32
    )
    part_one = jnp.dot(across_ref[:cols, :], gate_grad, preferred_element_type=jnp.float32)
    part_two = jnp.dot(across_ref[cols:, :], activation, preferred_element_type=jnp.float32)
    lanes = part_ref.shape[2]
    bits = part_ref.shape[0].bit_length() - 1
    per_step = part_one.shape[1] // lanes
    for block in range(per_step):
        window = slice(block * lanes, (block + 1) * lanes)
        owner = step * per_step + block
        place = sum(((owner >> bit) & 1) << (bits - 1 - bit) for bit in range(bits))
        part_ref[place, :cols, :] = part_one[:, window].astype(part_ref.dtype)
        part_ref[place, cols:, :] = part_two[:, window].astype(part_ref.dtype)

    @pl.when(step == pl.num_programs(0) - 1)
    def _():
        width = result_acc.shape[1]
        back_ref[:, :width] = result_acc[...].astype(back_ref.dtype)
        back_ref[:, width:] = input_acc[...].astype(back_ref.dtype)


def expert(inbound, weight_one, weight_two, chunk, blocks):
    slots, both = inbound.shape
    cols, hidden = weight_one.shape
    channels = weight_two.shape[1]
    lanes = hidden // blocks
    flops = 2 * slots * hidden * (3 * cols + 3 * channels)
    return pl.pallas_call(
        functools.partial(expert_kernel, cols),
        grid=(hidden // chunk,),
        in_specs=[
            pl.BlockSpec((slots, both), lambda h: (0, 0)),
            pl.BlockSpec((cols, chunk), lambda h: (0, h)),
            pl.BlockSpec((chunk, channels), lambda h: (h, 0)),
        ],
        out_specs=[
            pl.BlockSpec((slots, both), lambda h: (0, 0)),
            pl.BlockSpec((blocks, both, lanes), lambda h: (0, 0, 0)),
        ],
        out_shape=[
            jax.ShapeDtypeStruct((slots, both), jnp.bfloat16),
            jax.ShapeDtypeStruct((blocks, both, lanes), jnp.bfloat16),
        ],
        scratch_shapes=[
            pltpu.VMEM((slots, channels), jnp.float32),
            pltpu.VMEM((slots, cols), jnp.float32),
            pltpu.VMEM((both, slots), jnp.bfloat16),
        ],
        compiler_params=pltpu.CompilerParams(
            dimension_semantics=("arbitrary",), vmem_limit_bytes=56 * 1024 * 1024
        ),
        cost_estimate=pl.CostEstimate(
            flops=flops,
            transcendentals=slots * hidden,
            bytes_accessed=2 * (2 * slots * both + hidden * (cols + channels)) + 2 * hidden * both,
        ),
    )(inbound, weight_one, weight_two)


def per_device(feats, labels, w_first, w_second, kernel, cotangent):
    experts = lax.axis_size("expert")
    slabs = lax.axis_size("dp")
    rows_y = feats.shape[1]
    depth_cells = feats.shape[2]
    feat_width = feats.shape[3]
    channels = kernel.shape[2]
    hidden = w_first.shape[2]
    patch_count = rows_y * depth_cells
    capacity = 2 * patch_count // experts
    slots = experts * capacity
    regime = labels.reshape(patch_count)
    onehot = (regime[:, None] == jnp.arange(experts, dtype=jnp.int32)[None, :]).astype(
        jnp.bfloat16
    )
    lower = (
        jnp.arange(patch_count)[:, None] >= jnp.arange(patch_count)[None, :]
    ).astype(jnp.bfloat16)
    ranking = jnp.dot(lower, onehot, preferred_element_type=jnp.float32)
    slot_index = jnp.sum(ranking * onehot.astype(jnp.float32), axis=1).astype(jnp.int32) - 1
    target = regime * capacity + slot_index
    route = (target[None, :] == jnp.arange(slots, dtype=jnp.int32)[:, None]).astype(jnp.bfloat16)

    flat_feats = feats.reshape(patch_count, feat_width)
    field_rows = conv_block(cotangent, kernel, True)
    local = jnp.concatenate([flat_feats, field_rows], axis=1)
    outbound = jnp.dot(route, local, preferred_element_type=jnp.float32).astype(jnp.bfloat16)
    both = feat_width + channels
    inbound = lax.all_to_all(
        outbound.reshape(experts, capacity, both), "expert", split_axis=0, concat_axis=0, tiled=True
    ).reshape(slots, both)
    back, part = expert(inbound, w_first[0], w_second[0], 1024, slabs)
    returned = lax.all_to_all(
        back.reshape(experts, capacity, both), "expert", split_axis=0, concat_axis=0, tiled=True
    )
    mixed = lax.dot_general(
        route,
        returned.reshape(slots, both),
        (((0,), (0,)), ((), ())),
        preferred_element_type=jnp.float32,
    ).astype(jnp.bfloat16)
    patch_grid = mixed[:, :channels].reshape(1, rows_y, depth_cells, channels)
    imitated = conv_block(patch_grid, kernel, False).reshape(1, rows_y, depth_cells, channels)
    feat_grad = mixed[:, channels:].reshape(1, rows_y, depth_cells, feat_width)

    grads = tree_scatter(part, (0, 1, 2, 3))
    grad_one = grads[:feat_width]
    grad_two = grads[feat_width:].T
    return (imitated, feat_grad, grad_one[None], grad_two[None])


def solution(mesh):
    in_specs = (
        P("dp", "expert", None, None),
        P("dp", "expert", None, None),
        P("expert", None, None),
        P("expert", None, None),
        P(),
        P("dp", "expert", None, None),
    )
    out_specs = (
        P("dp", "expert", None, None),
        P("dp", "expert", None, None),
        P("expert", None, "dp"),
        P("expert", "dp", None),
    )
    return jax.shard_map(
        per_device, mesh=mesh, in_specs=in_specs, out_specs=out_specs, check_vma=False
    )
```

```python
import functools

import jax
import jax.numpy as jnp
from jax import lax
from jax.experimental import pallas as pl
from jax.experimental.pallas import tpu as pltpu
from jax.sharding import PartitionSpec as P


def extended(x, sides, width):
    for axis, dim in sides:
        size, length = (lax.axis_size(axis), x.shape[dim])
        up = [(i, (i + 1) % size) for i in range(size - 1)]
        down = [(j, i) for i, j in up]
        last = lax.slice_in_dim(x, length - width, length, axis=dim)
        first = lax.slice_in_dim(x, 0, width, axis=dim)
        before = lax.ppermute(last, axis, up)
        after = lax.ppermute(first, axis, down)
        x = jnp.concatenate([before, x, after], axis=dim)
    return x


def gelu_act(value):
    return jax.nn.gelu(value, approximate=True)


def gelu_back(preact, upstream):
    return jax.vjp(gelu_act, preact)[1](upstream)[0]


def tree_scatter(blocks, order):
    count = blocks.shape[0]
    me = lax.axis_index("dp")
    bits = count.bit_length() - 1
    x = blocks.reshape((2,) * bits + blocks.shape[1:])
    remaining = list(range(bits))
    for bit in order:
        axis = remaining.index(bit)
        mine = (me >> bit) & 1
        keep = lax.dynamic_index_in_dim(x, mine, axis=axis, keepdims=False).astype(jnp.float32)
        send = lax.dynamic_index_in_dim(x, 1 - mine, axis=axis, keepdims=False)
        pairs = [(i, i ^ (1 << bit)) for i in range(count)]
        got = lax.ppermute(send.astype(jnp.bfloat16), "dp", pairs)
        x = keep + got.astype(jnp.float32)
        remaining.pop(axis)
    return x


def conv_kernel(flip, shifted_ref, taps_ref, out_ref, acc_ref):
    rows_y = shifted_ref.shape[3] - 2
    depth_cells = shifted_ref.shape[4]
    width = shifted_ref.shape[5]
    acc_ref[...] = jnp.zeros_like(acc_ref)
    for plane in range(3):
        for across in range(3):
            for along in range(3):
                tap = 9 * plane + 3 * across + along
                piece = shifted_ref[0, along, plane, across : across + rows_y]
                piece = piece.reshape(rows_y * depth_cells, width)
                if flip:
                    acc_ref[...] += lax.dot_general(
                        piece,
                        taps_ref[26 - tap],
                        (((1,), (1,)), ((), ())),
                        preferred_element_type=jnp.float32,
                    )
                else:
                    acc_ref[...] += jnp.dot(
                        piece, taps_ref[tap], preferred_element_type=jnp.float32
                    )
    out_ref[...] = acc_ref[...].astype(out_ref.dtype)


def conv_block(grid, kernel, flip, after=None):
    padded = extended(grid, (("expert", 1), ("dp", 0)), 1)
    if after is not None:
        after, padded = lax.optimization_barrier((after, padded))
    padded = jnp.pad(padded, ((0, 0), (0, 0), (1, 1), (0, 0)))
    depth_cells = grid.shape[2]
    shifted = jnp.stack(
        [padded[:, :, along : along + depth_cells] for along in range(3)], axis=0
    )[None]
    count = grid.shape[1] * depth_cells
    width = kernel.shape[2]
    result = pl.pallas_call(
        functools.partial(conv_kernel, flip),
        out_shape=jax.ShapeDtypeStruct((count, width), jnp.bfloat16),
        in_specs=[pl.BlockSpec(memory_space=pltpu.VMEM)] * 2,
        out_specs=pl.BlockSpec(memory_space=pltpu.VMEM),
        scratch_shapes=[pltpu.VMEM((count, width), jnp.float32)],
        compiler_params=pltpu.CompilerParams(vmem_limit_bytes=48 * 1024 * 1024),
        cost_estimate=pl.CostEstimate(
            flops=2 * 27 * count * width * width,
            transcendentals=0,
            bytes_accessed=2 * (shifted.size + kernel.size + count * width),
        ),
    )(shifted, kernel)
    if after is not None:
        return result, after
    return result


def expert_kernel(
    cols, rows_ref, first_ref, second_ref, back_ref, part_ref, result_acc, input_acc, across_ref
):
    step = pl.program_id(0)

    @pl.when(step == 0)
    def _():
        result_acc[...] = jnp.zeros_like(result_acc)
        input_acc[...] = jnp.zeros_like(input_acc)
        across_ref[...] = rows_ref[...].T

    rows = rows_ref[:, :cols]
    grads = rows_ref[:, cols:]
    first = first_ref[...]
    second = second_ref[...]
    preact = jnp.dot(rows, first, preferred_element_type=jnp.float32)
    activation = gelu_act(preact).astype(jnp.bfloat16)
    result_acc[...] += jnp.dot(activation, second, preferred_element_type=jnp.float32)
    upstream = lax.dot_general(
        grads, second, (((1,), (1,)), ((), ())), preferred_element_type=jnp.float32
    )
    gate_grad = gelu_back(preact, upstream).astype(jnp.bfloat16)
    input_acc[...] += lax.dot_general(
        gate_grad, first, (((1,), (1,)), ((), ())), preferred_element_type=jnp.float32
    )
    part_one = jnp.dot(across_ref[:cols, :], gate_grad, preferred_element_type=jnp.float32)
    part_two = jnp.dot(across_ref[cols:, :], activation, preferred_element_type=jnp.float32)
    lanes = part_ref.shape[2]
    bits = part_ref.shape[0].bit_length() - 1
    per_step = part_one.shape[1] // lanes
    for block in range(per_step):
        window = slice(block * lanes, (block + 1) * lanes)
        owner = step * per_step + block
        place = sum(((owner >> bit) & 1) << (bits - 1 - bit) for bit in range(bits))
        part_ref[place, :cols, :] = part_one[:, window].astype(part_ref.dtype)
        part_ref[place, cols:, :] = part_two[:, window].astype(part_ref.dtype)

    @pl.when(step == pl.num_programs(0) - 1)
    def _():
        width = result_acc.shape[1]
        back_ref[:, :width] = result_acc[...].astype(back_ref.dtype)
        back_ref[:, width:] = input_acc[...].astype(back_ref.dtype)


def expert(inbound, weight_one, weight_two, chunk, blocks):
    slots, both = inbound.shape
    cols, hidden = weight_one.shape
    channels = weight_two.shape[1]
    lanes = hidden // blocks
    flops = 2 * slots * hidden * (3 * cols + 3 * channels)
    return pl.pallas_call(
        functools.partial(expert_kernel, cols),
        grid=(hidden // chunk,),
        in_specs=[
            pl.BlockSpec((slots, both), lambda h: (0, 0)),
            pl.BlockSpec((cols, chunk), lambda h: (0, h)),
            pl.BlockSpec((chunk, channels), lambda h: (h, 0)),
        ],
        out_specs=[
            pl.BlockSpec((slots, both), lambda h: (0, 0)),
            pl.BlockSpec((blocks, both, lanes), lambda h: (0, 0, 0)),
        ],
        out_shape=[
            jax.ShapeDtypeStruct((slots, both), jnp.bfloat16),
            jax.ShapeDtypeStruct((blocks, both, lanes), jnp.bfloat16),
        ],
        scratch_shapes=[
            pltpu.VMEM((slots, channels), jnp.float32),
            pltpu.VMEM((slots, cols), jnp.float32),
            pltpu.VMEM((both, slots), jnp.bfloat16),
        ],
        compiler_params=pltpu.CompilerParams(
            dimension_semantics=("arbitrary",), vmem_limit_bytes=56 * 1024 * 1024
        ),
        cost_estimate=pl.CostEstimate(
            flops=flops,
            transcendentals=slots * hidden,
            bytes_accessed=2 * (2 * slots * both + hidden * (cols + channels)) + 2 * hidden * both,
        ),
    )(inbound, weight_one, weight_two)


def per_device(feats, labels, w_first, w_second, kernel, cotangent):
    experts = lax.axis_size("expert")
    slabs = lax.axis_size("dp")
    rows_y = feats.shape[1]
    depth_cells = feats.shape[2]
    feat_width = feats.shape[3]
    channels = kernel.shape[2]
    hidden = w_first.shape[2]
    patch_count = rows_y * depth_cells
    capacity = 2 * patch_count // experts
    slots = experts * capacity
    regime = labels.reshape(patch_count)
    onehot = (regime[:, None] == jnp.arange(experts, dtype=jnp.int32)[None, :]).astype(
        jnp.bfloat16
    )
    lower = (
        jnp.arange(patch_count)[:, None] >= jnp.arange(patch_count)[None, :]
    ).astype(jnp.bfloat16)
    ranking = jnp.dot(lower, onehot, preferred_element_type=jnp.float32)
    slot_index = jnp.sum(ranking * onehot.astype(jnp.float32), axis=1).astype(jnp.int32) - 1
    target = regime * capacity + slot_index
    route = (target[None, :] == jnp.arange(slots, dtype=jnp.int32)[:, None]).astype(jnp.bfloat16)

    flat_feats = feats.reshape(patch_count, feat_width)
    field_rows = conv_block(cotangent, kernel, True)
    local = jnp.concatenate([flat_feats, field_rows], axis=1)
    outbound = jnp.dot(route, local, preferred_element_type=jnp.float32).astype(jnp.bfloat16)
    both = feat_width + channels
    inbound = lax.all_to_all(
        outbound.reshape(experts, capacity, both), "expert", split_axis=0, concat_axis=0, tiled=True
    ).reshape(slots, both)
    back, part = expert(inbound, w_first[0], w_second[0], 1024, slabs)
    returned = lax.all_to_all(
        back.reshape(experts, capacity, both), "expert", split_axis=0, concat_axis=0, tiled=True
    )
    mixed = lax.dot_general(
        route,
        returned.reshape(slots, both),
        (((0,), (0,)), ((), ())),
        preferred_element_type=jnp.float32,
    ).astype(jnp.bfloat16)
    patch_grid = mixed[:, :channels].reshape(1, rows_y, depth_cells, channels)
    imitated = conv_block(patch_grid, kernel, False).reshape(1, rows_y, depth_cells, channels)
    feat_grad = mixed[:, channels:].reshape(1, rows_y, depth_cells, feat_width)

    grads = tree_scatter(part, (0, 1, 2, 3))
    grad_one = grads[:feat_width]
    grad_two = grads[feat_width:].T
    return (imitated, feat_grad, grad_one[None], grad_two[None])


def solution(mesh):
    in_specs = (
        P("dp", "expert", None, None),
        P("dp", "expert", None, None),
        P("expert", None, None),
        P("expert", None, None),
        P(),
        P("dp", "expert", None, None),
    )
    out_specs = (
        P("dp", "expert", None, None),
        P("dp", "expert", None, None),
        P("expert", None, "dp"),
        P("expert", "dp", None),
    )
    return jax.shard_map(
        per_device, mesh=mesh, in_specs=in_specs, out_specs=out_specs, check_vma=False
    )
```

```python
import functools

import jax
import jax.numpy as jnp
from jax import lax
from jax.experimental import pallas as pl
from jax.experimental.pallas import tpu as pltpu
from jax.sharding import PartitionSpec as P


def extended(x, sides, width):
    for axis, dim in sides:
        size, length = (lax.axis_size(axis), x.shape[dim])
        up = [(i, (i + 1) % size) for i in range(size - 1)]
        down = [(j, i) for i, j in up]
        last = lax.slice_in_dim(x, length - width, length, axis=dim)
        first = lax.slice_in_dim(x, 0, width, axis=dim)
        before = lax.ppermute(last, axis, up)
        after = lax.ppermute(first, axis, down)
        x = jnp.concatenate([before, x, after], axis=dim)
    return x


def gelu_act(value):
    return jax.nn.gelu(value, approximate=True)


def gelu_back(preact, upstream):
    return jax.vjp(gelu_act, preact)[1](upstream)[0]


def tree_scatter(blocks, order):
    count = blocks.shape[0]
    me = lax.axis_index("dp")
    bits = count.bit_length() - 1
    x = blocks.reshape((2,) * bits + blocks.shape[1:])
    remaining = list(range(bits))
    for bit in order:
        axis = remaining.index(bit)
        mine = (me >> bit) & 1
        keep = lax.dynamic_index_in_dim(x, mine, axis=axis, keepdims=False).astype(jnp.float32)
        send = lax.dynamic_index_in_dim(x, 1 - mine, axis=axis, keepdims=False)
        pairs = [(i, i ^ (1 << bit)) for i in range(count)]
        got = lax.ppermute(send.astype(jnp.bfloat16), "dp", pairs)
        x = keep + got.astype(jnp.float32)
        remaining.pop(axis)
    return x


def conv_kernel(flip, shifted_ref, taps_ref, out_ref, acc_ref):
    rows_y = shifted_ref.shape[3] - 2
    depth_cells = shifted_ref.shape[4]
    width = shifted_ref.shape[5]
    acc_ref[...] = jnp.zeros_like(acc_ref)
    for plane in range(3):
        for across in range(3):
            for along in range(3):
                tap = 9 * plane + 3 * across + along
                piece = shifted_ref[0, along, plane, across : across + rows_y]
                piece = piece.reshape(rows_y * depth_cells, width)
                if flip:
                    acc_ref[...] += lax.dot_general(
                        piece,
                        taps_ref[26 - tap],
                        (((1,), (1,)), ((), ())),
                        preferred_element_type=jnp.float32,
                    )
                else:
                    acc_ref[...] += jnp.dot(
                        piece, taps_ref[tap], preferred_element_type=jnp.float32
                    )
    out_ref[...] = acc_ref[...].astype(out_ref.dtype)


def conv_block(grid, kernel, flip, after=None):
    padded = extended(grid, (("expert", 1), ("dp", 0)), 1)
    if after is not None:
        after, padded = lax.optimization_barrier((after, padded))
    padded = jnp.pad(padded, ((0, 0), (0, 0), (1, 1), (0, 0)))
    depth_cells = grid.shape[2]
    shifted = jnp.stack(
        [padded[:, :, along : along + depth_cells] for along in range(3)], axis=0
    )[None]
    count = grid.shape[1] * depth_cells
    width = kernel.shape[2]
    result = pl.pallas_call(
        functools.partial(conv_kernel, flip),
        out_shape=jax.ShapeDtypeStruct((count, width), jnp.bfloat16),
        in_specs=[pl.BlockSpec(memory_space=pltpu.VMEM)] * 2,
        out_specs=pl.BlockSpec(memory_space=pltpu.VMEM),
        scratch_shapes=[pltpu.VMEM((count, width), jnp.float32)],
        compiler_params=pltpu.CompilerParams(vmem_limit_bytes=48 * 1024 * 1024),
        cost_estimate=pl.CostEstimate(
            flops=2 * 27 * count * width * width,
            transcendentals=0,
            bytes_accessed=2 * (shifted.size + kernel.size + count * width),
        ),
    )(shifted, kernel)
    if after is not None:
        return result, after
    return result


def expert_kernel(
    cols, rows_ref, first_ref, second_ref, back_ref, part_ref, result_acc, input_acc, across_ref
):
    step = pl.program_id(0)

    @pl.when(step == 0)
    def _():
        result_acc[...] = jnp.zeros_like(result_acc)
        input_acc[...] = jnp.zeros_like(input_acc)
        across_ref[...] = rows_ref[...].T

    rows = rows_ref[:, :cols]
    grads = rows_ref[:, cols:]
    first = first_ref[...]
    second = second_ref[...]
    preact = jnp.dot(rows, first, preferred_element_type=jnp.float32)
    activation = gelu_act(preact).astype(jnp.bfloat16)
    result_acc[...] += jnp.dot(activation, second, preferred_element_type=jnp.float32)
    upstream = lax.dot_general(
        grads, second, (((1,), (1,)), ((), ())), preferred_element_type=jnp.float32
    )
    gate_grad = gelu_back(preact, upstream).astype(jnp.bfloat16)
    input_acc[...] += lax.dot_general(
        gate_grad, first, (((1,), (1,)), ((), ())), preferred_element_type=jnp.float32
    )
    part_one = jnp.dot(across_ref[:cols, :], gate_grad, preferred_element_type=jnp.float32)
    part_two = jnp.dot(across_ref[cols:, :], activation, preferred_element_type=jnp.float32)
    lanes = part_ref.shape[2]
    bits = part_ref.shape[0].bit_length() - 1
    per_step = part_one.shape[1] // lanes
    for block in range(per_step):
        window = slice(block * lanes, (block + 1) * lanes)
        owner = step * per_step + block
        place = sum(((owner >> bit) & 1) << (bits - 1 - bit) for bit in range(bits))
        part_ref[place, :cols, :] = part_one[:, window].astype(part_ref.dtype)
        part_ref[place, cols:, :] = part_two[:, window].astype(part_ref.dtype)

    @pl.when(step == pl.num_programs(0) - 1)
    def _():
        width = result_acc.shape[1]
        back_ref[:, :width] = result_acc[...].astype(back_ref.dtype)
        back_ref[:, width:] = input_acc[...].astype(back_ref.dtype)


def expert(inbound, weight_one, weight_two, chunk, blocks):
    slots, both = inbound.shape
    cols, hidden = weight_one.shape
    channels = weight_two.shape[1]
    lanes = hidden // blocks
    flops = 2 * slots * hidden * (3 * cols + 3 * channels)
    return pl.pallas_call(
        functools.partial(expert_kernel, cols),
        grid=(hidden // chunk,),
        in_specs=[
            pl.BlockSpec((slots, both), lambda h: (0, 0)),
            pl.BlockSpec((cols, chunk), lambda h: (0, h)),
            pl.BlockSpec((chunk, channels), lambda h: (h, 0)),
        ],
        out_specs=[
            pl.BlockSpec((slots, both), lambda h: (0, 0)),
            pl.BlockSpec((blocks, both, lanes), lambda h: (0, 0, 0)),
        ],
        out_shape=[
            jax.ShapeDtypeStruct((slots, both), jnp.bfloat16),
            jax.ShapeDtypeStruct((blocks, both, lanes), jnp.bfloat16),
        ],
        scratch_shapes=[
            pltpu.VMEM((slots, channels), jnp.float32),
            pltpu.VMEM((slots, cols), jnp.float32),
            pltpu.VMEM((both, slots), jnp.bfloat16),
        ],
        compiler_params=pltpu.CompilerParams(
            dimension_semantics=("arbitrary",), vmem_limit_bytes=56 * 1024 * 1024
        ),
        cost_estimate=pl.CostEstimate(
            flops=flops,
            transcendentals=slots * hidden,
            bytes_accessed=2 * (2 * slots * both + hidden * (cols + channels)) + 2 * hidden * both,
        ),
    )(inbound, weight_one, weight_two)


def per_device(feats, labels, w_first, w_second, kernel, cotangent):
    experts = lax.axis_size("expert")
    slabs = lax.axis_size("dp")
    rows_y = feats.shape[1]
    depth_cells = feats.shape[2]
    feat_width = feats.shape[3]
    channels = kernel.shape[2]
    hidden = w_first.shape[2]
    patch_count = rows_y * depth_cells
    capacity = 2 * patch_count // experts
    slots = experts * capacity
    regime = labels.reshape(patch_count)
    onehot = (regime[:, None] == jnp.arange(experts, dtype=jnp.int32)[None, :]).astype(
        jnp.bfloat16
    )
    lower = (
        jnp.arange(patch_count)[:, None] >= jnp.arange(patch_count)[None, :]
    ).astype(jnp.bfloat16)
    ranking = jnp.dot(lower, onehot, preferred_element_type=jnp.float32)
    slot_index = jnp.sum(ranking * onehot.astype(jnp.float32), axis=1).astype(jnp.int32) - 1
    target = regime * capacity + slot_index
    route = (target[None, :] == jnp.arange(slots, dtype=jnp.int32)[:, None]).astype(jnp.bfloat16)

    flat_feats = feats.reshape(patch_count, feat_width)
    field_rows = conv_block(cotangent, kernel, True)
    local = jnp.concatenate([flat_feats, field_rows], axis=1)
    outbound = jnp.dot(route, local, preferred_element_type=jnp.float32).astype(jnp.bfloat16)
    both = feat_width + channels
    inbound = lax.all_to_all(
        outbound.reshape(experts, capacity, both), "expert", split_axis=0, concat_axis=0, tiled=True
    ).reshape(slots, both)
    back, part = expert(inbound, w_first[0], w_second[0], 1024, slabs)
    returned = lax.all_to_all(
        back.reshape(experts, capacity, both), "expert", split_axis=0, concat_axis=0, tiled=True
    )
    returned = returned.reshape(slots, both)
    mixed_out = lax.dot_general(
        route, returned[:, :channels], (((0,), (0,)), ((), ())), preferred_element_type=jnp.float32
    ).astype(jnp.bfloat16)
    patch_grid = mixed_out.reshape(1, rows_y, depth_cells, channels)
    imitated = conv_block(patch_grid, kernel, False).reshape(1, rows_y, depth_cells, channels)
    feat_grad = lax.dot_general(
        route, returned[:, channels:], (((0,), (0,)), ((), ())), preferred_element_type=jnp.float32
    ).astype(jnp.bfloat16)
    feat_grad = feat_grad.reshape(1, rows_y, depth_cells, feat_width)

    grads = tree_scatter(part, (0, 1, 2, 3))
    grad_one = grads[:feat_width]
    grad_two = grads[feat_width:].T
    return (imitated, feat_grad, grad_one[None], grad_two[None])


def solution(mesh):
    in_specs = (
        P("dp", "expert", None, None),
        P("dp", "expert", None, None),
        P("expert", None, None),
        P("expert", None, None),
        P(),
        P("dp", "expert", None, None),
    )
    out_specs = (
        P("dp", "expert", None, None),
        P("dp", "expert", None, None),
        P("expert", None, "dp"),
        P("expert", "dp", None),
    )
    return jax.shard_map(
        per_device, mesh=mesh, in_specs=in_specs, out_specs=out_specs, check_vma=False
    )
```

```python
import functools

import jax
import jax.numpy as jnp
from jax import lax
from jax.experimental import pallas as pl
from jax.experimental.pallas import tpu as pltpu
from jax.sharding import PartitionSpec as P


def extended(x, sides, width):
    for axis, dim in sides:
        size, length = (lax.axis_size(axis), x.shape[dim])
        up = [(i, (i + 1) % size) for i in range(size - 1)]
        down = [(j, i) for i, j in up]
        last = lax.slice_in_dim(x, length - width, length, axis=dim)
        first = lax.slice_in_dim(x, 0, width, axis=dim)
        before = lax.ppermute(last, axis, up)
        after = lax.ppermute(first, axis, down)
        x = jnp.concatenate([before, x, after], axis=dim)
    return x


def gelu_act(value):
    return jax.nn.gelu(value, approximate=True)


def gelu_back(preact, upstream):
    return jax.vjp(gelu_act, preact)[1](upstream)[0]


def tree_scatter(blocks, order):
    count = blocks.shape[0]
    me = lax.axis_index("dp")
    bits = count.bit_length() - 1
    x = blocks.reshape((2,) * bits + blocks.shape[1:])
    remaining = list(range(bits))
    for bit in order:
        axis = remaining.index(bit)
        mine = (me >> bit) & 1
        keep = lax.dynamic_index_in_dim(x, mine, axis=axis, keepdims=False).astype(jnp.float32)
        send = lax.dynamic_index_in_dim(x, 1 - mine, axis=axis, keepdims=False)
        pairs = [(i, i ^ (1 << bit)) for i in range(count)]
        got = lax.ppermute(send.astype(jnp.bfloat16), "dp", pairs)
        x = keep + got.astype(jnp.float32)
        remaining.pop(axis)
    return x


def conv_kernel(flip, shifted_ref, taps_ref, out_ref, acc_ref):
    rows_y = shifted_ref.shape[3] - 2
    depth_cells = shifted_ref.shape[4]
    width = shifted_ref.shape[5]
    acc_ref[...] = jnp.zeros_like(acc_ref)
    for plane in range(3):
        for across in range(3):
            for along in range(3):
                tap = 9 * plane + 3 * across + along
                piece = shifted_ref[0, along, plane, across : across + rows_y]
                piece = piece.reshape(rows_y * depth_cells, width)
                if flip:
                    acc_ref[...] += lax.dot_general(
                        piece,
                        taps_ref[26 - tap],
                        (((1,), (1,)), ((), ())),
                        preferred_element_type=jnp.float32,
                    )
                else:
                    acc_ref[...] += jnp.dot(
                        piece, taps_ref[tap], preferred_element_type=jnp.float32
                    )
    out_ref[...] = acc_ref[...].astype(out_ref.dtype)


def conv_block(grid, kernel, flip, after=None):
    padded = extended(grid, (("expert", 1), ("dp", 0)), 1)
    if after is not None:
        after, padded = lax.optimization_barrier((after, padded))
    padded = jnp.pad(padded, ((0, 0), (0, 0), (1, 1), (0, 0)))
    depth_cells = grid.shape[2]
    shifted = jnp.stack(
        [padded[:, :, along : along + depth_cells] for along in range(3)], axis=0
    )[None]
    count = grid.shape[1] * depth_cells
    width = kernel.shape[2]
    result = pl.pallas_call(
        functools.partial(conv_kernel, flip),
        out_shape=jax.ShapeDtypeStruct((count, width), jnp.bfloat16),
        in_specs=[pl.BlockSpec(memory_space=pltpu.VMEM)] * 2,
        out_specs=pl.BlockSpec(memory_space=pltpu.VMEM),
        scratch_shapes=[pltpu.VMEM((count, width), jnp.float32)],
        compiler_params=pltpu.CompilerParams(vmem_limit_bytes=48 * 1024 * 1024),
        cost_estimate=pl.CostEstimate(
            flops=2 * 27 * count * width * width,
            transcendentals=0,
            bytes_accessed=2 * (shifted.size + kernel.size + count * width),
        ),
    )(shifted, kernel)
    if after is not None:
        return result, after
    return result


def expert_kernel(
    cols, rows_ref, first_ref, second_ref, back_ref, part_ref, result_acc, input_acc, across_ref
):
    step = pl.program_id(0)

    @pl.when(step == 0)
    def _():
        result_acc[...] = jnp.zeros_like(result_acc)
        input_acc[...] = jnp.zeros_like(input_acc)
        across_ref[...] = rows_ref[...].T

    rows = rows_ref[:, :cols]
    grads = rows_ref[:, cols:]
    first = first_ref[...]
    second = second_ref[...]
    preact = jnp.dot(rows, first, preferred_element_type=jnp.float32)
    activation = gelu_act(preact).astype(jnp.bfloat16)
    result_acc[...] += jnp.dot(activation, second, preferred_element_type=jnp.float32)
    upstream = lax.dot_general(
        grads, second, (((1,), (1,)), ((), ())), preferred_element_type=jnp.float32
    )
    gate_grad = gelu_back(preact, upstream).astype(jnp.bfloat16)
    input_acc[...] += lax.dot_general(
        gate_grad, first, (((1,), (1,)), ((), ())), preferred_element_type=jnp.float32
    )
    part_one = jnp.dot(across_ref[:cols, :], gate_grad, preferred_element_type=jnp.float32)
    part_two = jnp.dot(across_ref[cols:, :], activation, preferred_element_type=jnp.float32)
    lanes = part_ref.shape[2]
    bits = part_ref.shape[0].bit_length() - 1
    per_step = part_one.shape[1] // lanes
    for block in range(per_step):
        window = slice(block * lanes, (block + 1) * lanes)
        owner = step * per_step + block
        place = sum(((owner >> bit) & 1) << (bits - 1 - bit) for bit in range(bits))
        part_ref[place, :cols, :] = part_one[:, window].astype(part_ref.dtype)
        part_ref[place, cols:, :] = part_two[:, window].astype(part_ref.dtype)

    @pl.when(step == pl.num_programs(0) - 1)
    def _():
        width = result_acc.shape[1]
        back_ref[:, :width] = result_acc[...].astype(back_ref.dtype)
        back_ref[:, width:] = input_acc[...].astype(back_ref.dtype)


def expert(inbound, weight_one, weight_two, chunk, blocks):
    slots, both = inbound.shape
    cols, hidden = weight_one.shape
    channels = weight_two.shape[1]
    lanes = hidden // blocks
    flops = 2 * slots * hidden * (3 * cols + 3 * channels)
    return pl.pallas_call(
        functools.partial(expert_kernel, cols),
        grid=(hidden // chunk,),
        in_specs=[
            pl.BlockSpec((slots, both), lambda h: (0, 0)),
            pl.BlockSpec((cols, chunk), lambda h: (0, h)),
            pl.BlockSpec((chunk, channels), lambda h: (h, 0)),
        ],
        out_specs=[
            pl.BlockSpec((slots, both), lambda h: (0, 0)),
            pl.BlockSpec((blocks, both, lanes), lambda h: (0, 0, 0)),
        ],
        out_shape=[
            jax.ShapeDtypeStruct((slots, both), jnp.bfloat16),
            jax.ShapeDtypeStruct((blocks, both, lanes), jnp.bfloat16),
        ],
        scratch_shapes=[
            pltpu.VMEM((slots, channels), jnp.float32),
            pltpu.VMEM((slots, cols), jnp.float32),
            pltpu.VMEM((both, slots), jnp.bfloat16),
        ],
        compiler_params=pltpu.CompilerParams(
            dimension_semantics=("arbitrary",), vmem_limit_bytes=56 * 1024 * 1024
        ),
        cost_estimate=pl.CostEstimate(
            flops=flops,
            transcendentals=slots * hidden,
            bytes_accessed=2 * (2 * slots * both + hidden * (cols + channels)) + 2 * hidden * both,
        ),
    )(inbound, weight_one, weight_two)


def per_device(feats, labels, w_first, w_second, kernel, cotangent):
    experts = lax.axis_size("expert")
    slabs = lax.axis_size("dp")
    rows_y = feats.shape[1]
    depth_cells = feats.shape[2]
    feat_width = feats.shape[3]
    channels = kernel.shape[2]
    hidden = w_first.shape[2]
    patch_count = rows_y * depth_cells
    capacity = 2 * patch_count // experts
    slots = experts * capacity
    regime = labels.reshape(patch_count)
    onehot = (regime[:, None] == jnp.arange(experts, dtype=jnp.int32)[None, :]).astype(
        jnp.bfloat16
    )
    lower = (
        jnp.arange(patch_count)[:, None] >= jnp.arange(patch_count)[None, :]
    ).astype(jnp.bfloat16)
    ranking = jnp.dot(lower, onehot, preferred_element_type=jnp.float32)
    slot_index = jnp.sum(ranking * onehot.astype(jnp.float32), axis=1).astype(jnp.int32) - 1
    target = regime * capacity + slot_index
    route = (target[None, :] == jnp.arange(slots, dtype=jnp.int32)[:, None]).astype(jnp.bfloat16)

    flat_feats = feats.reshape(patch_count, feat_width)
    field_rows = conv_block(cotangent, kernel, True)
    local = jnp.concatenate([flat_feats, field_rows], axis=1)
    outbound = jnp.dot(route, local, preferred_element_type=jnp.float32).astype(jnp.bfloat16)
    both = feat_width + channels
    inbound = lax.all_to_all(
        outbound.reshape(experts, capacity, both), "expert", split_axis=0, concat_axis=0, tiled=True
    ).reshape(slots, both)
    back, part = expert(inbound, w_first[0], w_second[0], 1024, slabs)
    returned = lax.all_to_all(
        back.reshape(experts, capacity, both), "expert", split_axis=0, concat_axis=0, tiled=True
    )
    returned = returned.reshape(slots, both)
    mixed_out = lax.dot_general(
        route, returned[:, :channels], (((0,), (0,)), ((), ())), preferred_element_type=jnp.float32
    ).astype(jnp.bfloat16)
    patch_grid = mixed_out.reshape(1, rows_y, depth_cells, channels)
    imitated = conv_block(patch_grid, kernel, False).reshape(1, rows_y, depth_cells, channels)
    feat_grad = lax.dot_general(
        route, returned[:, channels:], (((0,), (0,)), ((), ())), preferred_element_type=jnp.float32
    ).astype(jnp.bfloat16)
    feat_grad = feat_grad.reshape(1, rows_y, depth_cells, feat_width)

    grads = tree_scatter(part, (0, 1, 3, 2))
    grad_one = grads[:feat_width]
    grad_two = grads[feat_width:].T
    return (imitated, feat_grad, grad_one[None], grad_two[None])


def solution(mesh):
    in_specs = (
        P("dp", "expert", None, None),
        P("dp", "expert", None, None),
        P("expert", None, None),
        P("expert", None, None),
        P(),
        P("dp", "expert", None, None),
    )
    out_specs = (
        P("dp", "expert", None, None),
        P("dp", "expert", None, None),
        P("expert", None, "dp"),
        P("expert", "dp", None),
    )
    return jax.shard_map(
        per_device, mesh=mesh, in_specs=in_specs, out_specs=out_specs, check_vma=False
    )
```

```python
import functools

import jax
import jax.numpy as jnp
from jax import lax
from jax.experimental import pallas as pl
from jax.experimental.pallas import tpu as pltpu
from jax.sharding import PartitionSpec as P


def extended(x, sides, width):
    for axis, dim in sides:
        size, length = (lax.axis_size(axis), x.shape[dim])
        up = [(i, (i + 1) % size) for i in range(size - 1)]
        down = [(j, i) for i, j in up]
        last = lax.slice_in_dim(x, length - width, length, axis=dim)
        first = lax.slice_in_dim(x, 0, width, axis=dim)
        before = lax.ppermute(last, axis, up)
        after = lax.ppermute(first, axis, down)
        x = jnp.concatenate([before, x, after], axis=dim)
    return x


def gelu_act(value):
    return jax.nn.gelu(value, approximate=True)


def gelu_back(preact, upstream):
    return jax.vjp(gelu_act, preact)[1](upstream)[0]


def tree_scatter(blocks, order):
    count = blocks.shape[0]
    me = lax.axis_index("dp")
    bits = count.bit_length() - 1
    x = blocks.reshape((2,) * bits + blocks.shape[1:])
    remaining = list(range(bits))
    for bit in order:
        axis = remaining.index(bit)
        mine = (me >> bit) & 1
        if bit == 0:
            keep, send = x[0].astype(jnp.float32), x[1]
        else:
            keep = lax.dynamic_index_in_dim(x, mine, axis=axis, keepdims=False).astype(jnp.float32)
            send = lax.dynamic_index_in_dim(x, 1 - mine, axis=axis, keepdims=False)
        pairs = [(i, i ^ (1 << bit)) for i in range(count)]
        got = lax.ppermute(send.astype(jnp.bfloat16), "dp", pairs)
        x = keep + got.astype(jnp.float32)
        remaining.pop(axis)
    return x


def conv_kernel(flip, shifted_ref, taps_ref, out_ref, acc_ref):
    rows_y = shifted_ref.shape[3] - 2
    depth_cells = shifted_ref.shape[4]
    width = shifted_ref.shape[5]
    acc_ref[...] = jnp.zeros_like(acc_ref)
    for plane in range(3):
        for across in range(3):
            for along in range(3):
                tap = 9 * plane + 3 * across + along
                piece = shifted_ref[0, along, plane, across : across + rows_y]
                piece = piece.reshape(rows_y * depth_cells, width)
                if flip:
                    acc_ref[...] += lax.dot_general(
                        piece,
                        taps_ref[26 - tap],
                        (((1,), (1,)), ((), ())),
                        preferred_element_type=jnp.float32,
                    )
                else:
                    acc_ref[...] += jnp.dot(
                        piece, taps_ref[tap], preferred_element_type=jnp.float32
                    )
    out_ref[...] = acc_ref[...].astype(out_ref.dtype)


def conv_block(grid, kernel, flip, after=None):
    padded = extended(grid, (("expert", 1), ("dp", 0)), 1)
    if after is not None:
        after, padded = lax.optimization_barrier((after, padded))
    padded = jnp.pad(padded, ((0, 0), (0, 0), (1, 1), (0, 0)))
    depth_cells = grid.shape[2]
    shifted = jnp.stack(
        [padded[:, :, along : along + depth_cells] for along in range(3)], axis=0
    )[None]
    count = grid.shape[1] * depth_cells
    width = kernel.shape[2]
    result = pl.pallas_call(
        functools.partial(conv_kernel, flip),
        out_shape=jax.ShapeDtypeStruct((count, width), jnp.bfloat16),
        in_specs=[pl.BlockSpec(memory_space=pltpu.VMEM)] * 2,
        out_specs=pl.BlockSpec(memory_space=pltpu.VMEM),
        scratch_shapes=[pltpu.VMEM((count, width), jnp.float32)],
        compiler_params=pltpu.CompilerParams(vmem_limit_bytes=48 * 1024 * 1024),
        cost_estimate=pl.CostEstimate(
            flops=2 * 27 * count * width * width,
            transcendentals=0,
            bytes_accessed=2 * (shifted.size + kernel.size + count * width),
        ),
    )(shifted, kernel)
    if after is not None:
        return result, after
    return result


def expert_kernel(
    cols, rows_ref, first_ref, second_ref, back_ref, part_ref, result_acc, input_acc, across_ref
):
    step = pl.program_id(0)

    @pl.when(step == 0)
    def _():
        result_acc[...] = jnp.zeros_like(result_acc)
        input_acc[...] = jnp.zeros_like(input_acc)
        across_ref[...] = rows_ref[...].T

    rows = rows_ref[:, :cols]
    grads = rows_ref[:, cols:]
    first = first_ref[...]
    second = second_ref[...]
    preact = jnp.dot(rows, first, preferred_element_type=jnp.float32)
    activation = gelu_act(preact).astype(jnp.bfloat16)
    result_acc[...] += jnp.dot(activation, second, preferred_element_type=jnp.float32)
    upstream = lax.dot_general(
        grads, second, (((1,), (1,)), ((), ())), preferred_element_type=jnp.float32
    )
    gate_grad = gelu_back(preact, upstream).astype(jnp.bfloat16)
    input_acc[...] += lax.dot_general(
        gate_grad, first, (((1,), (1,)), ((), ())), preferred_element_type=jnp.float32
    )
    part_one = jnp.dot(across_ref[:cols, :], gate_grad, preferred_element_type=jnp.float32)
    part_two = jnp.dot(across_ref[cols:, :], activation, preferred_element_type=jnp.float32)
    lanes = part_ref.shape[2]
    bits = part_ref.shape[0].bit_length() - 1
    mine = lax.axis_index("dp") & 1
    per_step = part_one.shape[1] // lanes
    for block in range(per_step):
        window = slice(block * lanes, (block + 1) * lanes)
        owner = step * per_step + block
        place = sum(((owner >> bit) & 1) << (bits - 1 - bit) for bit in range(bits))
        place = place ^ (mine << (bits - 1))
        part_ref[place, :cols, :] = part_one[:, window].astype(part_ref.dtype)
        part_ref[place, cols:, :] = part_two[:, window].astype(part_ref.dtype)

    @pl.when(step == pl.num_programs(0) - 1)
    def _():
        width = result_acc.shape[1]
        back_ref[:, :width] = result_acc[...].astype(back_ref.dtype)
        back_ref[:, width:] = input_acc[...].astype(back_ref.dtype)


def expert(inbound, weight_one, weight_two, chunk, blocks):
    slots, both = inbound.shape
    cols, hidden = weight_one.shape
    channels = weight_two.shape[1]
    lanes = hidden // blocks
    flops = 2 * slots * hidden * (3 * cols + 3 * channels)
    return pl.pallas_call(
        functools.partial(expert_kernel, cols),
        grid=(hidden // chunk,),
        in_specs=[
            pl.BlockSpec((slots, both), lambda h: (0, 0)),
            pl.BlockSpec((cols, chunk), lambda h: (0, h)),
            pl.BlockSpec((chunk, channels), lambda h: (h, 0)),
        ],
        out_specs=[
            pl.BlockSpec((slots, both), lambda h: (0, 0)),
            pl.BlockSpec((blocks, both, lanes), lambda h: (0, 0, 0)),
        ],
        out_shape=[
            jax.ShapeDtypeStruct((slots, both), jnp.bfloat16),
            jax.ShapeDtypeStruct((blocks, both, lanes), jnp.bfloat16),
        ],
        scratch_shapes=[
            pltpu.VMEM((slots, channels), jnp.float32),
            pltpu.VMEM((slots, cols), jnp.float32),
            pltpu.VMEM((both, slots), jnp.bfloat16),
        ],
        compiler_params=pltpu.CompilerParams(
            dimension_semantics=("arbitrary",), vmem_limit_bytes=56 * 1024 * 1024
        ),
        cost_estimate=pl.CostEstimate(
            flops=flops,
            transcendentals=slots * hidden,
            bytes_accessed=2 * (2 * slots * both + hidden * (cols + channels)) + 2 * hidden * both,
        ),
    )(inbound, weight_one, weight_two)


def per_device(feats, labels, w_first, w_second, kernel, cotangent):
    experts = lax.axis_size("expert")
    slabs = lax.axis_size("dp")
    rows_y = feats.shape[1]
    depth_cells = feats.shape[2]
    feat_width = feats.shape[3]
    channels = kernel.shape[2]
    hidden = w_first.shape[2]
    patch_count = rows_y * depth_cells
    capacity = 2 * patch_count // experts
    slots = experts * capacity
    regime = labels.reshape(patch_count)
    onehot = (regime[:, None] == jnp.arange(experts, dtype=jnp.int32)[None, :]).astype(
        jnp.bfloat16
    )
    lower = (
        jnp.arange(patch_count)[:, None] >= jnp.arange(patch_count)[None, :]
    ).astype(jnp.bfloat16)
    ranking = jnp.dot(lower, onehot, preferred_element_type=jnp.float32)
    slot_index = jnp.sum(ranking * onehot.astype(jnp.float32), axis=1).astype(jnp.int32) - 1
    target = regime * capacity + slot_index
    route = (target[None, :] == jnp.arange(slots, dtype=jnp.int32)[:, None]).astype(jnp.bfloat16)

    flat_feats = feats.reshape(patch_count, feat_width)
    field_rows = conv_block(cotangent, kernel, True)
    local = jnp.concatenate([flat_feats, field_rows], axis=1)
    outbound = jnp.dot(route, local, preferred_element_type=jnp.float32).astype(jnp.bfloat16)
    both = feat_width + channels
    inbound = lax.all_to_all(
        outbound.reshape(experts, capacity, both), "expert", split_axis=0, concat_axis=0, tiled=True
    ).reshape(slots, both)
    back, part = expert(inbound, w_first[0], w_second[0], 1024, slabs)
    returned = lax.all_to_all(
        back.reshape(experts, capacity, both), "expert", split_axis=0, concat_axis=0, tiled=True
    )
    returned = returned.reshape(slots, both)
    mixed_out = lax.dot_general(
        route, returned[:, :channels], (((0,), (0,)), ((), ())), preferred_element_type=jnp.float32
    ).astype(jnp.bfloat16)
    patch_grid = mixed_out.reshape(1, rows_y, depth_cells, channels)
    imitated = conv_block(patch_grid, kernel, False).reshape(1, rows_y, depth_cells, channels)
    feat_grad = lax.dot_general(
        route, returned[:, channels:], (((0,), (0,)), ((), ())), preferred_element_type=jnp.float32
    ).astype(jnp.bfloat16)
    feat_grad = feat_grad.reshape(1, rows_y, depth_cells, feat_width)

    grads = tree_scatter(part, (0, 1, 2, 3))
    grad_one = grads[:feat_width]
    grad_two = grads[feat_width:].T
    return (imitated, feat_grad, grad_one[None], grad_two[None])


def solution(mesh):
    in_specs = (
        P("dp", "expert", None, None),
        P("dp", "expert", None, None),
        P("expert", None, None),
        P("expert", None, None),
        P(),
        P("dp", "expert", None, None),
    )
    out_specs = (
        P("dp", "expert", None, None),
        P("dp", "expert", None, None),
        P("expert", None, "dp"),
        P("expert", "dp", None),
    )
    return jax.shard_map(
        per_device, mesh=mesh, in_specs=in_specs, out_specs=out_specs, check_vma=False
    )
```

```python
import functools

import jax
import jax.numpy as jnp
from jax import lax
from jax.experimental import pallas as pl
from jax.experimental.pallas import tpu as pltpu
from jax.sharding import PartitionSpec as P


def extended(x, sides, width):
    for axis, dim in sides:
        size, length = (lax.axis_size(axis), x.shape[dim])
        up = [(i, (i + 1) % size) for i in range(size - 1)]
        down = [(j, i) for i, j in up]
        last = lax.slice_in_dim(x, length - width, length, axis=dim)
        first = lax.slice_in_dim(x, 0, width, axis=dim)
        before = lax.ppermute(last, axis, up)
        after = lax.ppermute(first, axis, down)
        x = jnp.concatenate([before, x, after], axis=dim)
    return x


def gelu_act(value):
    return jax.nn.gelu(value, approximate=True)


def gelu_back(preact, upstream):
    return jax.vjp(gelu_act, preact)[1](upstream)[0]


def tree_scatter(blocks, order):
    count = blocks.shape[0]
    me = lax.axis_index("dp")
    bits = count.bit_length() - 1
    x = blocks.reshape((2,) * bits + blocks.shape[1:])
    remaining = list(range(bits))
    for bit in order:
        axis = remaining.index(bit)
        mine = (me >> bit) & 1
        if axis == 0:
            keep, send = x[0].astype(jnp.float32), x[1]
        else:
            keep = lax.dynamic_index_in_dim(x, mine, axis=axis, keepdims=False).astype(jnp.float32)
            send = lax.dynamic_index_in_dim(x, 1 - mine, axis=axis, keepdims=False)
        pairs = [(i, i ^ (1 << bit)) for i in range(count)]
        got = lax.ppermute(send.astype(jnp.bfloat16), "dp", pairs)
        x = keep + got.astype(jnp.float32)
        remaining.pop(axis)
    return x


def conv_kernel(flip, shifted_ref, taps_ref, out_ref, acc_ref):
    rows_y = shifted_ref.shape[3] - 2
    depth_cells = shifted_ref.shape[4]
    width = shifted_ref.shape[5]
    acc_ref[...] = jnp.zeros_like(acc_ref)
    for plane in range(3):
        for across in range(3):
            for along in range(3):
                tap = 9 * plane + 3 * across + along
                piece = shifted_ref[0, along, plane, across : across + rows_y]
                piece = piece.reshape(rows_y * depth_cells, width)
                if flip:
                    acc_ref[...] += lax.dot_general(
                        piece,
                        taps_ref[26 - tap],
                        (((1,), (1,)), ((), ())),
                        preferred_element_type=jnp.float32,
                    )
                else:
                    acc_ref[...] += jnp.dot(
                        piece, taps_ref[tap], preferred_element_type=jnp.float32
                    )
    out_ref[...] = acc_ref[...].astype(out_ref.dtype)


def conv_block(grid, kernel, flip, after=None):
    padded = extended(grid, (("expert", 1), ("dp", 0)), 1)
    if after is not None:
        after, padded = lax.optimization_barrier((after, padded))
    padded = jnp.pad(padded, ((0, 0), (0, 0), (1, 1), (0, 0)))
    depth_cells = grid.shape[2]
    shifted = jnp.stack(
        [padded[:, :, along : along + depth_cells] for along in range(3)], axis=0
    )[None]
    count = grid.shape[1] * depth_cells
    width = kernel.shape[2]
    result = pl.pallas_call(
        functools.partial(conv_kernel, flip),
        out_shape=jax.ShapeDtypeStruct((count, width), jnp.bfloat16),
        in_specs=[pl.BlockSpec(memory_space=pltpu.VMEM)] * 2,
        out_specs=pl.BlockSpec(memory_space=pltpu.VMEM),
        scratch_shapes=[pltpu.VMEM((count, width), jnp.float32)],
        compiler_params=pltpu.CompilerParams(vmem_limit_bytes=48 * 1024 * 1024),
        cost_estimate=pl.CostEstimate(
            flops=2 * 27 * count * width * width,
            transcendentals=0,
            bytes_accessed=2 * (shifted.size + kernel.size + count * width),
        ),
    )(shifted, kernel)
    if after is not None:
        return result, after
    return result


def expert_kernel(
    cols, rows_ref, first_ref, second_ref, back_ref, part_ref, result_acc, input_acc, across_ref
):
    step = pl.program_id(0)

    @pl.when(step == 0)
    def _():
        result_acc[...] = jnp.zeros_like(result_acc)
        input_acc[...] = jnp.zeros_like(input_acc)
        across_ref[...] = rows_ref[...].T

    rows = rows_ref[:, :cols]
    grads = rows_ref[:, cols:]
    first = first_ref[...]
    second = second_ref[...]
    preact = jnp.dot(rows, first, preferred_element_type=jnp.float32)
    activation = gelu_act(preact).astype(jnp.bfloat16)
    result_acc[...] += jnp.dot(activation, second, preferred_element_type=jnp.float32)
    upstream = lax.dot_general(
        grads, second, (((1,), (1,)), ((), ())), preferred_element_type=jnp.float32
    )
    gate_grad = gelu_back(preact, upstream).astype(jnp.bfloat16)
    input_acc[...] += lax.dot_general(
        gate_grad, first, (((1,), (1,)), ((), ())), preferred_element_type=jnp.float32
    )
    part_one = jnp.dot(across_ref[:cols, :], gate_grad, preferred_element_type=jnp.float32)
    part_two = jnp.dot(across_ref[cols:, :], activation, preferred_element_type=jnp.float32)
    lanes = part_ref.shape[2]
    bits = part_ref.shape[0].bit_length() - 1
    mine = lax.axis_index("dp")
    per_step = part_one.shape[1] // lanes
    for block in range(per_step):
        window = slice(block * lanes, (block + 1) * lanes)
        owner = step * per_step + block
        relative = owner ^ mine
        place = sum(((relative >> bit) & 1) << (bits - 1 - bit) for bit in range(bits))
        part_ref[place, :cols, :] = part_one[:, window].astype(part_ref.dtype)
        part_ref[place, cols:, :] = part_two[:, window].astype(part_ref.dtype)

    @pl.when(step == pl.num_programs(0) - 1)
    def _():
        width = result_acc.shape[1]
        back_ref[:, :width] = result_acc[...].astype(back_ref.dtype)
        back_ref[:, width:] = input_acc[...].astype(back_ref.dtype)


def expert(inbound, weight_one, weight_two, chunk, blocks):
    slots, both = inbound.shape
    cols, hidden = weight_one.shape
    channels = weight_two.shape[1]
    lanes = hidden // blocks
    flops = 2 * slots * hidden * (3 * cols + 3 * channels)
    return pl.pallas_call(
        functools.partial(expert_kernel, cols),
        grid=(hidden // chunk,),
        in_specs=[
            pl.BlockSpec((slots, both), lambda h: (0, 0)),
            pl.BlockSpec((cols, chunk), lambda h: (0, h)),
            pl.BlockSpec((chunk, channels), lambda h: (h, 0)),
        ],
        out_specs=[
            pl.BlockSpec((slots, both), lambda h: (0, 0)),
            pl.BlockSpec((blocks, both, lanes), lambda h: (0, 0, 0)),
        ],
        out_shape=[
            jax.ShapeDtypeStruct((slots, both), jnp.bfloat16),
            jax.ShapeDtypeStruct((blocks, both, lanes), jnp.bfloat16),
        ],
        scratch_shapes=[
            pltpu.VMEM((slots, channels), jnp.float32),
            pltpu.VMEM((slots, cols), jnp.float32),
            pltpu.VMEM((both, slots), jnp.bfloat16),
        ],
        compiler_params=pltpu.CompilerParams(
            dimension_semantics=("arbitrary",), vmem_limit_bytes=56 * 1024 * 1024
        ),
        cost_estimate=pl.CostEstimate(
            flops=flops,
            transcendentals=slots * hidden,
            bytes_accessed=2 * (2 * slots * both + hidden * (cols + channels)) + 2 * hidden * both,
        ),
    )(inbound, weight_one, weight_two)


def per_device(feats, labels, w_first, w_second, kernel, cotangent):
    experts = lax.axis_size("expert")
    slabs = lax.axis_size("dp")
    rows_y = feats.shape[1]
    depth_cells = feats.shape[2]
    feat_width = feats.shape[3]
    channels = kernel.shape[2]
    hidden = w_first.shape[2]
    patch_count = rows_y * depth_cells
    capacity = 2 * patch_count // experts
    slots = experts * capacity
    regime = labels.reshape(patch_count)
    onehot = (regime[:, None] == jnp.arange(experts, dtype=jnp.int32)[None, :]).astype(
        jnp.bfloat16
    )
    lower = (
        jnp.arange(patch_count)[:, None] >= jnp.arange(patch_count)[None, :]
    ).astype(jnp.bfloat16)
    ranking = jnp.dot(lower, onehot, preferred_element_type=jnp.float32)
    slot_index = jnp.sum(ranking * onehot.astype(jnp.float32), axis=1).astype(jnp.int32) - 1
    target = regime * capacity + slot_index
    route = (target[None, :] == jnp.arange(slots, dtype=jnp.int32)[:, None]).astype(jnp.bfloat16)

    flat_feats = feats.reshape(patch_count, feat_width)
    field_rows = conv_block(cotangent, kernel, True)
    local = jnp.concatenate([flat_feats, field_rows], axis=1)
    outbound = jnp.dot(route, local, preferred_element_type=jnp.float32).astype(jnp.bfloat16)
    both = feat_width + channels
    inbound = lax.all_to_all(
        outbound.reshape(experts, capacity, both), "expert", split_axis=0, concat_axis=0, tiled=True
    ).reshape(slots, both)
    back, part = expert(inbound, w_first[0], w_second[0], 1024, slabs)
    returned = lax.all_to_all(
        back.reshape(experts, capacity, both), "expert", split_axis=0, concat_axis=0, tiled=True
    )
    returned = returned.reshape(slots, both)
    mixed_out = lax.dot_general(
        route, returned[:, :channels], (((0,), (0,)), ((), ())), preferred_element_type=jnp.float32
    ).astype(jnp.bfloat16)
    patch_grid = mixed_out.reshape(1, rows_y, depth_cells, channels)
    imitated = conv_block(patch_grid, kernel, False).reshape(1, rows_y, depth_cells, channels)
    feat_grad = lax.dot_general(
        route, returned[:, channels:], (((0,), (0,)), ((), ())), preferred_element_type=jnp.float32
    ).astype(jnp.bfloat16)
    feat_grad = feat_grad.reshape(1, rows_y, depth_cells, feat_width)

    grads = tree_scatter(part, (0, 1, 2, 3))
    grad_one = grads[:feat_width]
    grad_two = grads[feat_width:].T
    return (imitated, feat_grad, grad_one[None], grad_two[None])


def solution(mesh):
    in_specs = (
        P("dp", "expert", None, None),
        P("dp", "expert", None, None),
        P("expert", None, None),
        P("expert", None, None),
        P(),
        P("dp", "expert", None, None),
    )
    out_specs = (
        P("dp", "expert", None, None),
        P("dp", "expert", None, None),
        P("expert", None, "dp"),
        P("expert", "dp", None),
    )
    return jax.shard_map(
        per_device, mesh=mesh, in_specs=in_specs, out_specs=out_specs, check_vma=False
    )
```

```python
import functools

import jax
import jax.numpy as jnp
from jax import lax
from jax.experimental import pallas as pl
from jax.experimental.pallas import tpu as pltpu
from jax.sharding import PartitionSpec as P


def extended(x, sides, width):
    for axis, dim in sides:
        size, length = (lax.axis_size(axis), x.shape[dim])
        up = [(i, (i + 1) % size) for i in range(size - 1)]
        down = [(j, i) for i, j in up]
        last = lax.slice_in_dim(x, length - width, length, axis=dim)
        first = lax.slice_in_dim(x, 0, width, axis=dim)
        before = lax.ppermute(last, axis, up)
        after = lax.ppermute(first, axis, down)
        x = jnp.concatenate([before, x, after], axis=dim)
    return x


def gelu_act(value):
    return jax.nn.gelu(value, approximate=True)


def gelu_back(preact, upstream):
    return jax.vjp(gelu_act, preact)[1](upstream)[0]


def tree_scatter(blocks, order):
    count = blocks.shape[0]
    me = lax.axis_index("dp")
    bits = count.bit_length() - 1
    x = blocks.reshape((2,) * bits + blocks.shape[1:])
    remaining = list(range(bits))
    for bit in order:
        axis = remaining.index(bit)
        mine = (me >> bit) & 1
        if axis == 0:
            keep, send = x[0].astype(jnp.float32), x[1]
        else:
            keep = lax.dynamic_index_in_dim(x, mine, axis=axis, keepdims=False).astype(jnp.float32)
            send = lax.dynamic_index_in_dim(x, 1 - mine, axis=axis, keepdims=False)
        pairs = [(i, i ^ (1 << bit)) for i in range(count)]
        got = lax.ppermute(send.astype(jnp.bfloat16), "dp", pairs)
        x = keep + got.astype(jnp.float32)
        remaining.pop(axis)
    return x


def conv_kernel(flip, shifted_ref, taps_ref, out_ref, acc_ref):
    rows_y = shifted_ref.shape[3] - 2
    depth_cells = shifted_ref.shape[4]
    width = shifted_ref.shape[5]
    acc_ref[...] = jnp.zeros_like(acc_ref)
    for plane in range(3):
        for across in range(3):
            for along in range(3):
                tap = 9 * plane + 3 * across + along
                piece = shifted_ref[0, along, plane, across : across + rows_y]
                piece = piece.reshape(rows_y * depth_cells, width)
                if flip:
                    acc_ref[...] += lax.dot_general(
                        piece,
                        taps_ref[26 - tap],
                        (((1,), (1,)), ((), ())),
                        preferred_element_type=jnp.float32,
                    )
                else:
                    acc_ref[...] += jnp.dot(
                        piece, taps_ref[tap], preferred_element_type=jnp.float32
                    )
    out_ref[...] = acc_ref[...].astype(out_ref.dtype)


def conv_block(grid, kernel, flip, after=None):
    padded = extended(grid, (("expert", 1), ("dp", 0)), 1)
    if after is not None:
        after, padded = lax.optimization_barrier((after, padded))
    padded = jnp.pad(padded, ((0, 0), (0, 0), (1, 1), (0, 0)))
    depth_cells = grid.shape[2]
    shifted = jnp.stack(
        [padded[:, :, along : along + depth_cells] for along in range(3)], axis=0
    )[None]
    count = grid.shape[1] * depth_cells
    width = kernel.shape[2]
    result = pl.pallas_call(
        functools.partial(conv_kernel, flip),
        out_shape=jax.ShapeDtypeStruct((count, width), jnp.bfloat16),
        in_specs=[pl.BlockSpec(memory_space=pltpu.VMEM)] * 2,
        out_specs=pl.BlockSpec(memory_space=pltpu.VMEM),
        scratch_shapes=[pltpu.VMEM((count, width), jnp.float32)],
        compiler_params=pltpu.CompilerParams(vmem_limit_bytes=48 * 1024 * 1024),
        cost_estimate=pl.CostEstimate(
            flops=2 * 27 * count * width * width,
            transcendentals=0,
            bytes_accessed=2 * (shifted.size + kernel.size + count * width),
        ),
    )(shifted, kernel)
    if after is not None:
        return result, after
    return result


def expert_kernel(
    cols, rows_ref, first_ref, second_ref, back_ref, part_ref, result_acc, input_acc, across_ref
):
    step = pl.program_id(0)

    @pl.when(step == 0)
    def _():
        result_acc[...] = jnp.zeros_like(result_acc)
        input_acc[...] = jnp.zeros_like(input_acc)
        across_ref[...] = rows_ref[...].T

    rows = rows_ref[:, :cols]
    grads = rows_ref[:, cols:]
    first = first_ref[...]
    second = second_ref[...]
    preact = jnp.dot(rows, first, preferred_element_type=jnp.float32)
    activation = gelu_act(preact).astype(jnp.bfloat16)
    result_acc[...] += jnp.dot(activation, second, preferred_element_type=jnp.float32)
    upstream = lax.dot_general(
        grads, second, (((1,), (1,)), ((), ())), preferred_element_type=jnp.float32
    )
    gate_grad = gelu_back(preact, upstream).astype(jnp.bfloat16)
    input_acc[...] += lax.dot_general(
        gate_grad, first, (((1,), (1,)), ((), ())), preferred_element_type=jnp.float32
    )
    part_one = jnp.dot(across_ref[:cols, :], gate_grad, preferred_element_type=jnp.float32)
    part_two = jnp.dot(across_ref[cols:, :], activation, preferred_element_type=jnp.float32)
    lanes = part_ref.shape[2]
    bits = part_ref.shape[0].bit_length() - 1
    mine = lax.axis_index("dp")
    per_step = part_one.shape[1] // lanes
    for block in range(per_step):
        window = slice(block * lanes, (block + 1) * lanes)
        owner = step * per_step + block
        relative = owner ^ mine
        place = sum(((relative >> bit) & 1) << (bits - 1 - bit) for bit in range(bits))
        part_ref[place, :cols, :] = part_one[:, window].astype(part_ref.dtype)
        part_ref[place, cols:, :] = part_two[:, window].astype(part_ref.dtype)

    @pl.when(step == pl.num_programs(0) - 1)
    def _():
        width = result_acc.shape[1]
        back_ref[:, :width] = result_acc[...].astype(back_ref.dtype)
        back_ref[:, width:] = input_acc[...].astype(back_ref.dtype)


def expert(inbound, weight_one, weight_two, chunk, blocks):
    slots, both = inbound.shape
    cols, hidden = weight_one.shape
    channels = weight_two.shape[1]
    lanes = hidden // blocks
    flops = 2 * slots * hidden * (3 * cols + 3 * channels)
    return pl.pallas_call(
        functools.partial(expert_kernel, cols),
        grid=(hidden // chunk,),
        in_specs=[
            pl.BlockSpec((slots, both), lambda h: (0, 0)),
            pl.BlockSpec((cols, chunk), lambda h: (0, h)),
            pl.BlockSpec((chunk, channels), lambda h: (h, 0)),
        ],
        out_specs=[
            pl.BlockSpec((slots, both), lambda h: (0, 0)),
            pl.BlockSpec((blocks, both, lanes), lambda h: (0, 0, 0)),
        ],
        out_shape=[
            jax.ShapeDtypeStruct((slots, both), jnp.bfloat16),
            jax.ShapeDtypeStruct((blocks, both, lanes), jnp.bfloat16),
        ],
        scratch_shapes=[
            pltpu.VMEM((slots, channels), jnp.float32),
            pltpu.VMEM((slots, cols), jnp.float32),
            pltpu.VMEM((both, slots), jnp.bfloat16),
        ],
        compiler_params=pltpu.CompilerParams(
            dimension_semantics=("arbitrary",), vmem_limit_bytes=56 * 1024 * 1024
        ),
        cost_estimate=pl.CostEstimate(
            flops=flops,
            transcendentals=slots * hidden,
            bytes_accessed=2 * (2 * slots * both + hidden * (cols + channels)) + 2 * hidden * both,
        ),
    )(inbound, weight_one, weight_two)


def per_device(feats, labels, w_first, w_second, kernel, cotangent):
    experts = lax.axis_size("expert")
    slabs = lax.axis_size("dp")
    rows_y = feats.shape[1]
    depth_cells = feats.shape[2]
    feat_width = feats.shape[3]
    channels = kernel.shape[2]
    hidden = w_first.shape[2]
    patch_count = rows_y * depth_cells
    capacity = 2 * patch_count // experts
    slots = experts * capacity
    regime = labels.reshape(patch_count)
    onehot = (regime[:, None] == jnp.arange(experts, dtype=jnp.int32)[None, :]).astype(
        jnp.bfloat16
    )
    lower = (
        jnp.arange(patch_count)[:, None] >= jnp.arange(patch_count)[None, :]
    ).astype(jnp.bfloat16)
    ranking = jnp.dot(lower, onehot, preferred_element_type=jnp.float32)
    slot_index = jnp.sum(ranking * onehot.astype(jnp.float32), axis=1).astype(jnp.int32) - 1
    target = regime * capacity + slot_index
    route = (target[None, :] == jnp.arange(slots, dtype=jnp.int32)[:, None]).astype(jnp.bfloat16)

    flat_feats = feats.reshape(patch_count, feat_width)
    field_rows = conv_block(cotangent, kernel, True)
    sent_feats = jnp.dot(route, flat_feats, preferred_element_type=jnp.float32).astype(jnp.bfloat16)
    sent_grads = jnp.dot(route, field_rows, preferred_element_type=jnp.float32).astype(jnp.bfloat16)
    outbound = jnp.concatenate([sent_feats, sent_grads], axis=1)
    both = feat_width + channels
    inbound = lax.all_to_all(
        outbound.reshape(experts, capacity, both), "expert", split_axis=0, concat_axis=0, tiled=True
    ).reshape(slots, both)
    back, part = expert(inbound, w_first[0], w_second[0], 1024, slabs)
    returned = lax.all_to_all(
        back.reshape(experts, capacity, both), "expert", split_axis=0, concat_axis=0, tiled=True
    )
    returned = returned.reshape(slots, both)
    mixed_out = lax.dot_general(
        route, returned[:, :channels], (((0,), (0,)), ((), ())), preferred_element_type=jnp.float32
    ).astype(jnp.bfloat16)
    patch_grid = mixed_out.reshape(1, rows_y, depth_cells, channels)
    imitated = conv_block(patch_grid, kernel, False).reshape(1, rows_y, depth_cells, channels)
    feat_grad = lax.dot_general(
        route, returned[:, channels:], (((0,), (0,)), ((), ())), preferred_element_type=jnp.float32
    ).astype(jnp.bfloat16)
    feat_grad = feat_grad.reshape(1, rows_y, depth_cells, feat_width)

    grads = tree_scatter(part, (0, 1, 2, 3))
    grad_one = grads[:feat_width]
    grad_two = grads[feat_width:].T
    return (imitated, feat_grad, grad_one[None], grad_two[None])


def solution(mesh):
    in_specs = (
        P("dp", "expert", None, None),
        P("dp", "expert", None, None),
        P("expert", None, None),
        P("expert", None, None),
        P(),
        P("dp", "expert", None, None),
    )
    out_specs = (
        P("dp", "expert", None, None),
        P("dp", "expert", None, None),
        P("expert", None, "dp"),
        P("expert", "dp", None),
    )
    return jax.shard_map(
        per_device, mesh=mesh, in_specs=in_specs, out_specs=out_specs, check_vma=False
    )
```
